32 devices in a mesh: dp: 4 (over y, x), outer: 4 (over z), inner: 2 (over core).
Axes of the slice: x: 2, y: 2, z: 4, core: 2. Of those that a mesh axis runs over, the one named last changes fastest.
Arguments:
- queries: bfloat16 [4, 1024, 1024], P('dp', ('outer', 'inner')), may hold values from -6 to 6
- keys: bfloat16 [4, 1024, 2, 1024], P('dp', ('outer', 'inner')), may hold values from -6 to 6
- values: bfloat16 [4, 1024, 2, 1024], P('dp', ('outer', 'inner')), may hold values from -6 to 6
- betas: float32 [4, 8, 2, 1024], P('dp', None, None, ('outer', 'inner')), may hold values from 0.3 to 1.6
- grad_out: bfloat16 [4, 1024, 1024], P('dp', ('outer', 'inner')), may hold values from -16 to 16
- gain: float32 [1024], replicated, may hold values from 0.1 to 1.9
Outputs:
- grad_queries: bfloat16 [4, 1024, 1024], P('dp', ('outer', 'inner'))
- grad_keys: bfloat16 [4, 1024, 2, 1024], P('dp', ('outer', 'inner'))
- grad_values: bfloat16 [4, 1024, 2, 1024], P('dp', ('outer', 'inner'))
- gain_grad: float32 [1024], replicated
The draws below stay inside these ranges and needn't reach their ends.
All inputs are finite; a program needn't handle non-finite values.
Results may differ from the reference program's by a relative error of at most 0.001.
Values sent between devices are 32-bit elements; how exact they have to be, the bound alone decides.
No kernel may reach another device: no remote copies, remote signals or barrier semaphores. Data moves between devices by JAX's collectives and lax.ppermute only.
A program may use at most 128 MiB of HBM per device.

```python
import math
import jax
import jax.numpy as jnp
from jax import lax

HEADS = 8
HEAD_DIM = 128
TOK_DEV = 128
STRETCH = 64
BATCH = 4
SEQ = 1024
N_OUTER = 4
N_INNER = 2


def draw_keys(key, part):
    seeds = [jax.random.fold_in(key, 3 + offset) for offset in range(5)]
    share = 0.5
    gradual_forgetting = jax.random.bernoulli(seeds[0], share, (BATCH, 1, 1, HEADS, 1))
    baseline_amplitude = jax.random.bernoulli(seeds[1], 0.25, (BATCH, 1, 1, HEADS, HEAD_DIM))
    beginning_shifts = jax.random.randint(seeds[2], (BATCH, 1, 1, HEADS, 3), 0, SEQ)
    position_list = lax.broadcasted_iota(jnp.int32, (1, SEQ, 1, 1, 1), 1)
    cluster_length = jnp.any((position_list >= beginning_shifts) & (position_list < beginning_shifts + 48), axis=-1, keepdims=True)
    dispersion_extent = jnp.exp(jax.random.uniform(seeds[3], (BATCH, 1, 1, HEADS, HEAD_DIM), minval=-0.7, maxval=0.7))
    tiny_perturbation = 8.0 / math.sqrt(2.0 * SEQ)
    multiplier_value = jnp.where(gradual_forgetting, jnp.where(baseline_amplitude & jnp.logical_not(cluster_length), tiny_perturbation, 1.0), dispersion_extent)
    shape = (BATCH, SEQ, 2, HEADS, HEAD_DIM)
    noise = jax.random.normal(seeds[4], shape)
    field = jnp.clip(noise * multiplier_value, -6.0, 6.0)
    return field.reshape(BATCH, SEQ, 2, HEADS * HEAD_DIM).astype(jnp.bfloat16)


def draw_grad_out(key, part):
    seeds = [jax.random.fold_in(key, 11 + offset) for offset in range(3)]
    shape = (BATCH, SEQ, HEADS * HEAD_DIM)
    position_list = (lax.broadcasted_iota(jnp.int32, (BATCH, SEQ, 1), 0) * SEQ + lax.broadcasted_iota(jnp.int32, (BATCH, SEQ, 1), 1)).astype(jnp.float32)
    ramp = 1.0 + 2.0 * position_list / (BATCH * SEQ)
    field = jax.random.normal(seeds[0], shape)
    return jnp.clip(field * ramp, -16.0, 16.0).astype(jnp.bfloat16)


def block_scale(stream_key, dims, cuts, least, largest):
    def one(dim, parts):
        heights = jax.random.uniform(jax.random.fold_in(jax.random.fold_in(stream_key, 6), dim), (parts,), jnp.float32, least / len(cuts), largest / len(cuts))
        return jnp.repeat(jnp.exp(heights), dims[dim] // parts).reshape((-1,) + (1,) * (len(dims) - dim - 1))

    level = one(*cuts[0])
    for cut in cuts[1:]:
        level = level * one(*cut)
    return level


def bell_draw(own_key, extent, spread, limit, split=(), held_as=jnp.bfloat16):
    entries = spread * jax.random.normal(own_key, extent, jnp.float32)
    if split:
        entries = entries * block_scale(own_key, extent, split, -0.22, 0.18)
    return jnp.clip(entries, -limit, limit).astype(held_as)


def setup_inputs(seed: int = 0) -> dict:
    splits = jax.random.split(jax.random.key(seed), 7)
    queries = bell_draw(splits[0], (BATCH, SEQ, HEADS * HEAD_DIM), 1.0, 6.0, ((0, 4), (1, 8)))
    keys = draw_keys(jax.random.fold_in(splits[6], 71), 0)
    values = bell_draw(splits[2], (BATCH, SEQ, 2, HEADS * HEAD_DIM), 1.0, 6.0, ((0, 4), (1, 8)))
    betas = jnp.clip(0.3 + 1.3 * jax.random.uniform(splits[3], (BATCH, HEADS, 2, SEQ), jnp.float32) ** block_scale(splits[3], (BATCH, HEADS, 2, SEQ), ((0, 4), (3, 8)), -0.2, 0.2), 0.3, 1.6)
    grad_out = draw_grad_out(jax.random.fold_in(splits[6], 71), 0)
    gain = jnp.clip(1.0 + 0.18 * jax.random.normal(splits[5], (HEADS * HEAD_DIM,), jnp.float32), 0.1, 1.9)
    return {"queries": queries, "keys": keys, "values": values, "betas": betas, "grad_out": grad_out, "gain": gain}


EXACT = lax.Precision.HIGHEST

def product(left, right):
    return jnp.dot(left, right, precision=EXACT)

def unit_rows(raw):
    return raw * lax.rsqrt(lax.optimization_barrier(jnp.sum(raw * raw, axis=-1, keepdims=True)) + 1e-06)

def block_step(state, pieces):
    query_blk, key_blk, value_blk, rate_blk = pieces
    span = query_blk.shape[0]
    refl = key_blk.shape[0]
    token_ids = lax.broadcasted_iota(jnp.int32, (span, refl), 0)
    refl_ids = lax.broadcasted_iota(jnp.int32, (span, refl), 1)
    read_mask = (refl_ids <= 2 * token_ids + 1).astype(jnp.float32)
    row_ids = lax.broadcasted_iota(jnp.int32, (refl, refl), 0)
    col_ids = lax.broadcasted_iota(jnp.int32, (refl, refl), 1)
    strict = (col_ids < row_ids).astype(jnp.float32)
    lower_mat = jnp.eye(refl, dtype=jnp.float32) + rate_blk[:, None] * product(key_blk, key_blk.T) * strict
    target = rate_blk[:, None] * (value_blk - product(key_blk, state.T))
    update = jax.scipy.linalg.solve_triangular(lower_mat, target, lower=True)
    scores = product(query_blk, key_blk.T) * read_mask
    output = product(query_blk, state.T) + product(scores, update)
    return (state + product(update.T, key_blk), output)

def segment_step(state, pieces):
    return lax.scan(jax.checkpoint(block_step), state, pieces)

def head_output(query_n, key_n, value_f, rate_f):
    segments = N_OUTER * N_INNER
    per_seg = TOK_DEV // STRETCH
    pieces = (query_n.reshape(segments, per_seg, STRETCH, HEAD_DIM), key_n.reshape(segments, per_seg, 2 * STRETCH, HEAD_DIM), value_f.reshape(segments, per_seg, 2 * STRETCH, HEAD_DIM), rate_f.reshape(segments, per_seg, 2 * STRETCH))
    start = jnp.zeros((HEAD_DIM, HEAD_DIM), jnp.float32)
    final_state, outputs = lax.scan(jax.checkpoint(segment_step), start, pieces)
    return outputs.reshape(SEQ, HEAD_DIM)

def pair_grads(index, queries, keys, values, betas, grad_out, gain):
    batch_id = (index // HEADS).astype(jnp.int32)
    head_id = (index % HEADS).astype(jnp.int32)
    zero_id = jnp.zeros((), jnp.int32)
    column = (head_id * HEAD_DIM).astype(jnp.int32)
    query_h = lax.dynamic_slice(queries, (batch_id, zero_id, column), (1, SEQ, HEAD_DIM))[0].astype(jnp.float32)
    key_h = lax.dynamic_slice(keys, (batch_id, zero_id, zero_id, column), (1, SEQ, 2, HEAD_DIM))[0].astype(jnp.float32)
    value_h = lax.dynamic_slice(values, (batch_id, zero_id, zero_id, column), (1, SEQ, 2, HEAD_DIM))[0].astype(jnp.float32)
    rate_h = lax.dynamic_slice(betas, (batch_id, head_id, zero_id, zero_id), (1, 1, 2, SEQ))[0, 0]
    cotan_h = lax.dynamic_slice(grad_out, (batch_id, zero_id, column), (1, SEQ, HEAD_DIM))[0].astype(jnp.float32)
    gain_h = lax.dynamic_slice(gain, (column,), (HEAD_DIM,))
    rate_f = rate_h.T.reshape(2 * SEQ)

    def forward(query_raw, key_raw, value_raw, gain_raw):
        query_n = unit_rows(query_raw)
        key_n = unit_rows(key_raw).reshape(2 * SEQ, HEAD_DIM)
        output = head_output(query_n, key_n, value_raw.reshape(2 * SEQ, HEAD_DIM), rate_f)
        scale_inv = lax.rsqrt(lax.optimization_barrier(jnp.mean(output * output, axis=-1, keepdims=True)) + 1e-05)
        return output * scale_inv * gain_raw[None, :]
    result, pullback = jax.vjp(forward, query_h, key_h, value_h, gain_h)
    return pullback(cotan_h)

def reference(queries, keys, values, betas, grad_out, gain):
    indices = jnp.arange(BATCH * HEADS, dtype=jnp.int32)
    grad_q, grad_k, grad_v, grad_g = lax.map(lambda index: pair_grads(index, queries, keys, values, betas, grad_out, gain), indices)
    grad_q = grad_q.reshape(BATCH, HEADS, SEQ, HEAD_DIM).transpose(0, 2, 1, 3).reshape(BATCH, SEQ, HEADS * HEAD_DIM)
    grad_k = grad_k.reshape(BATCH, HEADS, SEQ, 2, HEAD_DIM).transpose(0, 2, 3, 1, 4).reshape(BATCH, SEQ, 2, HEADS * HEAD_DIM)
    grad_v = grad_v.reshape(BATCH, HEADS, SEQ, 2, HEAD_DIM).transpose(0, 2, 3, 1, 4).reshape(BATCH, SEQ, 2, HEADS * HEAD_DIM)
    grad_g = lax.optimization_barrier(jnp.sum(grad_g.reshape(BATCH, HEADS, HEAD_DIM), axis=0)).reshape(HEADS * HEAD_DIM)
    factor = 1.0 / jnp.sqrt(jnp.float32(BATCH * SEQ))
    return (grad_q.astype(jnp.bfloat16), grad_k.astype(jnp.bfloat16), grad_v.astype(jnp.bfloat16), grad_g * factor)
```

```python
import math

import jax
import jax.numpy as jnp
from jax import lax
from jax.sharding import PartitionSpec as P

HEADS = 8
HEAD_DIM = 128
STRETCH = 64


EXACT = lax.Precision.HIGHEST
EPS_KEY = 1e-06
EPS_OUT = 1e-05


def product(spec, left, right):
    return jnp.einsum(spec, left, right, precision=EXACT, preferred_element_type=jnp.float32)


def unit_rows(raw):
    scale_inv = lax.rsqrt(jnp.sum(raw * raw, axis=-1, keepdims=True) + EPS_KEY)
    return (raw * scale_inv, scale_inv)


def unit_back(unit, scale_inv, grad):
    return scale_inv * (grad - unit * jnp.sum(unit * grad, axis=-1, keepdims=True))


def compose(earlier, later):
    through = product("mhij,hjk->mhik", earlier, later[0])
    return through + jnp.stack([jnp.zeros_like(later[1]), later[1]])


def unit_lower_inverse(lower_mat):
    size = lower_mat.shape[-1]
    row_ids = lax.broadcasted_iota(jnp.int32, (size, size), 0)
    col_ids = lax.broadcasted_iota(jnp.int32, (size, size), 1)
    eye = (row_ids == col_ids).astype(jnp.float32)
    first = ((row_ids // 2) == (col_ids // 2)) & (row_ids > col_ids)
    inverse = eye - lower_mat * first.astype(jnp.float32)
    width = 2
    while width < size:
        inside = (row_ids // (2 * width)) == (col_ids // (2 * width))
        below = (row_ids // width) > (col_ids // width)
        coupling = lower_mat * (inside & below).astype(jnp.float32)
        left = product("bij,bjk->bik", inverse, coupling)
        inverse = inverse - product("bij,bjk->bik", left, inverse)
        width *= 2
    return inverse


def stretch_factors(key_blk, value_blk, rate_blk, inverse, eye_head):
    head_dim = key_blk.shape[2]
    rhs = jnp.concatenate(
        [rate_blk[:, :, None] * key_blk, rate_blk[:, :, None] * value_blk], axis=2
    )
    solved = product("hrs,hsd->hrd", inverse, rhs)
    w_mat = solved[:, :, :head_dim]
    t_vals = solved[:, :, head_dim:]
    transit = eye_head - product("hrd,hre->hde", w_mat, key_blk)
    return (inverse, w_mat, t_vals, transit)


def scan_maps(own_map, identity, step):
    axes = ("outer", "inner")
    size = lax.axis_size("outer") * lax.axis_size("inner")
    here = lax.axis_index("outer") * lax.axis_size("inner") + lax.axis_index("inner")

    def shifted(block, distance):
        route = [(i, i + step * distance) for i in range(size) if 0 <= i + step * distance < size]
        return lax.ppermute(block, axes, route)

    def reached(distance):
        source = here - step * distance
        return (source >= 0) & (source < size)

    excl = jnp.where(reached(1), shifted(own_map, 1), identity)
    incl = compose(excl, own_map)
    distance = 2
    while distance < size:
        if 2 * distance >= size:
            got = shifted(incl[1], distance)
            state = product("hij,hjk->hik", got, excl[0]) + excl[1]
            return jnp.where(reached(distance), state, excl[1])
        got = shifted(incl, distance)
        ok = reached(distance)
        excl = jnp.where(ok, compose(got, excl), excl)
        incl = jnp.where(ok, compose(got, incl), incl)
        distance *= 2
    return excl[1]


def on_device(queries, keys, values, betas, grad_out, gain):
    length_here = queries.shape[1]
    heads = HEADS
    head_dim = HEAD_DIM
    span = STRETCH
    refl = 2 * span
    count = length_here // span
    query_raw = (
        queries[0].astype(jnp.float32).reshape(length_here, heads, head_dim).transpose(1, 0, 2)
    )
    key_raw = (
        keys[0]
        .astype(jnp.float32)
        .reshape(length_here, 2, heads, head_dim)
        .transpose(2, 0, 1, 3)
        .reshape(heads, 2 * length_here, head_dim)
    )
    value_all = (
        values[0]
        .astype(jnp.float32)
        .reshape(length_here, 2, heads, head_dim)
        .transpose(2, 0, 1, 3)
        .reshape(heads, 2 * length_here, head_dim)
    )
    rate_all = betas[0].transpose(0, 2, 1).reshape(heads, 2 * length_here)
    cotan_all = (
        grad_out[0].astype(jnp.float32).reshape(length_here, heads, head_dim).transpose(1, 0, 2)
    )
    gains = gain.reshape(heads, head_dim)
    query_n, query_inv = unit_rows(query_raw)
    key_n, key_inv = unit_rows(key_raw)
    token_ids = lax.broadcasted_iota(jnp.int32, (span, refl), 0)
    refl_ids = lax.broadcasted_iota(jnp.int32, (span, refl), 1)
    read_mask = (refl_ids <= 2 * token_ids + 1).astype(jnp.float32)
    row_ids = lax.broadcasted_iota(jnp.int32, (refl, refl), 0)
    col_ids = lax.broadcasted_iota(jnp.int32, (refl, refl), 1)
    strict = (col_ids < row_ids).astype(jnp.float32)
    eye_refl = jnp.eye(refl, dtype=jnp.float32)
    eye_head = jnp.eye(head_dim, dtype=jnp.float32)
    identity = jnp.stack(
        [
            jnp.broadcast_to(eye_head, (heads, head_dim, head_dim)),
            jnp.zeros((heads, head_dim, head_dim), jnp.float32),
        ]
    )

    def refl_rows(array, block_id):
        return array[:, block_id * refl : (block_id + 1) * refl]

    def token_rows(array, block_id):
        return array[:, block_id * span : (block_id + 1) * span]

    lower_all = []
    for block_id in range(count):
        key_blk = refl_rows(key_n, block_id)
        gram = product("hrd,hsd->hrs", key_blk, key_blk)
        lower_all.append(eye_refl + refl_rows(rate_all, block_id)[:, :, None] * gram * strict)
    inverse_all = unit_lower_inverse(jnp.concatenate(lower_all, axis=0)).reshape(
        count, heads, refl, refl
    )
    stash = []
    block_map = identity
    for block_id in range(count):
        key_blk = refl_rows(key_n, block_id)
        factor_set = stretch_factors(
            key_blk,
            refl_rows(value_all, block_id),
            refl_rows(rate_all, block_id),
            inverse_all[block_id],
            eye_head,
        )
        offset = product("hrv,hre->hve", factor_set[2], key_blk)
        block_map = compose(block_map, jnp.stack([factor_set[3], offset]))
        stash.append(factor_set)

    def factors_of(block_id):
        return stash[block_id]

    state = scan_maps(block_map, identity, 1)
    records = []
    adjoint_maps = []
    gain_sum = jnp.zeros((heads, head_dim), jnp.float32)
    for block_id in range(count):
        inverse, w_mat, t_vals, transit = factors_of(block_id)
        key_blk = refl_rows(key_n, block_id)
        query_blk = token_rows(query_n, block_id)
        cotan_blk = token_rows(cotan_all, block_id)
        update = t_vals - product("hrk,hvk->hrv", w_mat, state)
        scores = product("htd,hrd->htr", query_blk, key_blk) * read_mask
        output = product("htk,hvk->htv", query_blk, state) + product("htr,hrv->htv", scores, update)
        scale_inv = lax.rsqrt(jnp.mean(output * output, axis=2, keepdims=True) + EPS_OUT)
        normed = output * scale_inv
        scaled = cotan_blk * gains[:, None, :]
        d_out = scale_inv * (scaled - normed * jnp.mean(normed * scaled, axis=2, keepdims=True))
        gain_sum = gain_sum + jnp.sum(cotan_blk * normed, axis=1)
        source = product("htv,htk->hvk", d_out, query_blk - product("htr,hrk->htk", scores, w_mat))
        records.append((state, update, scores, d_out))
        adjoint_maps.append(jnp.stack([jnp.swapaxes(transit, 1, 2), source]))
        state = state + product("hrv,hrk->hvk", update, key_blk)
    adjoint_block = identity
    for block_id in reversed(range(count)):
        adjoint_block = compose(adjoint_block, adjoint_maps[block_id])
    adjoint = scan_maps(adjoint_block, identity, -1)
    grad_q_parts = [None] * count
    grad_k_parts = [None] * count
    grad_v_parts = [None] * count
    for block_id in reversed(range(count)):
        inverse, w_mat, t_vals, transit = factors_of(block_id)
        start_state, update, scores, d_out = records[block_id]
        key_blk = refl_rows(key_n, block_id)
        query_blk = token_rows(query_n, block_id)
        rate_blk = refl_rows(rate_all, block_id)
        d_update = product("htr,htv->hrv", scores, d_out) + product(
            "hrk,hvk->hrv", key_blk, adjoint
        )
        solved = product("hsr,hsv->hrv", inverse, d_update)
        d_target = rate_blk[:, :, None] * solved
        d_scores = product("htv,hrv->htr", d_out, update) * read_mask
        grad_q_parts[block_id] = product("htv,hvk->htk", d_out, start_state) + product(
            "htr,hrk->htk", d_scores, key_blk
        )
        d_gram = -product("hrv,hsv->hrs", d_target, update) * strict
        grad_k_parts[block_id] = (
            product("hrv,hvk->hrk", update, adjoint)
            + product("htr,htk->hrk", d_scores, query_blk)
            - product("hrv,hvk->hrk", d_target, start_state)
            + product("hrs,hsk->hrk", d_gram + jnp.swapaxes(d_gram, 1, 2), key_blk)
        )
        grad_v_parts[block_id] = d_target
        adjoint = (
            adjoint
            + product("htv,htk->hvk", d_out, query_blk)
            - product("hrv,hrk->hvk", d_target, key_blk)
        )
    grad_qn = jnp.concatenate(grad_q_parts, axis=1)
    grad_kn = jnp.concatenate(grad_k_parts, axis=1)
    grad_val = jnp.concatenate(grad_v_parts, axis=1)
    grad_q = unit_back(query_n, query_inv, grad_qn)
    grad_k = unit_back(key_n, key_inv, grad_kn)
    grad_q = (
        grad_q.transpose(1, 0, 2).reshape(1, length_here, heads * head_dim).astype(jnp.bfloat16)
    )
    grad_k = (
        grad_k.reshape(heads, length_here, 2, head_dim)
        .transpose(1, 2, 0, 3)
        .reshape(1, length_here, 2, heads * head_dim)
        .astype(jnp.bfloat16)
    )
    grad_val = (
        grad_val.reshape(heads, length_here, 2, head_dim)
        .transpose(1, 2, 0, 3)
        .reshape(1, length_here, 2, heads * head_dim)
        .astype(jnp.bfloat16)
    )
    total = jnp.sum(lax.all_gather(gain_sum, ("dp", "outer", "inner")), axis=0)
    tokens_all = length_here * lax.axis_size("dp") * lax.axis_size("outer") * lax.axis_size("inner")
    gain_grad = total.reshape(heads * head_dim) * (1.0 / math.sqrt(tokens_all))
    return (grad_q, grad_k, grad_val, gain_grad)


def solution(mesh):
    return jax.shard_map(
        on_device,
        mesh=mesh,
        in_specs=(
            P("dp", ("outer", "inner"), None),
            P("dp", ("outer", "inner"), None, None),
            P("dp", ("outer", "inner"), None, None),
            P("dp", None, None, ("outer", "inner")),
            P("dp", ("outer", "inner"), None),
            P(),
        ),
        out_specs=(
            P("dp", ("outer", "inner"), None),
            P("dp", ("outer", "inner"), None, None),
            P("dp", ("outer", "inner"), None, None),
            P(),
        ),
        check_vma=False,
    )
```

```python
import math

import jax
import jax.numpy as jnp
from jax import lax
from jax.sharding import PartitionSpec as P

HEADS = 8
HEAD_DIM = 128
STRETCH = 64


EXACT = lax.Precision.HIGHEST
EPS_KEY = 1e-06
EPS_OUT = 1e-05


def total_over(value, axes):
    size = 1
    for axis in axes:
        size *= lax.axis_size(axis)
    if size & (size - 1):
        return lax.psum(value, axes)
    distance = 1
    while distance < size:
        route = [(i, i ^ distance) for i in range(size)]
        value = value + lax.ppermute(value, axes, route)
        distance *= 2
    return value


def product(spec, left, right):
    return jnp.einsum(spec, left, right, precision=EXACT, preferred_element_type=jnp.float32)


def unit_rows(raw):
    scale_inv = lax.rsqrt(jnp.sum(raw * raw, axis=-1, keepdims=True) + EPS_KEY)
    return (raw * scale_inv, scale_inv)


def unit_back(unit, scale_inv, grad):
    along = lax.optimization_barrier(jnp.sum(unit * grad, axis=-1, keepdims=True))
    return scale_inv * (grad - unit * along)


def compose(earlier, later):
    through = product("mhij,hjk->mhik", earlier, later[0])
    return through + jnp.stack([jnp.zeros_like(later[1]), later[1]])


def unit_lower_inverse(lower_mat):
    size = lower_mat.shape[-1]
    row_ids = lax.broadcasted_iota(jnp.int32, (size, size), 0)
    col_ids = lax.broadcasted_iota(jnp.int32, (size, size), 1)
    eye = (row_ids == col_ids).astype(jnp.float32)
    first = ((row_ids // 2) == (col_ids // 2)) & (row_ids > col_ids)
    inverse = eye - lower_mat * first.astype(jnp.float32)
    width = 2
    while width < size:
        inside = (row_ids // (2 * width)) == (col_ids // (2 * width))
        below = (row_ids // width) > (col_ids // width)
        coupling = lower_mat * (inside & below).astype(jnp.float32)
        left = product("bij,bjk->bik", inverse, coupling)
        inverse = inverse - product("bij,bjk->bik", left, inverse)
        width *= 2
    return inverse


def stretch_factors(key_blk, value_blk, rate_blk, inverse, eye_head):
    head_dim = key_blk.shape[2]
    rhs = jnp.concatenate(
        [rate_blk[:, :, None] * key_blk, rate_blk[:, :, None] * value_blk], axis=2
    )
    solved = product("hrs,hsd->hrd", inverse, rhs)
    w_mat = solved[:, :, :head_dim]
    t_vals = solved[:, :, head_dim:]
    transit = eye_head - product("hrd,hre->hde", w_mat, key_blk)
    return (inverse, w_mat, t_vals, transit)


def scan_maps(own_map, identity, step):
    axes = ("outer", "inner")
    size = lax.axis_size("outer") * lax.axis_size("inner")
    here = lax.axis_index("outer") * lax.axis_size("inner") + lax.axis_index("inner")

    def shifted(block, distance):
        route = [(i, i + step * distance) for i in range(size) if 0 <= i + step * distance < size]
        return lax.ppermute(block, axes, route)

    def reached(distance):
        source = here - step * distance
        return (source >= 0) & (source < size)

    excl = jnp.where(reached(1), shifted(own_map, 1), identity)
    incl = compose(excl, own_map)
    distance = 2
    while distance < size:
        if 2 * distance >= size:
            got = shifted(incl[1], distance)
            state = product("hij,hjk->hik", got, excl[0]) + excl[1]
            return jnp.where(reached(distance), state, excl[1])
        got = shifted(incl, distance)
        ok = reached(distance)
        excl = jnp.where(ok, compose(got, excl), excl)
        incl = jnp.where(ok, compose(got, incl), incl)
        distance *= 2
    return excl[1]


def on_device(queries, keys, values, betas, grad_out, gain):
    length_here = queries.shape[1]
    heads = HEADS
    head_dim = HEAD_DIM
    span = STRETCH
    refl = 2 * span
    count = length_here // span
    query_raw = (
        queries[0].astype(jnp.float32).reshape(length_here, heads, head_dim).transpose(1, 0, 2)
    )
    key_raw = (
        keys[0]
        .astype(jnp.float32)
        .reshape(length_here, 2, heads, head_dim)
        .transpose(2, 0, 1, 3)
        .reshape(heads, 2 * length_here, head_dim)
    )
    value_all = (
        values[0]
        .astype(jnp.float32)
        .reshape(length_here, 2, heads, head_dim)
        .transpose(2, 0, 1, 3)
        .reshape(heads, 2 * length_here, head_dim)
    )
    rate_all = betas[0].transpose(0, 2, 1).reshape(heads, 2 * length_here)
    cotan_all = (
        grad_out[0].astype(jnp.float32).reshape(length_here, heads, head_dim).transpose(1, 0, 2)
    )
    gains = gain.reshape(heads, head_dim)
    query_n, query_inv = unit_rows(query_raw)
    key_n, key_inv = unit_rows(key_raw)
    token_ids = lax.broadcasted_iota(jnp.int32, (span, refl), 0)
    refl_ids = lax.broadcasted_iota(jnp.int32, (span, refl), 1)
    read_mask = (refl_ids <= 2 * token_ids + 1).astype(jnp.float32)
    row_ids = lax.broadcasted_iota(jnp.int32, (refl, refl), 0)
    col_ids = lax.broadcasted_iota(jnp.int32, (refl, refl), 1)
    strict = (col_ids < row_ids).astype(jnp.float32)
    eye_refl = jnp.eye(refl, dtype=jnp.float32)
    eye_head = jnp.eye(head_dim, dtype=jnp.float32)
    identity = jnp.stack(
        [
            jnp.broadcast_to(eye_head, (heads, head_dim, head_dim)),
            jnp.zeros((heads, head_dim, head_dim), jnp.float32),
        ]
    )

    def refl_rows(array, block_id):
        return array[:, block_id * refl : (block_id + 1) * refl]

    def token_rows(array, block_id):
        return array[:, block_id * span : (block_id + 1) * span]

    lower_all = []
    for block_id in range(count):
        key_blk = refl_rows(key_n, block_id)
        gram = product("hrd,hsd->hrs", key_blk, key_blk)
        lower_all.append(eye_refl + refl_rows(rate_all, block_id)[:, :, None] * gram * strict)
    inverse_all = unit_lower_inverse(jnp.concatenate(lower_all, axis=0)).reshape(
        count, heads, refl, refl
    )
    stash = []
    block_map = identity
    for block_id in range(count):
        key_blk = refl_rows(key_n, block_id)
        factor_set = stretch_factors(
            key_blk,
            refl_rows(value_all, block_id),
            refl_rows(rate_all, block_id),
            inverse_all[block_id],
            eye_head,
        )
        offset = product("hrv,hre->hve", factor_set[2], key_blk)
        block_map = compose(block_map, jnp.stack([factor_set[3], offset]))
        stash.append(factor_set)

    def factors_of(block_id):
        return stash[block_id]

    state = scan_maps(block_map, identity, 1)
    records = []
    adjoint_maps = []
    gain_sum = jnp.zeros((heads, head_dim), jnp.float32)
    for block_id in range(count):
        inverse, w_mat, t_vals, transit = factors_of(block_id)
        key_blk = refl_rows(key_n, block_id)
        query_blk = token_rows(query_n, block_id)
        cotan_blk = token_rows(cotan_all, block_id)
        update = t_vals - product("hrk,hvk->hrv", w_mat, state)
        scores = product("htd,hrd->htr", query_blk, key_blk) * read_mask
        output = product("htk,hvk->htv", query_blk, state) + product("htr,hrv->htv", scores, update)
        scale_inv = lax.rsqrt(jnp.mean(output * output, axis=2, keepdims=True) + EPS_OUT)
        normed = output * scale_inv
        scaled = cotan_blk * gains[:, None, :]
        d_out = scale_inv * (scaled - normed * jnp.mean(normed * scaled, axis=2, keepdims=True))
        gain_sum = gain_sum + jnp.sum(cotan_blk * normed, axis=1)
        source = product("htv,htk->hvk", d_out, query_blk - product("htr,hrk->htk", scores, w_mat))
        records.append((state, update, scores, d_out))
        adjoint_maps.append(jnp.stack([jnp.swapaxes(transit, 1, 2), source]))
        state = state + product("hrv,hrk->hvk", update, key_blk)
    adjoint_block = identity
    for block_id in reversed(range(count)):
        adjoint_block = compose(adjoint_block, adjoint_maps[block_id])
    adjoint = scan_maps(adjoint_block, identity, -1)
    grad_q_parts = [None] * count
    grad_k_parts = [None] * count
    grad_v_parts = [None] * count
    for block_id in reversed(range(count)):
        inverse, w_mat, t_vals, transit = factors_of(block_id)
        start_state, update, scores, d_out = records[block_id]
        key_blk = refl_rows(key_n, block_id)
        query_blk = token_rows(query_n, block_id)
        rate_blk = refl_rows(rate_all, block_id)
        d_update = product("htr,htv->hrv", scores, d_out) + product(
            "hrk,hvk->hrv", key_blk, adjoint
        )
        solved = product("hsr,hsv->hrv", inverse, d_update)
        d_target = rate_blk[:, :, None] * solved
        d_scores = product("htv,hrv->htr", d_out, update) * read_mask
        grad_q_parts[block_id] = product("htv,hvk->htk", d_out, start_state) + product(
            "htr,hrk->htk", d_scores, key_blk
        )
        d_gram = -product("hrv,hsv->hrs", d_target, update) * strict
        grad_k_parts[block_id] = (
            product("hrv,hvk->hrk", update, adjoint)
            + product("htr,htk->hrk", d_scores, query_blk)
            - product("hrv,hvk->hrk", d_target, start_state)
            + product("hrs,hsk->hrk", d_gram + jnp.swapaxes(d_gram, 1, 2), key_blk)
        )
        grad_v_parts[block_id] = d_target
        adjoint = (
            adjoint
            + product("htv,htk->hvk", d_out, query_blk)
            - product("hrv,hrk->hvk", d_target, key_blk)
        )
    grad_qn = jnp.concatenate(grad_q_parts, axis=1)
    grad_kn = jnp.concatenate(grad_k_parts, axis=1)
    grad_val = jnp.concatenate(grad_v_parts, axis=1)
    grad_q = unit_back(query_n, query_inv, grad_qn)
    grad_k = unit_back(key_n, key_inv, grad_kn)
    grad_q = (
        grad_q.transpose(1, 0, 2).reshape(1, length_here, heads * head_dim).astype(jnp.bfloat16)
    )
    grad_k = (
        grad_k.reshape(heads, length_here, 2, head_dim)
        .transpose(1, 2, 0, 3)
        .reshape(1, length_here, 2, heads * head_dim)
        .astype(jnp.bfloat16)
    )
    grad_val = (
        grad_val.reshape(heads, length_here, 2, head_dim)
        .transpose(1, 2, 0, 3)
        .reshape(1, length_here, 2, heads * head_dim)
        .astype(jnp.bfloat16)
    )
    total = total_over(gain_sum, ("dp", "outer", "inner"))
    tokens_all = length_here * lax.axis_size("dp") * lax.axis_size("outer") * lax.axis_size("inner")
    gain_grad = total.reshape(heads * head_dim) * (1.0 / math.sqrt(tokens_all))
    return (grad_q, grad_k, grad_val, gain_grad)


def solution(mesh):
    return jax.shard_map(
        on_device,
        mesh=mesh,
        in_specs=(
            P("dp", ("outer", "inner"), None),
            P("dp", ("outer", "inner"), None, None),
            P("dp", ("outer", "inner"), None, None),
            P("dp", None, None, ("outer", "inner")),
            P("dp", ("outer", "inner"), None),
            P(),
        ),
        out_specs=(
            P("dp", ("outer", "inner"), None),
            P("dp", ("outer", "inner"), None, None),
            P("dp", ("outer", "inner"), None, None),
            P(),
        ),
        check_vma=False,
    )
```

```python
import math

import jax
import jax.numpy as jnp
from jax import lax
from jax.sharding import PartitionSpec as P

HEADS = 8
HEAD_DIM = 128
STRETCH = 64


EXACT = lax.Precision.HIGHEST
EPS_KEY = 1e-06
EPS_OUT = 1e-05


def total_over(value, axes):
    size = 1
    for axis in axes:
        size *= lax.axis_size(axis)
    if size & (size - 1):
        return lax.psum(value, axes)
    distance = 1
    while distance < size:
        route = [(i, i ^ distance) for i in range(size)]
        value = value + lax.ppermute(value, axes, route)
        distance *= 2
    return value


def product(spec, left, right):
    return jnp.einsum(spec, left, right, precision=EXACT, preferred_element_type=jnp.float32)


def unit_rows(raw):
    scale_inv = lax.rsqrt(jnp.sum(raw * raw, axis=-1, keepdims=True) + EPS_KEY)
    return (raw * scale_inv, scale_inv)


def unit_back(unit, scale_inv, grad):
    width = unit.shape[-1]
    ones = jnp.ones((width, width), jnp.float32)
    along = product("hrd,de->hre", unit * grad, ones)
    return scale_inv * (grad - unit * along)


def compose(earlier, later):
    through = product("mhij,hjk->mhik", earlier, later[0])
    return through + jnp.stack([jnp.zeros_like(later[1]), later[1]])


def unit_lower_inverse(lower_mat):
    size = lower_mat.shape[-1]
    row_ids = lax.broadcasted_iota(jnp.int32, (size, size), 0)
    col_ids = lax.broadcasted_iota(jnp.int32, (size, size), 1)
    eye = (row_ids == col_ids).astype(jnp.float32)
    first = ((row_ids // 2) == (col_ids // 2)) & (row_ids > col_ids)
    inverse = eye - lower_mat * first.astype(jnp.float32)
    width = 2
    while width < size:
        inside = (row_ids // (2 * width)) == (col_ids // (2 * width))
        below = (row_ids // width) > (col_ids // width)
        coupling = lower_mat * (inside & below).astype(jnp.float32)
        left = product("bij,bjk->bik", inverse, coupling)
        inverse = inverse - product("bij,bjk->bik", left, inverse)
        width *= 2
    return inverse


def stretch_factors(key_blk, value_blk, rate_blk, inverse, eye_head):
    head_dim = key_blk.shape[2]
    rhs = jnp.concatenate(
        [rate_blk[:, :, None] * key_blk, rate_blk[:, :, None] * value_blk], axis=2
    )
    solved = product("hrs,hsd->hrd", inverse, rhs)
    w_mat = solved[:, :, :head_dim]
    t_vals = solved[:, :, head_dim:]
    transit = eye_head - product("hrd,hre->hde", w_mat, key_blk)
    return (inverse, w_mat, t_vals, transit)


def scan_maps(own_map, identity, step):
    axes = ("outer", "inner")
    size = lax.axis_size("outer") * lax.axis_size("inner")
    here = lax.axis_index("outer") * lax.axis_size("inner") + lax.axis_index("inner")

    def shifted(block, distance):
        route = [(i, i + step * distance) for i in range(size) if 0 <= i + step * distance < size]
        return lax.ppermute(block, axes, route)

    def reached(distance):
        source = here - step * distance
        return (source >= 0) & (source < size)

    excl = jnp.where(reached(1), shifted(own_map, 1), identity)
    incl = compose(excl, own_map)
    distance = 2
    while distance < size:
        if 2 * distance >= size:
            got = shifted(incl[1], distance)
            state = product("hij,hjk->hik", got, excl[0]) + excl[1]
            return jnp.where(reached(distance), state, excl[1])
        got = shifted(incl, distance)
        ok = reached(distance)
        excl = jnp.where(ok, compose(got, excl), excl)
        incl = jnp.where(ok, compose(got, incl), incl)
        distance *= 2
    return excl[1]


def on_device(queries, keys, values, betas, grad_out, gain):
    length_here = queries.shape[1]
    heads = HEADS
    head_dim = HEAD_DIM
    span = STRETCH
    refl = 2 * span
    count = length_here // span
    query_raw = (
        queries[0].astype(jnp.float32).reshape(length_here, heads, head_dim).transpose(1, 0, 2)
    )
    key_raw = (
        keys[0]
        .astype(jnp.float32)
        .reshape(length_here, 2, heads, head_dim)
        .transpose(2, 0, 1, 3)
        .reshape(heads, 2 * length_here, head_dim)
    )
    value_all = (
        values[0]
        .astype(jnp.float32)
        .reshape(length_here, 2, heads, head_dim)
        .transpose(2, 0, 1, 3)
        .reshape(heads, 2 * length_here, head_dim)
    )
    rate_all = betas[0].transpose(0, 2, 1).reshape(heads, 2 * length_here)
    cotan_all = (
        grad_out[0].astype(jnp.float32).reshape(length_here, heads, head_dim).transpose(1, 0, 2)
    )
    gains = gain.reshape(heads, head_dim)
    query_n, query_inv = unit_rows(query_raw)
    key_n, key_inv = unit_rows(key_raw)
    token_ids = lax.broadcasted_iota(jnp.int32, (span, refl), 0)
    refl_ids = lax.broadcasted_iota(jnp.int32, (span, refl), 1)
    read_mask = (refl_ids <= 2 * token_ids + 1).astype(jnp.float32)
    row_ids = lax.broadcasted_iota(jnp.int32, (refl, refl), 0)
    col_ids = lax.broadcasted_iota(jnp.int32, (refl, refl), 1)
    strict = (col_ids < row_ids).astype(jnp.float32)
    eye_refl = jnp.eye(refl, dtype=jnp.float32)
    eye_head = jnp.eye(head_dim, dtype=jnp.float32)
    identity = jnp.stack(
        [
            jnp.broadcast_to(eye_head, (heads, head_dim, head_dim)),
            jnp.zeros((heads, head_dim, head_dim), jnp.float32),
        ]
    )

    def refl_rows(array, block_id):
        return array[:, block_id * refl : (block_id + 1) * refl]

    def token_rows(array, block_id):
        return array[:, block_id * span : (block_id + 1) * span]

    lower_all = []
    for block_id in range(count):
        key_blk = refl_rows(key_n, block_id)
        gram = product("hrd,hsd->hrs", key_blk, key_blk)
        lower_all.append(eye_refl + refl_rows(rate_all, block_id)[:, :, None] * gram * strict)
    inverse_all = unit_lower_inverse(jnp.concatenate(lower_all, axis=0)).reshape(
        count, heads, refl, refl
    )
    stash = []
    block_map = identity
    for block_id in range(count):
        key_blk = refl_rows(key_n, block_id)
        factor_set = stretch_factors(
            key_blk,
            refl_rows(value_all, block_id),
            refl_rows(rate_all, block_id),
            inverse_all[block_id],
            eye_head,
        )
        offset = product("hrv,hre->hve", factor_set[2], key_blk)
        block_map = compose(block_map, jnp.stack([factor_set[3], offset]))
        stash.append(factor_set)

    def factors_of(block_id):
        return stash[block_id]

    state = scan_maps(block_map, identity, 1)
    records = []
    adjoint_maps = []
    gain_sum = jnp.zeros((heads, head_dim), jnp.float32)
    for block_id in range(count):
        inverse, w_mat, t_vals, transit = factors_of(block_id)
        key_blk = refl_rows(key_n, block_id)
        query_blk = token_rows(query_n, block_id)
        cotan_blk = token_rows(cotan_all, block_id)
        update = t_vals - product("hrk,hvk->hrv", w_mat, state)
        scores = product("htd,hrd->htr", query_blk, key_blk) * read_mask
        output = product("htk,hvk->htv", query_blk, state) + product("htr,hrv->htv", scores, update)
        scale_inv = lax.rsqrt(jnp.mean(output * output, axis=2, keepdims=True) + EPS_OUT)
        normed = output * scale_inv
        scaled = cotan_blk * gains[:, None, :]
        d_out = scale_inv * (scaled - normed * jnp.mean(normed * scaled, axis=2, keepdims=True))
        gain_sum = gain_sum + jnp.sum(cotan_blk * normed, axis=1)
        source = product("htv,htk->hvk", d_out, query_blk - product("htr,hrk->htk", scores, w_mat))
        records.append((state, update, scores, d_out))
        adjoint_maps.append(jnp.stack([jnp.swapaxes(transit, 1, 2), source]))
        state = state + product("hrv,hrk->hvk", update, key_blk)
    adjoint_block = identity
    for block_id in reversed(range(count)):
        adjoint_block = compose(adjoint_block, adjoint_maps[block_id])
    adjoint = scan_maps(adjoint_block, identity, -1)
    adjoint, gain_sum = lax.optimization_barrier((adjoint, gain_sum))
    grad_q_parts = [None] * count
    grad_k_parts = [None] * count
    grad_v_parts = [None] * count
    for block_id in reversed(range(count)):
        inverse, w_mat, t_vals, transit = factors_of(block_id)
        start_state, update, scores, d_out = records[block_id]
        key_blk = refl_rows(key_n, block_id)
        query_blk = token_rows(query_n, block_id)
        rate_blk = refl_rows(rate_all, block_id)
        d_update = product("htr,htv->hrv", scores, d_out) + product(
            "hrk,hvk->hrv", key_blk, adjoint
        )
        solved = product("hsr,hsv->hrv", inverse, d_update)
        d_target = rate_blk[:, :, None] * solved
        d_scores = product("htv,hrv->htr", d_out, update) * read_mask
        grad_q_parts[block_id] = product("htv,hvk->htk", d_out, start_state) + product(
            "htr,hrk->htk", d_scores, key_blk
        )
        d_gram = -product("hrv,hsv->hrs", d_target, update) * strict
        grad_k_parts[block_id] = (
            product("hrv,hvk->hrk", update, adjoint)
            + product("htr,htk->hrk", d_scores, query_blk)
            - product("hrv,hvk->hrk", d_target, start_state)
            + product("hrs,hsk->hrk", d_gram + jnp.swapaxes(d_gram, 1, 2), key_blk)
        )
        grad_v_parts[block_id] = d_target
        adjoint = (
            adjoint
            + product("htv,htk->hvk", d_out, query_blk)
            - product("hrv,hrk->hvk", d_target, key_blk)
        )
    grad_qn = jnp.concatenate(grad_q_parts, axis=1)
    grad_kn = jnp.concatenate(grad_k_parts, axis=1)
    grad_val = jnp.concatenate(grad_v_parts, axis=1)
    grad_q = unit_back(query_n, query_inv, grad_qn)
    grad_k = unit_back(key_n, key_inv, grad_kn)
    grad_q = (
        grad_q.transpose(1, 0, 2).reshape(1, length_here, heads * head_dim).astype(jnp.bfloat16)
    )
    grad_k = (
        grad_k.reshape(heads, length_here, 2, head_dim)
        .transpose(1, 2, 0, 3)
        .reshape(1, length_here, 2, heads * head_dim)
        .astype(jnp.bfloat16)
    )
    grad_val = (
        grad_val.reshape(heads, length_here, 2, head_dim)
        .transpose(1, 2, 0, 3)
        .reshape(1, length_here, 2, heads * head_dim)
        .astype(jnp.bfloat16)
    )
    total = total_over(gain_sum, ("dp", "outer", "inner"))
    tokens_all = length_here * lax.axis_size("dp") * lax.axis_size("outer") * lax.axis_size("inner")
    gain_grad = total.reshape(heads * head_dim) * (1.0 / math.sqrt(tokens_all))
    return (grad_q, grad_k, grad_val, gain_grad)


def solution(mesh):
    return jax.shard_map(
        on_device,
        mesh=mesh,
        in_specs=(
            P("dp", ("outer", "inner"), None),
            P("dp", ("outer", "inner"), None, None),
            P("dp", ("outer", "inner"), None, None),
            P("dp", None, None, ("outer", "inner")),
            P("dp", ("outer", "inner"), None),
            P(),
        ),
        out_specs=(
            P("dp", ("outer", "inner"), None),
            P("dp", ("outer", "inner"), None, None),
            P("dp", ("outer", "inner"), None, None),
            P(),
        ),
        check_vma=False,
    )
```

```python
import math

import jax
import jax.numpy as jnp
from jax import lax
from jax.sharding import PartitionSpec as P

HEADS = 8
HEAD_DIM = 128
STRETCH = 64


EXACT = lax.Precision.HIGHEST
EPS_KEY = 1e-06
EPS_OUT = 1e-05


def total_over(value, axes):
    size = 1
    for axis in axes:
        size *= lax.axis_size(axis)
    if size & (size - 1):
        return lax.psum(value, axes)
    distance = 1
    while distance < size:
        route = [(i, i ^ distance) for i in range(size)]
        value = value + lax.ppermute(value, axes, route)
        distance *= 2
    return value


def product(spec, left, right):
    return jnp.einsum(spec, left, right, precision=EXACT, preferred_element_type=jnp.float32)


def unit_rows(raw):
    scale_inv = lax.rsqrt(jnp.sum(raw * raw, axis=-1, keepdims=True) + EPS_KEY)
    return (raw * scale_inv, scale_inv)


def unit_back(unit, scale_inv, grad):
    width = unit.shape[-1]
    ones = jnp.ones((width, width), jnp.float32)
    along = product("hrd,de->hre", unit * grad, ones)
    return scale_inv * (grad - unit * along)


def compose(earlier, later):
    through = product("mhij,hjk->mhik", earlier, later[0])
    return through + jnp.stack([jnp.zeros_like(later[1]), later[1]])


def unit_lower_inverse(lower_mat):
    size = lower_mat.shape[-1]
    row_ids = lax.broadcasted_iota(jnp.int32, (size, size), 0)
    col_ids = lax.broadcasted_iota(jnp.int32, (size, size), 1)
    eye = (row_ids == col_ids).astype(jnp.float32)
    first = ((row_ids // 2) == (col_ids // 2)) & (row_ids > col_ids)
    inverse = eye - lower_mat * first.astype(jnp.float32)
    width = 2
    while width < size:
        inside = (row_ids // (2 * width)) == (col_ids // (2 * width))
        below = (row_ids // width) > (col_ids // width)
        coupling = lower_mat * (inside & below).astype(jnp.float32)
        left = product("bij,bjk->bik", inverse, coupling)
        inverse = inverse - product("bij,bjk->bik", left, inverse)
        width *= 2
    return inverse


def stretch_factors(key_blk, value_blk, rate_blk, inverse, eye_head):
    head_dim = key_blk.shape[2]
    rhs = jnp.concatenate(
        [rate_blk[:, :, None] * key_blk, rate_blk[:, :, None] * value_blk], axis=2
    )
    solved = product("hrs,hsd->hrd", inverse, rhs)
    w_mat = solved[:, :, :head_dim]
    t_vals = solved[:, :, head_dim:]
    transit = eye_head - product("hrd,hre->hde", w_mat, key_blk)
    return (inverse, w_mat, t_vals, transit)


def scan_maps(own_map, identity, step, axes):
    size = 1
    here = 0
    for axis in axes:
        size *= lax.axis_size(axis)
        here = here * lax.axis_size(axis) + lax.axis_index(axis)

    def shifted(block, distance):
        route = [(i, i + step * distance) for i in range(size) if 0 <= i + step * distance < size]
        return lax.ppermute(block, axes, route)

    def reached(distance):
        source = here - step * distance
        return (source >= 0) & (source < size)

    excl = jnp.where(reached(1), shifted(own_map, 1), identity)
    incl = compose(excl, own_map)
    distance = 2
    while distance < size:
        if 2 * distance >= size:
            got = shifted(incl[1], distance)
            state = product("hij,hjk->hik", got, excl[0]) + excl[1]
            return jnp.where(reached(distance), state, excl[1])
        got = shifted(incl, distance)
        ok = reached(distance)
        excl = jnp.where(ok, compose(got, excl), excl)
        incl = jnp.where(ok, compose(got, incl), incl)
        distance *= 2
    return excl[1]


def scan_split(own_map, identity, step):
    heads = own_map.shape[1]
    if lax.axis_size("inner") != 2 or heads % 2:
        return scan_maps(own_map, identity, step, ("outer", "inner"))
    half = heads // 2
    core = lax.axis_index("inner")
    lead = core == (0 if step > 0 else 1)
    swap = [(0, 1), (1, 0)]
    low = own_map[:, :half]
    high = own_map[:, half:]
    own_part = jnp.where(core == 0, low, high)
    other_part = jnp.where(core == 0, high, low)
    got = lax.ppermute(other_part, "inner", swap)
    first = jnp.where(lead, own_part, got)
    second = jnp.where(lead, got, own_part)
    chip_map = compose(first, second)
    start = scan_maps(chip_map, identity[:, :half], step, ("outer",))
    applied = product("hij,hjk->hik", start, first[0]) + first[1]
    for_other = jnp.where(lead, applied, start)
    keep = jnp.where(lead, start, applied)
    back = lax.ppermute(for_other, "inner", swap)
    return jnp.where(
        core == 0,
        jnp.concatenate([keep, back], axis=0),
        jnp.concatenate([back, keep], axis=0),
    )


def on_device(queries, keys, values, betas, grad_out, gain):
    length_here = queries.shape[1]
    heads = HEADS
    head_dim = HEAD_DIM
    span = STRETCH
    refl = 2 * span
    count = length_here // span
    query_raw = (
        queries[0].astype(jnp.float32).reshape(length_here, heads, head_dim).transpose(1, 0, 2)
    )
    key_raw = (
        keys[0]
        .astype(jnp.float32)
        .reshape(length_here, 2, heads, head_dim)
        .transpose(2, 0, 1, 3)
        .reshape(heads, 2 * length_here, head_dim)
    )
    value_all = (
        values[0]
        .astype(jnp.float32)
        .reshape(length_here, 2, heads, head_dim)
        .transpose(2, 0, 1, 3)
        .reshape(heads, 2 * length_here, head_dim)
    )
    rate_all = betas[0].transpose(0, 2, 1).reshape(heads, 2 * length_here)
    cotan_all = (
        grad_out[0].astype(jnp.float32).reshape(length_here, heads, head_dim).transpose(1, 0, 2)
    )
    gains = gain.reshape(heads, head_dim)
    query_n, query_inv = unit_rows(query_raw)
    key_n, key_inv = unit_rows(key_raw)
    token_ids = lax.broadcasted_iota(jnp.int32, (span, refl), 0)
    refl_ids = lax.broadcasted_iota(jnp.int32, (span, refl), 1)
    read_mask = (refl_ids <= 2 * token_ids + 1).astype(jnp.float32)
    row_ids = lax.broadcasted_iota(jnp.int32, (refl, refl), 0)
    col_ids = lax.broadcasted_iota(jnp.int32, (refl, refl), 1)
    strict = (col_ids < row_ids).astype(jnp.float32)
    eye_refl = jnp.eye(refl, dtype=jnp.float32)
    eye_head = jnp.eye(head_dim, dtype=jnp.float32)
    identity = jnp.stack(
        [
            jnp.broadcast_to(eye_head, (heads, head_dim, head_dim)),
            jnp.zeros((heads, head_dim, head_dim), jnp.float32),
        ]
    )

    def refl_rows(array, block_id):
        return array[:, block_id * refl : (block_id + 1) * refl]

    def token_rows(array, block_id):
        return array[:, block_id * span : (block_id + 1) * span]

    lower_all = []
    for block_id in range(count):
        key_blk = refl_rows(key_n, block_id)
        gram = product("hrd,hsd->hrs", key_blk, key_blk)
        lower_all.append(eye_refl + refl_rows(rate_all, block_id)[:, :, None] * gram * strict)
    inverse_all = unit_lower_inverse(jnp.concatenate(lower_all, axis=0)).reshape(
        count, heads, refl, refl
    )
    stash = []
    block_map = identity
    for block_id in range(count):
        key_blk = refl_rows(key_n, block_id)
        factor_set = stretch_factors(
            key_blk,
            refl_rows(value_all, block_id),
            refl_rows(rate_all, block_id),
            inverse_all[block_id],
            eye_head,
        )
        offset = product("hrv,hre->hve", factor_set[2], key_blk)
        block_map = compose(block_map, jnp.stack([factor_set[3], offset]))
        stash.append(factor_set)

    def factors_of(block_id):
        return stash[block_id]

    state = scan_split(block_map, identity, 1)
    records = []
    adjoint_maps = []
    gain_sum = jnp.zeros((heads, head_dim), jnp.float32)
    for block_id in range(count):
        inverse, w_mat, t_vals, transit = factors_of(block_id)
        key_blk = refl_rows(key_n, block_id)
        query_blk = token_rows(query_n, block_id)
        cotan_blk = token_rows(cotan_all, block_id)
        update = t_vals - product("hrk,hvk->hrv", w_mat, state)
        scores = product("htd,hrd->htr", query_blk, key_blk) * read_mask
        output = product("htk,hvk->htv", query_blk, state) + product("htr,hrv->htv", scores, update)
        scale_inv = lax.rsqrt(jnp.mean(output * output, axis=2, keepdims=True) + EPS_OUT)
        normed = output * scale_inv
        scaled = cotan_blk * gains[:, None, :]
        d_out = scale_inv * (scaled - normed * jnp.mean(normed * scaled, axis=2, keepdims=True))
        gain_sum = gain_sum + jnp.sum(cotan_blk * normed, axis=1)
        source = product("htv,htk->hvk", d_out, query_blk - product("htr,hrk->htk", scores, w_mat))
        records.append((state, update, scores, d_out))
        adjoint_maps.append(jnp.stack([jnp.swapaxes(transit, 1, 2), source]))
        state = state + product("hrv,hrk->hvk", update, key_blk)
    adjoint_block = identity
    for block_id in reversed(range(count)):
        adjoint_block = compose(adjoint_block, adjoint_maps[block_id])
    adjoint = scan_split(adjoint_block, identity, -1)
    adjoint, gain_sum = lax.optimization_barrier((adjoint, gain_sum))
    grad_q_parts = [None] * count
    grad_k_parts = [None] * count
    grad_v_parts = [None] * count
    for block_id in reversed(range(count)):
        inverse, w_mat, t_vals, transit = factors_of(block_id)
        start_state, update, scores, d_out = records[block_id]
        key_blk = refl_rows(key_n, block_id)
        query_blk = token_rows(query_n, block_id)
        rate_blk = refl_rows(rate_all, block_id)
        d_update = product("htr,htv->hrv", scores, d_out) + product(
            "hrk,hvk->hrv", key_blk, adjoint
        )
        solved = product("hsr,hsv->hrv", inverse, d_update)
        d_target = rate_blk[:, :, None] * solved
        d_scores = product("htv,hrv->htr", d_out, update) * read_mask
        grad_q_parts[block_id] = product("htv,hvk->htk", d_out, start_state) + product(
            "htr,hrk->htk", d_scores, key_blk
        )
        d_gram = -product("hrv,hsv->hrs", d_target, update) * strict
        grad_k_parts[block_id] = (
            product("hrv,hvk->hrk", update, adjoint)
            + product("htr,htk->hrk", d_scores, query_blk)
            - product("hrv,hvk->hrk", d_target, start_state)
            + product("hrs,hsk->hrk", d_gram + jnp.swapaxes(d_gram, 1, 2), key_blk)
        )
        grad_v_parts[block_id] = d_target
        adjoint = (
            adjoint
            + product("htv,htk->hvk", d_out, query_blk)
            - product("hrv,hrk->hvk", d_target, key_blk)
        )
    grad_qn = jnp.concatenate(grad_q_parts, axis=1)
    grad_kn = jnp.concatenate(grad_k_parts, axis=1)
    grad_val = jnp.concatenate(grad_v_parts, axis=1)
    grad_q = unit_back(query_n, query_inv, grad_qn)
    grad_k = unit_back(key_n, key_inv, grad_kn)
    grad_q = (
        grad_q.transpose(1, 0, 2).reshape(1, length_here, heads * head_dim).astype(jnp.bfloat16)
    )
    grad_k = (
        grad_k.reshape(heads, length_here, 2, head_dim)
        .transpose(1, 2, 0, 3)
        .reshape(1, length_here, 2, heads * head_dim)
        .astype(jnp.bfloat16)
    )
    grad_val = (
        grad_val.reshape(heads, length_here, 2, head_dim)
        .transpose(1, 2, 0, 3)
        .reshape(1, length_here, 2, heads * head_dim)
        .astype(jnp.bfloat16)
    )
    total = total_over(gain_sum, ("dp", "outer", "inner"))
    tokens_all = length_here * lax.axis_size("dp") * lax.axis_size("outer") * lax.axis_size("inner")
    gain_grad = total.reshape(heads * head_dim) * (1.0 / math.sqrt(tokens_all))
    return (grad_q, grad_k, grad_val, gain_grad)


def solution(mesh):
    return jax.shard_map(
        on_device,
        mesh=mesh,
        in_specs=(
            P("dp", ("outer", "inner"), None),
            P("dp", ("outer", "inner"), None, None),
            P("dp", ("outer", "inner"), None, None),
            P("dp", None, None, ("outer", "inner")),
            P("dp", ("outer", "inner"), None),
            P(),
        ),
        out_specs=(
            P("dp", ("outer", "inner"), None),
            P("dp", ("outer", "inner"), None, None),
            P("dp", ("outer", "inner"), None, None),
            P(),
        ),
        check_vma=False,
    )
```

```python
import math

import jax
import jax.numpy as jnp
from jax import lax
from jax.sharding import PartitionSpec as P

HEADS = 8
HEAD_DIM = 128
STRETCH = 64


EXACT = lax.Precision.HIGHEST
EPS_KEY = 1e-06
EPS_OUT = 1e-05


def total_over(value, axes):
    size = 1
    for axis in axes:
        size *= lax.axis_size(axis)
    if size & (size - 1):
        return lax.psum(value, axes)
    distance = size // 2
    while distance >= 1:
        route = [(i, i ^ distance) for i in range(size)]
        value = value + lax.ppermute(value, axes, route)
        distance //= 2
    return value


def product(spec, left, right):
    return jnp.einsum(spec, left, right, precision=EXACT, preferred_element_type=jnp.float32)


def unit_rows(raw):
    scale_inv = lax.rsqrt(jnp.sum(raw * raw, axis=-1, keepdims=True) + EPS_KEY)
    return (raw * scale_inv, scale_inv)


def unit_back(unit, scale_inv, grad):
    width = unit.shape[-1]
    ones = jnp.ones((width, width), jnp.float32)
    along = product("hrd,de->hre", unit * grad, ones)
    return scale_inv * (grad - unit * along)


def compose(earlier, later):
    through = product("mhij,hjk->mhik", earlier, later[0])
    return through + jnp.stack([jnp.zeros_like(later[1]), later[1]])


def unit_lower_inverse(lower_mat):
    size = lower_mat.shape[-1]
    row_ids = lax.broadcasted_iota(jnp.int32, (size, size), 0)
    col_ids = lax.broadcasted_iota(jnp.int32, (size, size), 1)
    eye = (row_ids == col_ids).astype(jnp.float32)
    first = ((row_ids // 2) == (col_ids // 2)) & (row_ids > col_ids)
    inverse = eye - lower_mat * first.astype(jnp.float32)
    width = 2
    while width < size:
        inside = (row_ids // (2 * width)) == (col_ids // (2 * width))
        below = (row_ids // width) > (col_ids // width)
        coupling = lower_mat * (inside & below).astype(jnp.float32)
        left = product("bij,bjk->bik", inverse, coupling)
        inverse = inverse - product("bij,bjk->bik", left, inverse)
        width *= 2
    return inverse


def stretch_factors(key_blk, value_blk, rate_blk, inverse, eye_head):
    head_dim = key_blk.shape[2]
    rhs = jnp.concatenate(
        [rate_blk[:, :, None] * key_blk, rate_blk[:, :, None] * value_blk], axis=2
    )
    solved = product("hrs,hsd->hrd", inverse, rhs)
    w_mat = solved[:, :, :head_dim]
    t_vals = solved[:, :, head_dim:]
    transit = eye_head - product("hrd,hre->hde", w_mat, key_blk)
    return (inverse, w_mat, t_vals, transit)


def scan_maps(own_map, identity, step, axes):
    size = 1
    here = 0
    for axis in axes:
        size *= lax.axis_size(axis)
        here = here * lax.axis_size(axis) + lax.axis_index(axis)

    def shifted(block, distance):
        route = [(i, i + step * distance) for i in range(size) if 0 <= i + step * distance < size]
        return lax.ppermute(block, axes, route)

    def reached(distance):
        source = here - step * distance
        return (source >= 0) & (source < size)

    excl = jnp.where(reached(1), shifted(own_map, 1), identity)
    incl = compose(excl, own_map)
    distance = 2
    while distance < size:
        if 2 * distance >= size:
            got = shifted(incl[1], distance)
            state = product("hij,hjk->hik", got, excl[0]) + excl[1]
            return jnp.where(reached(distance), state, excl[1])
        got = shifted(incl, distance)
        ok = reached(distance)
        excl = jnp.where(ok, compose(got, excl), excl)
        incl = jnp.where(ok, compose(got, incl), incl)
        distance *= 2
    return excl[1]


def scan_split(own_map, identity, step):
    heads = own_map.shape[1]
    if lax.axis_size("inner") != 2 or heads % 2:
        return scan_maps(own_map, identity, step, ("outer", "inner"))
    half = heads // 2
    core = lax.axis_index("inner")
    lead = core == (0 if step > 0 else 1)
    swap = [(0, 1), (1, 0)]
    low = own_map[:, :half]
    high = own_map[:, half:]
    own_part = jnp.where(core == 0, low, high)
    other_part = jnp.where(core == 0, high, low)
    got = lax.ppermute(other_part, "inner", swap)
    first = jnp.where(lead, own_part, got)
    second = jnp.where(lead, got, own_part)
    chip_map = compose(first, second)
    start = scan_maps(chip_map, identity[:, :half], step, ("outer",))
    applied = product("hij,hjk->hik", start, first[0]) + first[1]
    for_other = jnp.where(lead, applied, start)
    keep = jnp.where(lead, start, applied)
    back = lax.ppermute(for_other, "inner", swap)
    return jnp.where(
        core == 0,
        jnp.concatenate([keep, back], axis=0),
        jnp.concatenate([back, keep], axis=0),
    )


def on_device(queries, keys, values, betas, grad_out, gain):
    length_here = queries.shape[1]
    heads = HEADS
    head_dim = HEAD_DIM
    span = STRETCH
    refl = 2 * span
    count = length_here // span
    query_raw = (
        queries[0].astype(jnp.float32).reshape(length_here, heads, head_dim).transpose(1, 0, 2)
    )
    key_raw = (
        keys[0]
        .astype(jnp.float32)
        .reshape(length_here, 2, heads, head_dim)
        .transpose(2, 0, 1, 3)
        .reshape(heads, 2 * length_here, head_dim)
    )
    value_all = (
        values[0]
        .astype(jnp.float32)
        .reshape(length_here, 2, heads, head_dim)
        .transpose(2, 0, 1, 3)
        .reshape(heads, 2 * length_here, head_dim)
    )
    rate_all = betas[0].transpose(0, 2, 1).reshape(heads, 2 * length_here)
    cotan_all = (
        grad_out[0].astype(jnp.float32).reshape(length_here, heads, head_dim).transpose(1, 0, 2)
    )
    gains = gain.reshape(heads, head_dim)
    query_n, query_inv = unit_rows(query_raw)
    key_n, key_inv = unit_rows(key_raw)
    token_ids = lax.broadcasted_iota(jnp.int32, (span, refl), 0)
    refl_ids = lax.broadcasted_iota(jnp.int32, (span, refl), 1)
    read_mask = (refl_ids <= 2 * token_ids + 1).astype(jnp.float32)
    row_ids = lax.broadcasted_iota(jnp.int32, (refl, refl), 0)
    col_ids = lax.broadcasted_iota(jnp.int32, (refl, refl), 1)
    strict = (col_ids < row_ids).astype(jnp.float32)
    eye_refl = jnp.eye(refl, dtype=jnp.float32)
    eye_head = jnp.eye(head_dim, dtype=jnp.float32)
    identity = jnp.stack(
        [
            jnp.broadcast_to(eye_head, (heads, head_dim, head_dim)),
            jnp.zeros((heads, head_dim, head_dim), jnp.float32),
        ]
    )

    def refl_rows(array, block_id):
        return array[:, block_id * refl : (block_id + 1) * refl]

    def token_rows(array, block_id):
        return array[:, block_id * span : (block_id + 1) * span]

    lower_all = []
    for block_id in range(count):
        key_blk = refl_rows(key_n, block_id)
        gram = product("hrd,hsd->hrs", key_blk, key_blk)
        lower_all.append(eye_refl + refl_rows(rate_all, block_id)[:, :, None] * gram * strict)
    inverse_all = unit_lower_inverse(jnp.concatenate(lower_all, axis=0)).reshape(
        count, heads, refl, refl
    )
    stash = []
    block_map = identity
    for block_id in range(count):
        key_blk = refl_rows(key_n, block_id)
        factor_set = stretch_factors(
            key_blk,
            refl_rows(value_all, block_id),
            refl_rows(rate_all, block_id),
            inverse_all[block_id],
            eye_head,
        )
        offset = product("hrv,hre->hve", factor_set[2], key_blk)
        block_map = compose(block_map, jnp.stack([factor_set[3], offset]))
        stash.append(factor_set)

    def factors_of(block_id):
        return stash[block_id]

    state = scan_split(block_map, identity, 1)
    records = []
    adjoint_maps = []
    gain_sum = jnp.zeros((heads, head_dim), jnp.float32)
    for block_id in range(count):
        inverse, w_mat, t_vals, transit = factors_of(block_id)
        key_blk = refl_rows(key_n, block_id)
        query_blk = token_rows(query_n, block_id)
        cotan_blk = token_rows(cotan_all, block_id)
        update = t_vals - product("hrk,hvk->hrv", w_mat, state)
        scores = product("htd,hrd->htr", query_blk, key_blk) * read_mask
        output = product("htk,hvk->htv", query_blk, state) + product("htr,hrv->htv", scores, update)
        scale_inv = lax.rsqrt(jnp.mean(output * output, axis=2, keepdims=True) + EPS_OUT)
        normed = output * scale_inv
        scaled = cotan_blk * gains[:, None, :]
        d_out = scale_inv * (scaled - normed * jnp.mean(normed * scaled, axis=2, keepdims=True))
        gain_sum = gain_sum + jnp.sum(cotan_blk * normed, axis=1)
        source = product("htv,htk->hvk", d_out, query_blk - product("htr,hrk->htk", scores, w_mat))
        records.append((state, update, scores, d_out))
        adjoint_maps.append(jnp.stack([jnp.swapaxes(transit, 1, 2), source]))
        state = state + product("hrv,hrk->hvk", update, key_blk)
    adjoint_block = identity
    for block_id in reversed(range(count)):
        adjoint_block = compose(adjoint_block, adjoint_maps[block_id])
    adjoint = scan_split(adjoint_block, identity, -1)
    grad_q_parts = [None] * count
    grad_k_parts = [None] * count
    grad_v_parts = [None] * count
    for block_id in reversed(range(count)):
        inverse, w_mat, t_vals, transit = factors_of(block_id)
        start_state, update, scores, d_out = records[block_id]
        key_blk = refl_rows(key_n, block_id)
        query_blk = token_rows(query_n, block_id)
        rate_blk = refl_rows(rate_all, block_id)
        d_update = product("htr,htv->hrv", scores, d_out) + product(
            "hrk,hvk->hrv", key_blk, adjoint
        )
        solved = product("hsr,hsv->hrv", inverse, d_update)
        d_target = rate_blk[:, :, None] * solved
        d_scores = product("htv,hrv->htr", d_out, update) * read_mask
        grad_q_parts[block_id] = product("htv,hvk->htk", d_out, start_state) + product(
            "htr,hrk->htk", d_scores, key_blk
        )
        d_gram = -product("hrv,hsv->hrs", d_target, update) * strict
        grad_k_parts[block_id] = (
            product("hrv,hvk->hrk", update, adjoint)
            + product("htr,htk->hrk", d_scores, query_blk)
            - product("hrv,hvk->hrk", d_target, start_state)
            + product("hrs,hsk->hrk", d_gram + jnp.swapaxes(d_gram, 1, 2), key_blk)
        )
        grad_v_parts[block_id] = d_target
        adjoint = (
            adjoint
            + product("htv,htk->hvk", d_out, query_blk)
            - product("hrv,hrk->hvk", d_target, key_blk)
        )
    grad_qn = jnp.concatenate(grad_q_parts, axis=1)
    grad_kn = jnp.concatenate(grad_k_parts, axis=1)
    grad_val = jnp.concatenate(grad_v_parts, axis=1)
    grad_q = unit_back(query_n, query_inv, grad_qn)
    grad_k = unit_back(key_n, key_inv, grad_kn)
    grad_q = (
        grad_q.transpose(1, 0, 2).reshape(1, length_here, heads * head_dim).astype(jnp.bfloat16)
    )
    grad_k = (
        grad_k.reshape(heads, length_here, 2, head_dim)
        .transpose(1, 2, 0, 3)
        .reshape(1, length_here, 2, heads * head_dim)
        .astype(jnp.bfloat16)
    )
    grad_val = (
        grad_val.reshape(heads, length_here, 2, head_dim)
        .transpose(1, 2, 0, 3)
        .reshape(1, length_here, 2, heads * head_dim)
        .astype(jnp.bfloat16)
    )
    total = total_over(gain_sum, ("dp", "outer", "inner"))
    tokens_all = length_here * lax.axis_size("dp") * lax.axis_size("outer") * lax.axis_size("inner")
    gain_grad = total.reshape(heads * head_dim) * (1.0 / math.sqrt(tokens_all))
    return (grad_q, grad_k, grad_val, gain_grad)


def solution(mesh):
    return jax.shard_map(
        on_device,
        mesh=mesh,
        in_specs=(
            P("dp", ("outer", "inner"), None),
            P("dp", ("outer", "inner"), None, None),
            P("dp", ("outer", "inner"), None, None),
            P("dp", None, None, ("outer", "inner")),
            P("dp", ("outer", "inner"), None),
            P(),
        ),
        out_specs=(
            P("dp", ("outer", "inner"), None),
            P("dp", ("outer", "inner"), None, None),
            P("dp", ("outer", "inner"), None, None),
            P(),
        ),
        check_vma=False,
    )
```

```python
import math

import jax
import jax.numpy as jnp
from jax import lax
from jax.sharding import PartitionSpec as P

HEADS = 8
HEAD_DIM = 128
STRETCH = 64


EXACT = lax.Precision.HIGH
EPS_KEY = 1e-06
EPS_OUT = 1e-05


def total_over(value, axes):
    size = 1
    for axis in axes:
        size *= lax.axis_size(axis)
    if size & (size - 1):
        return lax.psum(value, axes)
    distance = size // 2
    while distance >= 1:
        route = [(i, i ^ distance) for i in range(size)]
        value = value + lax.ppermute(value, axes, route)
        distance //= 2
    return value


def product(spec, left, right):
    return jnp.einsum(spec, left, right, precision=EXACT, preferred_element_type=jnp.float32)


def unit_rows(raw):
    scale_inv = lax.rsqrt(jnp.sum(raw * raw, axis=-1, keepdims=True) + EPS_KEY)
    return (raw * scale_inv, scale_inv)


def unit_back(unit, scale_inv, grad):
    width = unit.shape[-1]
    ones = jnp.ones((width, width), jnp.float32)
    along = product("hrd,de->hre", unit * grad, ones)
    return scale_inv * (grad - unit * along)


def compose(earlier, later):
    through = product("mhij,hjk->mhik", earlier, later[0])
    return through + jnp.stack([jnp.zeros_like(later[1]), later[1]])


def unit_lower_inverse(lower_mat):
    size = lower_mat.shape[-1]
    row_ids = lax.broadcasted_iota(jnp.int32, (size, size), 0)
    col_ids = lax.broadcasted_iota(jnp.int32, (size, size), 1)
    eye = (row_ids == col_ids).astype(jnp.float32)
    first = ((row_ids // 2) == (col_ids // 2)) & (row_ids > col_ids)
    inverse = eye - lower_mat * first.astype(jnp.float32)
    width = 2
    while width < size:
        inside = (row_ids // (2 * width)) == (col_ids // (2 * width))
        below = (row_ids // width) > (col_ids // width)
        coupling = lower_mat * (inside & below).astype(jnp.float32)
        left = product("bij,bjk->bik", inverse, coupling)
        inverse = inverse - product("bij,bjk->bik", left, inverse)
        width *= 2
    return inverse


def stretch_factors(key_blk, value_blk, rate_blk, inverse, eye_head):
    head_dim = key_blk.shape[2]
    rhs = jnp.concatenate(
        [rate_blk[:, :, None] * key_blk, rate_blk[:, :, None] * value_blk], axis=2
    )
    solved = product("hrs,hsd->hrd", inverse, rhs)
    w_mat = solved[:, :, :head_dim]
    t_vals = solved[:, :, head_dim:]
    transit = eye_head - product("hrd,hre->hde", w_mat, key_blk)
    return (inverse, w_mat, t_vals, transit)


def scan_maps(own_map, identity, step, axes):
    size = 1
    here = 0
    for axis in axes:
        size *= lax.axis_size(axis)
        here = here * lax.axis_size(axis) + lax.axis_index(axis)

    def shifted(block, distance):
        route = [(i, i + step * distance) for i in range(size) if 0 <= i + step * distance < size]
        return lax.ppermute(block, axes, route)

    def reached(distance):
        source = here - step * distance
        return (source >= 0) & (source < size)

    excl = jnp.where(reached(1), shifted(own_map, 1), identity)
    incl = compose(excl, own_map)
    distance = 2
    while distance < size:
        if 2 * distance >= size:
            got = shifted(incl[1], distance)
            state = product("hij,hjk->hik", got, excl[0]) + excl[1]
            return jnp.where(reached(distance), state, excl[1])
        got = shifted(incl, distance)
        ok = reached(distance)
        excl = jnp.where(ok, compose(got, excl), excl)
        incl = jnp.where(ok, compose(got, incl), incl)
        distance *= 2
    return excl[1]


def scan_split(own_map, identity, step):
    heads = own_map.shape[1]
    if lax.axis_size("inner") != 2 or heads % 2:
        return scan_maps(own_map, identity, step, ("outer", "inner"))
    half = heads // 2
    core = lax.axis_index("inner")
    lead = core == (0 if step > 0 else 1)
    swap = [(0, 1), (1, 0)]
    low = own_map[:, :half]
    high = own_map[:, half:]
    own_part = jnp.where(core == 0, low, high)
    other_part = jnp.where(core == 0, high, low)
    got = lax.ppermute(other_part, "inner", swap)
    first = jnp.where(lead, own_part, got)
    second = jnp.where(lead, got, own_part)
    chip_map = compose(first, second)
    start = scan_maps(chip_map, identity[:, :half], step, ("outer",))
    applied = product("hij,hjk->hik", start, first[0]) + first[1]
    for_other = jnp.where(lead, applied, start)
    keep = jnp.where(lead, start, applied)
    back = lax.ppermute(for_other, "inner", swap)
    return jnp.where(
        core == 0,
        jnp.concatenate([keep, back], axis=0),
        jnp.concatenate([back, keep], axis=0),
    )


def on_device(queries, keys, values, betas, grad_out, gain):
    length_here = queries.shape[1]
    heads = HEADS
    head_dim = HEAD_DIM
    span = STRETCH
    refl = 2 * span
    count = length_here // span
    query_raw = (
        queries[0].astype(jnp.float32).reshape(length_here, heads, head_dim).transpose(1, 0, 2)
    )
    key_raw = (
        keys[0]
        .astype(jnp.float32)
        .reshape(length_here, 2, heads, head_dim)
        .transpose(2, 0, 1, 3)
        .reshape(heads, 2 * length_here, head_dim)
    )
    value_all = (
        values[0]
        .astype(jnp.float32)
        .reshape(length_here, 2, heads, head_dim)
        .transpose(2, 0, 1, 3)
        .reshape(heads, 2 * length_here, head_dim)
    )
    rate_all = betas[0].transpose(0, 2, 1).reshape(heads, 2 * length_here)
    cotan_all = (
        grad_out[0].astype(jnp.float32).reshape(length_here, heads, head_dim).transpose(1, 0, 2)
    )
    gains = gain.reshape(heads, head_dim)
    query_n, query_inv = unit_rows(query_raw)
    key_n, key_inv = unit_rows(key_raw)
    token_ids = lax.broadcasted_iota(jnp.int32, (span, refl), 0)
    refl_ids = lax.broadcasted_iota(jnp.int32, (span, refl), 1)
    read_mask = (refl_ids <= 2 * token_ids + 1).astype(jnp.float32)
    row_ids = lax.broadcasted_iota(jnp.int32, (refl, refl), 0)
    col_ids = lax.broadcasted_iota(jnp.int32, (refl, refl), 1)
    strict = (col_ids < row_ids).astype(jnp.float32)
    eye_refl = jnp.eye(refl, dtype=jnp.float32)
    eye_head = jnp.eye(head_dim, dtype=jnp.float32)
    identity = jnp.stack(
        [
            jnp.broadcast_to(eye_head, (heads, head_dim, head_dim)),
            jnp.zeros((heads, head_dim, head_dim), jnp.float32),
        ]
    )

    def refl_rows(array, block_id):
        return array[:, block_id * refl : (block_id + 1) * refl]

    def token_rows(array, block_id):
        return array[:, block_id * span : (block_id + 1) * span]

    lower_all = []
    for block_id in range(count):
        key_blk = refl_rows(key_n, block_id)
        gram = product("hrd,hsd->hrs", key_blk, key_blk)
        lower_all.append(eye_refl + refl_rows(rate_all, block_id)[:, :, None] * gram * strict)
    inverse_all = unit_lower_inverse(jnp.concatenate(lower_all, axis=0)).reshape(
        count, heads, refl, refl
    )
    stash = []
    block_map = identity
    for block_id in range(count):
        key_blk = refl_rows(key_n, block_id)
        factor_set = stretch_factors(
            key_blk,
            refl_rows(value_all, block_id),
            refl_rows(rate_all, block_id),
            inverse_all[block_id],
            eye_head,
        )
        offset = product("hrv,hre->hve", factor_set[2], key_blk)
        block_map = compose(block_map, jnp.stack([factor_set[3], offset]))
        stash.append(factor_set)

    def factors_of(block_id):
        return stash[block_id]

    state = scan_split(block_map, identity, 1)
    records = []
    adjoint_maps = []
    gain_sum = jnp.zeros((heads, head_dim), jnp.float32)
    for block_id in range(count):
        inverse, w_mat, t_vals, transit = factors_of(block_id)
        key_blk = refl_rows(key_n, block_id)
        query_blk = token_rows(query_n, block_id)
        cotan_blk = token_rows(cotan_all, block_id)
        update = t_vals - product("hrk,hvk->hrv", w_mat, state)
        scores = product("htd,hrd->htr", query_blk, key_blk) * read_mask
        output = product("htk,hvk->htv", query_blk, state) + product("htr,hrv->htv", scores, update)
        scale_inv = lax.rsqrt(jnp.mean(output * output, axis=2, keepdims=True) + EPS_OUT)
        normed = output * scale_inv
        scaled = cotan_blk * gains[:, None, :]
        d_out = scale_inv * (scaled - normed * jnp.mean(normed * scaled, axis=2, keepdims=True))
        gain_sum = gain_sum + jnp.sum(cotan_blk * normed, axis=1)
        source = product("htv,htk->hvk", d_out, query_blk - product("htr,hrk->htk", scores, w_mat))
        records.append((state, update, scores, d_out))
        adjoint_maps.append(jnp.stack([jnp.swapaxes(transit, 1, 2), source]))
        state = state + product("hrv,hrk->hvk", update, key_blk)
    adjoint_block = identity
    for block_id in reversed(range(count)):
        adjoint_block = compose(adjoint_block, adjoint_maps[block_id])
    adjoint = scan_split(adjoint_block, identity, -1)
    grad_q_parts = [None] * count
    grad_k_parts = [None] * count
    grad_v_parts = [None] * count
    for block_id in reversed(range(count)):
        inverse, w_mat, t_vals, transit = factors_of(block_id)
        start_state, update, scores, d_out = records[block_id]
        key_blk = refl_rows(key_n, block_id)
        query_blk = token_rows(query_n, block_id)
        rate_blk = refl_rows(rate_all, block_id)
        d_update = product("htr,htv->hrv", scores, d_out) + product(
            "hrk,hvk->hrv", key_blk, adjoint
        )
        solved = product("hsr,hsv->hrv", inverse, d_update)
        d_target = rate_blk[:, :, None] * solved
        d_scores = product("htv,hrv->htr", d_out, update) * read_mask
        grad_q_parts[block_id] = product("htv,hvk->htk", d_out, start_state) + product(
            "htr,hrk->htk", d_scores, key_blk
        )
        d_gram = -product("hrv,hsv->hrs", d_target, update) * strict
        grad_k_parts[block_id] = (
            product("hrv,hvk->hrk", update, adjoint)
            + product("htr,htk->hrk", d_scores, query_blk)
            - product("hrv,hvk->hrk", d_target, start_state)
            + product("hrs,hsk->hrk", d_gram + jnp.swapaxes(d_gram, 1, 2), key_blk)
        )
        grad_v_parts[block_id] = d_target
        adjoint = (
            adjoint
            + product("htv,htk->hvk", d_out, query_blk)
            - product("hrv,hrk->hvk", d_target, key_blk)
        )
    grad_qn = jnp.concatenate(grad_q_parts, axis=1)
    grad_kn = jnp.concatenate(grad_k_parts, axis=1)
    grad_val = jnp.concatenate(grad_v_parts, axis=1)
    grad_q = unit_back(query_n, query_inv, grad_qn)
    grad_k = unit_back(key_n, key_inv, grad_kn)
    grad_q = (
        grad_q.transpose(1, 0, 2).reshape(1, length_here, heads * head_dim).astype(jnp.bfloat16)
    )
    grad_k = (
        grad_k.reshape(heads, length_here, 2, head_dim)
        .transpose(1, 2, 0, 3)
        .reshape(1, length_here, 2, heads * head_dim)
        .astype(jnp.bfloat16)
    )
    grad_val = (
        grad_val.reshape(heads, length_here, 2, head_dim)
        .transpose(1, 2, 0, 3)
        .reshape(1, length_here, 2, heads * head_dim)
        .astype(jnp.bfloat16)
    )
    total = total_over(gain_sum, ("dp", "outer", "inner"))
    tokens_all = length_here * lax.axis_size("dp") * lax.axis_size("outer") * lax.axis_size("inner")
    gain_grad = total.reshape(heads * head_dim) * (1.0 / math.sqrt(tokens_all))
    return (grad_q, grad_k, grad_val, gain_grad)


def solution(mesh):
    return jax.shard_map(
        on_device,
        mesh=mesh,
        in_specs=(
            P("dp", ("outer", "inner"), None),
            P("dp", ("outer", "inner"), None, None),
            P("dp", ("outer", "inner"), None, None),
            P("dp", None, None, ("outer", "inner")),
            P("dp", ("outer", "inner"), None),
            P(),
        ),
        out_specs=(
            P("dp", ("outer", "inner"), None),
            P("dp", ("outer", "inner"), None, None),
            P("dp", ("outer", "inner"), None, None),
            P(),
        ),
        check_vma=False,
    )
```

```python
import math

import jax
import jax.numpy as jnp
from jax import lax
from jax.sharding import PartitionSpec as P

HEADS = 8
HEAD_DIM = 128
STRETCH = 64


EXACT = lax.Precision.HIGH
EPS_KEY = 1e-06
EPS_OUT = 1e-05


def total_over(value, axes):
    size = 1
    for axis in axes:
        size *= lax.axis_size(axis)
    if size & (size - 1):
        return lax.psum(value, axes)
    distance = size // 2
    while distance >= 1:
        route = [(i, i ^ distance) for i in range(size)]
        value = value + lax.ppermute(value, axes, route)
        distance //= 2
    return value


def product(spec, left, right):
    return jnp.einsum(spec, left, right, precision=EXACT, preferred_element_type=jnp.float32)


def unit_rows(raw):
    scale_inv = lax.rsqrt(jnp.sum(raw * raw, axis=-1, keepdims=True) + EPS_KEY)
    return (raw * scale_inv, scale_inv)


def unit_back(unit, scale_inv, grad):
    width = unit.shape[-1]
    ones = jnp.ones((width, width), jnp.float32)
    along = product("hrd,de->hre", unit * grad, ones)
    return scale_inv * (grad - unit * along)


def compose(earlier, later):
    through = product("mhij,hjk->mhik", earlier, later[0])
    return through + jnp.stack([jnp.zeros_like(later[1]), later[1]])


def unit_lower_inverse(lower_mat):
    size = lower_mat.shape[-1]
    row_ids = lax.broadcasted_iota(jnp.int32, (size, size), 0)
    col_ids = lax.broadcasted_iota(jnp.int32, (size, size), 1)
    eye = (row_ids == col_ids).astype(jnp.float32)
    first = ((row_ids // 2) == (col_ids // 2)) & (row_ids > col_ids)
    inverse = eye - lower_mat * first.astype(jnp.float32)
    width = 2
    while width < size:
        inside = (row_ids // (2 * width)) == (col_ids // (2 * width))
        below = (row_ids // width) > (col_ids // width)
        coupling = lower_mat * (inside & below).astype(jnp.float32)
        left = product("bij,bjk->bik", inverse, coupling)
        inverse = inverse - product("bij,bjk->bik", left, inverse)
        width *= 2
    return inverse


def stretch_factors(key_blk, value_blk, rate_blk, inverse, eye_head):
    head_dim = key_blk.shape[2]
    rhs = jnp.concatenate(
        [rate_blk[:, :, None] * key_blk, rate_blk[:, :, None] * value_blk], axis=2
    )
    solved = product("hrs,hsd->hrd", inverse, rhs)
    w_mat = solved[:, :, :head_dim]
    t_vals = solved[:, :, head_dim:]
    transit = eye_head - product("hrd,hre->hde", w_mat, key_blk)
    return (inverse, w_mat, t_vals, transit)


def scan_maps(own_map, identity, step, axes):
    size = 1
    here = 0
    for axis in axes:
        size *= lax.axis_size(axis)
        here = here * lax.axis_size(axis) + lax.axis_index(axis)

    def shifted(block, distance):
        route = [(i, i + step * distance) for i in range(size) if 0 <= i + step * distance < size]
        return lax.ppermute(block, axes, route)

    def reached(distance):
        source = here - step * distance
        return (source >= 0) & (source < size)

    excl = jnp.where(reached(1), shifted(own_map, 1), identity)
    incl = compose(excl, own_map)
    distance = 2
    while distance < size:
        if 2 * distance >= size:
            got = shifted(incl[1], distance)
            state = product("hij,hjk->hik", got, excl[0]) + excl[1]
            return jnp.where(reached(distance), state, excl[1])
        got = shifted(incl, distance)
        ok = reached(distance)
        excl = jnp.where(ok, compose(got, excl), excl)
        incl = jnp.where(ok, compose(got, incl), incl)
        distance *= 2
    return excl[1]


def scan_split(own_map, identity, step, side):
    heads = own_map.shape[1]
    if lax.axis_size("inner") != 2 or heads % 2:
        own_map, side = lax.optimization_barrier((own_map, side))
        return scan_maps(own_map, identity, step, ("outer", "inner")), side
    half = heads // 2
    core = lax.axis_index("inner")
    lead = core == (0 if step > 0 else 1)
    swap = [(0, 1), (1, 0)]
    low = own_map[:, :half]
    high = own_map[:, half:]
    own_part = jnp.where(core == 0, low, high)
    other_part = jnp.where(core == 0, high, low)
    got = lax.ppermute(other_part, "inner", swap)
    first = jnp.where(lead, own_part, got)
    second = jnp.where(lead, got, own_part)
    chip_map = compose(first, second)
    chip_map, side = lax.optimization_barrier((chip_map, side))
    start = scan_maps(chip_map, identity[:, :half], step, ("outer",))
    applied = product("hij,hjk->hik", start, first[0]) + first[1]
    for_other = jnp.where(lead, applied, start)
    keep = jnp.where(lead, start, applied)
    back = lax.ppermute(for_other, "inner", swap)
    whole = jnp.where(
        core == 0,
        jnp.concatenate([keep, back], axis=0),
        jnp.concatenate([back, keep], axis=0),
    )
    return whole, side


def on_device(queries, keys, values, betas, grad_out, gain):
    length_here = queries.shape[1]
    heads = HEADS
    head_dim = HEAD_DIM
    span = STRETCH
    refl = 2 * span
    count = length_here // span
    query_raw = (
        queries[0].astype(jnp.float32).reshape(length_here, heads, head_dim).transpose(1, 0, 2)
    )
    key_raw = (
        keys[0]
        .astype(jnp.float32)
        .reshape(length_here, 2, heads, head_dim)
        .transpose(2, 0, 1, 3)
        .reshape(heads, 2 * length_here, head_dim)
    )
    value_all = (
        values[0]
        .astype(jnp.float32)
        .reshape(length_here, 2, heads, head_dim)
        .transpose(2, 0, 1, 3)
        .reshape(heads, 2 * length_here, head_dim)
    )
    rate_all = betas[0].transpose(0, 2, 1).reshape(heads, 2 * length_here)
    cotan_all = (
        grad_out[0].astype(jnp.float32).reshape(length_here, heads, head_dim).transpose(1, 0, 2)
    )
    gains = gain.reshape(heads, head_dim)
    query_n, query_inv = unit_rows(query_raw)
    key_n, key_inv = unit_rows(key_raw)
    token_ids = lax.broadcasted_iota(jnp.int32, (span, refl), 0)
    refl_ids = lax.broadcasted_iota(jnp.int32, (span, refl), 1)
    read_mask = (refl_ids <= 2 * token_ids + 1).astype(jnp.float32)
    row_ids = lax.broadcasted_iota(jnp.int32, (refl, refl), 0)
    col_ids = lax.broadcasted_iota(jnp.int32, (refl, refl), 1)
    strict = (col_ids < row_ids).astype(jnp.float32)
    eye_refl = jnp.eye(refl, dtype=jnp.float32)
    eye_head = jnp.eye(head_dim, dtype=jnp.float32)
    identity = jnp.stack(
        [
            jnp.broadcast_to(eye_head, (heads, head_dim, head_dim)),
            jnp.zeros((heads, head_dim, head_dim), jnp.float32),
        ]
    )

    def refl_rows(array, block_id):
        return array[:, block_id * refl : (block_id + 1) * refl]

    def token_rows(array, block_id):
        return array[:, block_id * span : (block_id + 1) * span]

    lower_all = []
    for block_id in range(count):
        key_blk = refl_rows(key_n, block_id)
        gram = product("hrd,hsd->hrs", key_blk, key_blk)
        lower_all.append(eye_refl + refl_rows(rate_all, block_id)[:, :, None] * gram * strict)
    inverse_all = unit_lower_inverse(jnp.concatenate(lower_all, axis=0)).reshape(
        count, heads, refl, refl
    )
    stash = []
    block_map = identity
    for block_id in range(count):
        key_blk = refl_rows(key_n, block_id)
        factor_set = stretch_factors(
            key_blk,
            refl_rows(value_all, block_id),
            refl_rows(rate_all, block_id),
            inverse_all[block_id],
            eye_head,
        )
        offset = product("hrv,hre->hve", factor_set[2], key_blk)
        block_map = compose(block_map, jnp.stack([factor_set[3], offset]))
        stash.append(factor_set)

    def factors_of(block_id):
        return stash[block_id]

    state, (query_t, key_t, stash_t) = scan_split(
        block_map, identity, 1, (query_n, key_n, [factor_set[1:3] for factor_set in stash])
    )
    early = []
    for block_id in range(count):
        w_mat, t_vals = stash_t[block_id]
        key_blk = refl_rows(key_t, block_id)
        query_blk = token_rows(query_t, block_id)
        scores = product("htd,hrd->htr", query_blk, key_blk) * read_mask
        query_eff = query_blk - product("htr,hrk->htk", scores, w_mat)
        inside = product("htr,hrv->htv", scores, t_vals)
        early.append((scores, query_eff, inside))
    records = []
    adjoint_maps = []
    grad_q_parts = [None] * count
    gain_sum = jnp.zeros((heads, head_dim), jnp.float32)
    for block_id in range(count):
        inverse, w_mat, t_vals, transit = factors_of(block_id)
        scores, query_eff, inside = early[block_id]
        key_blk = refl_rows(key_n, block_id)
        query_blk = token_rows(query_n, block_id)
        cotan_blk = token_rows(cotan_all, block_id)
        update = t_vals - product("hrk,hvk->hrv", w_mat, state)
        output = product("htk,hvk->htv", query_eff, state) + inside
        scale_inv = lax.rsqrt(jnp.mean(output * output, axis=2, keepdims=True) + EPS_OUT)
        normed = output * scale_inv
        scaled = cotan_blk * gains[:, None, :]
        d_out = scale_inv * (scaled - normed * jnp.mean(normed * scaled, axis=2, keepdims=True))
        gain_sum = gain_sum + jnp.sum(cotan_blk * normed, axis=1)
        source = product("htv,htk->hvk", d_out, query_eff)
        records.append((state, update, scores, d_out))
        adjoint_maps.append(jnp.stack([jnp.swapaxes(transit, 1, 2), source]))
        state = state + product("hrv,hrk->hvk", update, key_blk)
    adjoint_block = identity
    for block_id in reversed(range(count)):
        adjoint_block = compose(adjoint_block, adjoint_maps[block_id])
    adjoint, (records, query_t, key_t) = scan_split(
        adjoint_block, identity, -1, (records, query_n, key_n)
    )
    pieces = []
    for block_id in range(count):
        state, update, scores, d_out = records[block_id]
        key_blk = refl_rows(key_t, block_id)
        query_blk = token_rows(query_t, block_id)
        d_scores = product("htv,hrv->htr", d_out, update) * read_mask
        grad_q_parts[block_id] = product("htv,hvk->htk", d_out, state) + product(
            "htr,hrk->htk", d_scores, key_blk
        )
        d_update_pre = product("htr,htv->hrv", scores, d_out)
        grad_k_pre = product("htr,htk->hrk", d_scores, query_blk)
        adjoint_pre = product("htv,htk->hvk", d_out, query_blk)
        pieces.append((state, update, d_update_pre, grad_k_pre, adjoint_pre))
    grad_k_parts = [None] * count
    grad_v_parts = [None] * count
    for block_id in reversed(range(count)):
        inverse, w_mat, t_vals, transit = factors_of(block_id)
        start_state, update, d_update_pre, grad_k_pre, adjoint_pre = pieces[block_id]
        key_blk = refl_rows(key_n, block_id)
        rate_blk = refl_rows(rate_all, block_id)
        d_update = d_update_pre + product("hrk,hvk->hrv", key_blk, adjoint)
        solved = product("hsr,hsv->hrv", inverse, d_update)
        d_target = rate_blk[:, :, None] * solved
        d_gram = -product("hrv,hsv->hrs", d_target, update) * strict
        grad_k_parts[block_id] = (
            product("hrv,hvk->hrk", update, adjoint)
            + grad_k_pre
            - product("hrv,hvk->hrk", d_target, start_state)
            + product("hrs,hsk->hrk", d_gram + jnp.swapaxes(d_gram, 1, 2), key_blk)
        )
        grad_v_parts[block_id] = d_target
        adjoint = adjoint + adjoint_pre - product("hrv,hrk->hvk", d_target, key_blk)
    grad_qn = jnp.concatenate(grad_q_parts, axis=1)
    grad_kn = jnp.concatenate(grad_k_parts, axis=1)
    grad_val = jnp.concatenate(grad_v_parts, axis=1)
    grad_q = unit_back(query_n, query_inv, grad_qn)
    grad_k = unit_back(key_n, key_inv, grad_kn)
    grad_q = (
        grad_q.transpose(1, 0, 2).reshape(1, length_here, heads * head_dim).astype(jnp.bfloat16)
    )
    grad_k = (
        grad_k.reshape(heads, length_here, 2, head_dim)
        .transpose(1, 2, 0, 3)
        .reshape(1, length_here, 2, heads * head_dim)
        .astype(jnp.bfloat16)
    )
    grad_val = (
        grad_val.reshape(heads, length_here, 2, head_dim)
        .transpose(1, 2, 0, 3)
        .reshape(1, length_here, 2, heads * head_dim)
        .astype(jnp.bfloat16)
    )
    total = total_over(gain_sum, ("dp", "outer", "inner"))
    tokens_all = length_here * lax.axis_size("dp") * lax.axis_size("outer") * lax.axis_size("inner")
    gain_grad = total.reshape(heads * head_dim) * (1.0 / math.sqrt(tokens_all))
    return (grad_q, grad_k, grad_val, gain_grad)


def solution(mesh):
    return jax.shard_map(
        on_device,
        mesh=mesh,
        in_specs=(
            P("dp", ("outer", "inner"), None),
            P("dp", ("outer", "inner"), None, None),
            P("dp", ("outer", "inner"), None, None),
            P("dp", None, None, ("outer", "inner")),
            P("dp", ("outer", "inner"), None),
            P(),
        ),
        out_specs=(
            P("dp", ("outer", "inner"), None),
            P("dp", ("outer", "inner"), None, None),
            P("dp", ("outer", "inner"), None, None),
            P(),
        ),
        check_vma=False,
    )
```

```python
import math

import jax
import jax.numpy as jnp
from jax import lax
from jax.sharding import PartitionSpec as P

HEADS = 8
HEAD_DIM = 128
STRETCH = 64


EXACT = lax.Precision.HIGH
EPS_KEY = 1e-06
EPS_OUT = 1e-05


def total_over(value, axes):
    size = 1
    for axis in axes:
        size *= lax.axis_size(axis)
    if size & (size - 1):
        return lax.psum(value, axes)
    distance = size // 2
    while distance >= 1:
        route = [(i, i ^ distance) for i in range(size)]
        value = value + lax.ppermute(value, axes, route)
        distance //= 2
    return value


def product(spec, left, right):
    return jnp.einsum(spec, left, right, precision=EXACT, preferred_element_type=jnp.float32)


def unit_rows(raw):
    scale_inv = lax.rsqrt(jnp.sum(raw * raw, axis=-1, keepdims=True) + EPS_KEY)
    return (raw * scale_inv, scale_inv)


def unit_back(unit, scale_inv, grad):
    width = unit.shape[-1]
    ones = jnp.ones((width, width), jnp.float32)
    along = product("hrd,de->hre", unit * grad, ones)
    return scale_inv * (grad - unit * along)


def compose(earlier, later):
    through = product("mhij,hjk->mhik", earlier, later[0])
    return through + jnp.stack([jnp.zeros_like(later[1]), later[1]])


def unit_lower_inverse(lower_mat):
    size = lower_mat.shape[-1]
    row_ids = lax.broadcasted_iota(jnp.int32, (size, size), 0)
    col_ids = lax.broadcasted_iota(jnp.int32, (size, size), 1)
    eye = (row_ids == col_ids).astype(jnp.float32)
    first = ((row_ids // 2) == (col_ids // 2)) & (row_ids > col_ids)
    inverse = eye - lower_mat * first.astype(jnp.float32)
    width = 2
    while width < size:
        inside = (row_ids // (2 * width)) == (col_ids // (2 * width))
        below = (row_ids // width) > (col_ids // width)
        coupling = lower_mat * (inside & below).astype(jnp.float32)
        left = product("bij,bjk->bik", inverse, coupling)
        inverse = inverse - product("bij,bjk->bik", left, inverse)
        width *= 2
    return inverse


def stretch_factors(key_blk, value_blk, rate_blk, inverse, eye_head):
    head_dim = key_blk.shape[2]
    rhs = jnp.concatenate(
        [rate_blk[:, :, None] * key_blk, rate_blk[:, :, None] * value_blk], axis=2
    )
    solved = product("hrs,hsd->hrd", inverse, rhs)
    w_mat = solved[:, :, :head_dim]
    t_vals = solved[:, :, head_dim:]
    transit = eye_head - product("hrd,hre->hde", w_mat, key_blk)
    return (inverse, w_mat, t_vals, transit)


def scan_maps(own_map, identity, step, axes):
    size = 1
    here = 0
    for axis in axes:
        size *= lax.axis_size(axis)
        here = here * lax.axis_size(axis) + lax.axis_index(axis)

    def shifted(block, distance):
        route = [(i, i + step * distance) for i in range(size) if 0 <= i + step * distance < size]
        return lax.ppermute(block, axes, route)

    def reached(distance):
        source = here - step * distance
        return (source >= 0) & (source < size)

    excl = jnp.where(reached(1), shifted(own_map, 1), identity)
    incl = compose(excl, own_map)
    distance = 2
    while distance < size:
        if 2 * distance >= size:
            got = shifted(incl[1], distance)
            state = product("hij,hjk->hik", got, excl[0]) + excl[1]
            return jnp.where(reached(distance), state, excl[1])
        got = shifted(incl, distance)
        ok = reached(distance)
        excl = jnp.where(ok, compose(got, excl), excl)
        incl = jnp.where(ok, compose(got, incl), incl)
        distance *= 2
    return excl[1]


def scan_split(own_map, identity, step, side):
    heads = own_map.shape[1]
    if lax.axis_size("inner") != 2 or heads % 2:
        own_map, side = lax.optimization_barrier((own_map, side))
        return scan_maps(own_map, identity, step, ("outer", "inner")), side
    half = heads // 2
    core = lax.axis_index("inner")
    lead = core == (0 if step > 0 else 1)
    swap = [(0, 1), (1, 0)]
    low = own_map[:, :half]
    high = own_map[:, half:]
    own_part = jnp.where(core == 0, low, high)
    other_part = jnp.where(core == 0, high, low)
    got = lax.ppermute(other_part, "inner", swap)
    first = jnp.where(lead, own_part, got)
    second = jnp.where(lead, got, own_part)
    chip_map = compose(first, second)
    chip_map, side = lax.optimization_barrier((chip_map, side))
    start = scan_maps(chip_map, identity[:, :half], step, ("outer",))
    applied = product("hij,hjk->hik", start, first[0]) + first[1]
    for_other = jnp.where(lead, applied, start)
    keep = jnp.where(lead, start, applied)
    back = lax.ppermute(for_other, "inner", swap)
    whole = jnp.where(
        core == 0,
        jnp.concatenate([keep, back], axis=0),
        jnp.concatenate([back, keep], axis=0),
    )
    return whole, side


def on_device(queries, keys, values, betas, grad_out, gain):
    length_here = queries.shape[1]
    heads = HEADS
    head_dim = HEAD_DIM
    span = STRETCH
    refl = 2 * span
    count = length_here // span
    query_raw = (
        queries[0].astype(jnp.float32).reshape(length_here, heads, head_dim).transpose(1, 0, 2)
    )
    key_raw = (
        keys[0]
        .astype(jnp.float32)
        .reshape(length_here, 2, heads, head_dim)
        .transpose(2, 0, 1, 3)
        .reshape(heads, 2 * length_here, head_dim)
    )
    value_all = (
        values[0]
        .astype(jnp.float32)
        .reshape(length_here, 2, heads, head_dim)
        .transpose(2, 0, 1, 3)
        .reshape(heads, 2 * length_here, head_dim)
    )
    rate_all = betas[0].transpose(0, 2, 1).reshape(heads, 2 * length_here)
    cotan_all = (
        grad_out[0].astype(jnp.float32).reshape(length_here, heads, head_dim).transpose(1, 0, 2)
    )
    gains = gain.reshape(heads, head_dim)
    query_n, query_inv = unit_rows(query_raw)
    key_n, key_inv = unit_rows(key_raw)
    token_ids = lax.broadcasted_iota(jnp.int32, (span, refl), 0)
    refl_ids = lax.broadcasted_iota(jnp.int32, (span, refl), 1)
    read_mask = (refl_ids <= 2 * token_ids + 1).astype(jnp.float32)
    row_ids = lax.broadcasted_iota(jnp.int32, (refl, refl), 0)
    col_ids = lax.broadcasted_iota(jnp.int32, (refl, refl), 1)
    strict = (col_ids < row_ids).astype(jnp.float32)
    eye_refl = jnp.eye(refl, dtype=jnp.float32)
    eye_head = jnp.eye(head_dim, dtype=jnp.float32)
    identity = jnp.stack(
        [
            jnp.broadcast_to(eye_head, (heads, head_dim, head_dim)),
            jnp.zeros((heads, head_dim, head_dim), jnp.float32),
        ]
    )

    def refl_rows(array, block_id):
        return array[:, block_id * refl : (block_id + 1) * refl]

    def token_rows(array, block_id):
        return array[:, block_id * span : (block_id + 1) * span]

    lower_all = []
    for block_id in range(count):
        key_blk = refl_rows(key_n, block_id)
        gram = product("hrd,hsd->hrs", key_blk, key_blk)
        lower_all.append(eye_refl + refl_rows(rate_all, block_id)[:, :, None] * gram * strict)
    inverse_all = unit_lower_inverse(jnp.concatenate(lower_all, axis=0)).reshape(
        count, heads, refl, refl
    )
    stash = []
    block_map = identity
    for block_id in range(count):
        key_blk = refl_rows(key_n, block_id)
        factor_set = stretch_factors(
            key_blk,
            refl_rows(value_all, block_id),
            refl_rows(rate_all, block_id),
            inverse_all[block_id],
            eye_head,
        )
        offset = product("hrv,hre->hve", factor_set[2], key_blk)
        block_map = compose(block_map, jnp.stack([factor_set[3], offset]))
        stash.append(factor_set)

    def factors_of(block_id):
        return stash[block_id]

    state, (query_t, key_t, stash_t) = scan_split(
        block_map, identity, 1, (query_n, key_n, [factor_set[1:3] for factor_set in stash])
    )
    early = []
    for block_id in range(count):
        w_mat, t_vals = stash_t[block_id]
        key_blk = refl_rows(key_t, block_id)
        query_blk = token_rows(query_t, block_id)
        scores = product("htd,hrd->htr", query_blk, key_blk) * read_mask
        query_eff = query_blk - product("htr,hrk->htk", scores, w_mat)
        inside = product("htr,hrv->htv", scores, t_vals)
        early.append((scores, query_eff, inside))
    records = []
    adjoint_maps = []
    grad_q_parts = [None] * count
    gain_sum = jnp.zeros((heads, head_dim), jnp.float32)
    for block_id in range(count):
        inverse, w_mat, t_vals, transit = factors_of(block_id)
        scores, query_eff, inside = early[block_id]
        key_blk = refl_rows(key_n, block_id)
        query_blk = token_rows(query_n, block_id)
        cotan_blk = token_rows(cotan_all, block_id)
        update = t_vals - product("hrk,hvk->hrv", w_mat, state)
        output = product("htk,hvk->htv", query_eff, state) + inside
        scale_inv = lax.rsqrt(jnp.mean(output * output, axis=2, keepdims=True) + EPS_OUT)
        normed = output * scale_inv
        scaled = cotan_blk * gains[:, None, :]
        d_out = scale_inv * (scaled - normed * jnp.mean(normed * scaled, axis=2, keepdims=True))
        gain_sum = gain_sum + jnp.sum(cotan_blk * normed, axis=1)
        source = product("htv,htk->hvk", d_out, query_eff)
        records.append((state, update, scores, d_out))
        adjoint_maps.append(jnp.stack([jnp.swapaxes(transit, 1, 2), source]))
        state = state + product("hrv,hrk->hvk", update, key_blk)
    adjoint_block = identity
    for block_id in reversed(range(count)):
        adjoint_block = compose(adjoint_block, adjoint_maps[block_id])
    adjoint, (records, query_t, key_t, gain_sum) = scan_split(
        adjoint_block, identity, -1, (records, query_n, key_n, gain_sum)
    )
    pieces = []
    for block_id in range(count):
        state, update, scores, d_out = records[block_id]
        key_blk = refl_rows(key_t, block_id)
        query_blk = token_rows(query_t, block_id)
        d_scores = product("htv,hrv->htr", d_out, update) * read_mask
        grad_q_parts[block_id] = product("htv,hvk->htk", d_out, state) + product(
            "htr,hrk->htk", d_scores, key_blk
        )
        d_update_pre = product("htr,htv->hrv", scores, d_out)
        grad_k_pre = product("htr,htk->hrk", d_scores, query_blk)
        adjoint_pre = product("htv,htk->hvk", d_out, query_blk)
        pieces.append((state, update, d_update_pre, grad_k_pre, adjoint_pre))
    grad_k_parts = [None] * count
    grad_v_parts = [None] * count
    for block_id in reversed(range(count)):
        inverse, w_mat, t_vals, transit = factors_of(block_id)
        start_state, update, d_update_pre, grad_k_pre, adjoint_pre = pieces[block_id]
        key_blk = refl_rows(key_n, block_id)
        rate_blk = refl_rows(rate_all, block_id)
        d_update = d_update_pre + product("hrk,hvk->hrv", key_blk, adjoint)
        solved = product("hsr,hsv->hrv", inverse, d_update)
        d_target = rate_blk[:, :, None] * solved
        d_gram = -product("hrv,hsv->hrs", d_target, update) * strict
        grad_k_parts[block_id] = (
            product("hrv,hvk->hrk", update, adjoint)
            + grad_k_pre
            - product("hrv,hvk->hrk", d_target, start_state)
            + product("hrs,hsk->hrk", d_gram + jnp.swapaxes(d_gram, 1, 2), key_blk)
        )
        grad_v_parts[block_id] = d_target
        adjoint = adjoint + adjoint_pre - product("hrv,hrk->hvk", d_target, key_blk)
    grad_qn = jnp.concatenate(grad_q_parts, axis=1)
    grad_kn = jnp.concatenate(grad_k_parts, axis=1)
    grad_val = jnp.concatenate(grad_v_parts, axis=1)
    grad_q = unit_back(query_n, query_inv, grad_qn)
    grad_k = unit_back(key_n, key_inv, grad_kn)
    grad_q = (
        grad_q.transpose(1, 0, 2).reshape(1, length_here, heads * head_dim).astype(jnp.bfloat16)
    )
    grad_k = (
        grad_k.reshape(heads, length_here, 2, head_dim)
        .transpose(1, 2, 0, 3)
        .reshape(1, length_here, 2, heads * head_dim)
        .astype(jnp.bfloat16)
    )
    grad_val = (
        grad_val.reshape(heads, length_here, 2, head_dim)
        .transpose(1, 2, 0, 3)
        .reshape(1, length_here, 2, heads * head_dim)
        .astype(jnp.bfloat16)
    )
    total = total_over(gain_sum, ("dp", "outer", "inner"))
    tokens_all = length_here * lax.axis_size("dp") * lax.axis_size("outer") * lax.axis_size("inner")
    gain_grad = total.reshape(heads * head_dim) * (1.0 / math.sqrt(tokens_all))
    return (grad_q, grad_k, grad_val, gain_grad)


def solution(mesh):
    return jax.shard_map(
        on_device,
        mesh=mesh,
        in_specs=(
            P("dp", ("outer", "inner"), None),
            P("dp", ("outer", "inner"), None, None),
            P("dp", ("outer", "inner"), None, None),
            P("dp", None, None, ("outer", "inner")),
            P("dp", ("outer", "inner"), None),
            P(),
        ),
        out_specs=(
            P("dp", ("outer", "inner"), None),
            P("dp", ("outer", "inner"), None, None),
            P("dp", ("outer", "inner"), None, None),
            P(),
        ),
        check_vma=False,
    )
```

```python
import math

import jax
import jax.numpy as jnp
from jax import lax
from jax.sharding import PartitionSpec as P

HEADS = 8
HEAD_DIM = 128
STRETCH = 64


EXACT = lax.Precision.HIGH
EPS_KEY = 1e-06
EPS_OUT = 1e-05


def butterfly(value, axes, distances):
    size = 1
    for axis in axes:
        size *= lax.axis_size(axis)
    for distance in distances:
        route = [(i, i ^ distance) for i in range(size)]
        value = value + lax.ppermute(value, axes, route)
    return value


def axis_bits(axis, stride):
    count = lax.axis_size(axis)
    return [stride * (count >> k) for k in range(1, count.bit_length())][::1]


def product(spec, left, right):
    return jnp.einsum(spec, left, right, precision=EXACT, preferred_element_type=jnp.float32)


def unit_rows(raw):
    scale_inv = lax.rsqrt(jnp.sum(raw * raw, axis=-1, keepdims=True) + EPS_KEY)
    return (raw * scale_inv, scale_inv)


def unit_back(unit, scale_inv, grad):
    width = unit.shape[-1]
    ones = jnp.ones((width, width), jnp.float32)
    along = product("hrd,de->hre", unit * grad, ones)
    return scale_inv * (grad - unit * along)


def compose(earlier, later):
    through = product("mhij,hjk->mhik", earlier, later[0])
    return through + jnp.stack([jnp.zeros_like(later[1]), later[1]])


def unit_lower_inverse(lower_mat):
    size = lower_mat.shape[-1]
    row_ids = lax.broadcasted_iota(jnp.int32, (size, size), 0)
    col_ids = lax.broadcasted_iota(jnp.int32, (size, size), 1)
    eye = (row_ids == col_ids).astype(jnp.float32)
    first = ((row_ids // 2) == (col_ids // 2)) & (row_ids > col_ids)
    inverse = eye - lower_mat * first.astype(jnp.float32)
    width = 2
    while width < size:
        inside = (row_ids // (2 * width)) == (col_ids // (2 * width))
        below = (row_ids // width) > (col_ids // width)
        coupling = lower_mat * (inside & below).astype(jnp.float32)
        left = product("bij,bjk->bik", inverse, coupling)
        inverse = inverse - product("bij,bjk->bik", left, inverse)
        width *= 2
    return inverse


def stretch_factors(key_blk, value_blk, rate_blk, inverse, eye_head):
    head_dim = key_blk.shape[2]
    rhs = jnp.concatenate(
        [rate_blk[:, :, None] * key_blk, rate_blk[:, :, None] * value_blk], axis=2
    )
    solved = product("hrs,hsd->hrd", inverse, rhs)
    w_mat = solved[:, :, :head_dim]
    t_vals = solved[:, :, head_dim:]
    transit = eye_head - product("hrd,hre->hde", w_mat, key_blk)
    return (inverse, w_mat, t_vals, transit)


def scan_maps(own_map, identity, step, axes):
    size = 1
    here = 0
    for axis in axes:
        size *= lax.axis_size(axis)
        here = here * lax.axis_size(axis) + lax.axis_index(axis)

    def shifted(block, distance):
        route = [(i, i + step * distance) for i in range(size) if 0 <= i + step * distance < size]
        return lax.ppermute(block, axes, route)

    def reached(distance):
        source = here - step * distance
        return (source >= 0) & (source < size)

    excl = jnp.where(reached(1), shifted(own_map, 1), identity)
    incl = compose(excl, own_map)
    distance = 2
    while distance < size:
        if 2 * distance >= size:
            got = shifted(incl[1], distance)
            state = product("hij,hjk->hik", got, excl[0]) + excl[1]
            return jnp.where(reached(distance), state, excl[1])
        got = shifted(incl, distance)
        ok = reached(distance)
        excl = jnp.where(ok, compose(got, excl), excl)
        incl = jnp.where(ok, compose(got, incl), incl)
        distance *= 2
    return excl[1]


def scan_split(own_map, identity, step):
    heads = own_map.shape[1]
    if lax.axis_size("inner") != 2 or heads % 2:
        return scan_maps(own_map, identity, step, ("outer", "inner"))
    half = heads // 2
    core = lax.axis_index("inner")
    lead = core == (0 if step > 0 else 1)
    swap = [(0, 1), (1, 0)]
    low = own_map[:, :half]
    high = own_map[:, half:]
    own_part = jnp.where(core == 0, low, high)
    other_part = jnp.where(core == 0, high, low)
    got = lax.ppermute(other_part, "inner", swap)
    first = jnp.where(lead, own_part, got)
    second = jnp.where(lead, got, own_part)
    chip_map = compose(first, second)
    start = scan_maps(chip_map, identity[:, :half], step, ("outer",))
    applied = product("hij,hjk->hik", start, first[0]) + first[1]
    for_other = jnp.where(lead, applied, start)
    keep = jnp.where(lead, start, applied)
    back = lax.ppermute(for_other, "inner", swap)
    return jnp.where(
        core == 0,
        jnp.concatenate([keep, back], axis=0),
        jnp.concatenate([back, keep], axis=0),
    )


def on_device(queries, keys, values, betas, grad_out, gain):
    length_here = queries.shape[1]
    heads = HEADS
    head_dim = HEAD_DIM
    span = STRETCH
    refl = 2 * span
    count = length_here // span
    query_raw = (
        queries[0].astype(jnp.float32).reshape(length_here, heads, head_dim).transpose(1, 0, 2)
    )
    key_raw = (
        keys[0]
        .astype(jnp.float32)
        .reshape(length_here, 2, heads, head_dim)
        .transpose(2, 0, 1, 3)
        .reshape(heads, 2 * length_here, head_dim)
    )
    value_all = (
        values[0]
        .astype(jnp.float32)
        .reshape(length_here, 2, heads, head_dim)
        .transpose(2, 0, 1, 3)
        .reshape(heads, 2 * length_here, head_dim)
    )
    rate_all = betas[0].transpose(0, 2, 1).reshape(heads, 2 * length_here)
    cotan_all = (
        grad_out[0].astype(jnp.float32).reshape(length_here, heads, head_dim).transpose(1, 0, 2)
    )
    gains = gain.reshape(heads, head_dim)
    query_n, query_inv = unit_rows(query_raw)
    key_n, key_inv = unit_rows(key_raw)
    token_ids = lax.broadcasted_iota(jnp.int32, (span, refl), 0)
    refl_ids = lax.broadcasted_iota(jnp.int32, (span, refl), 1)
    read_mask = (refl_ids <= 2 * token_ids + 1).astype(jnp.float32)
    row_ids = lax.broadcasted_iota(jnp.int32, (refl, refl), 0)
    col_ids = lax.broadcasted_iota(jnp.int32, (refl, refl), 1)
    strict = (col_ids < row_ids).astype(jnp.float32)
    eye_refl = jnp.eye(refl, dtype=jnp.float32)
    eye_head = jnp.eye(head_dim, dtype=jnp.float32)
    identity = jnp.stack(
        [
            jnp.broadcast_to(eye_head, (heads, head_dim, head_dim)),
            jnp.zeros((heads, head_dim, head_dim), jnp.float32),
        ]
    )

    def refl_rows(array, block_id):
        return array[:, block_id * refl : (block_id + 1) * refl]

    def token_rows(array, block_id):
        return array[:, block_id * span : (block_id + 1) * span]

    lower_all = []
    for block_id in range(count):
        key_blk = refl_rows(key_n, block_id)
        gram = product("hrd,hsd->hrs", key_blk, key_blk)
        lower_all.append(eye_refl + refl_rows(rate_all, block_id)[:, :, None] * gram * strict)
    inverse_all = unit_lower_inverse(jnp.concatenate(lower_all, axis=0)).reshape(
        count, heads, refl, refl
    )
    stash = []
    block_map = identity
    for block_id in range(count):
        key_blk = refl_rows(key_n, block_id)
        factor_set = stretch_factors(
            key_blk,
            refl_rows(value_all, block_id),
            refl_rows(rate_all, block_id),
            inverse_all[block_id],
            eye_head,
        )
        offset = product("hrv,hre->hve", factor_set[2], key_blk)
        block_map = compose(block_map, jnp.stack([factor_set[3], offset]))
        stash.append(factor_set)

    def factors_of(block_id):
        return stash[block_id]

    state = scan_split(block_map, identity, 1)
    records = []
    adjoint_maps = []
    gain_sum = jnp.zeros((heads, head_dim), jnp.float32)
    for block_id in range(count):
        inverse, w_mat, t_vals, transit = factors_of(block_id)
        key_blk = refl_rows(key_n, block_id)
        query_blk = token_rows(query_n, block_id)
        cotan_blk = token_rows(cotan_all, block_id)
        update = t_vals - product("hrk,hvk->hrv", w_mat, state)
        scores = product("htd,hrd->htr", query_blk, key_blk) * read_mask
        output = product("htk,hvk->htv", query_blk, state) + product("htr,hrv->htv", scores, update)
        scale_inv = lax.rsqrt(jnp.mean(output * output, axis=2, keepdims=True) + EPS_OUT)
        normed = output * scale_inv
        scaled = cotan_blk * gains[:, None, :]
        d_out = scale_inv * (scaled - normed * jnp.mean(normed * scaled, axis=2, keepdims=True))
        gain_sum = gain_sum + jnp.sum(cotan_blk * normed, axis=1)
        source = product("htv,htk->hvk", d_out, query_blk - product("htr,hrk->htk", scores, w_mat))
        records.append((state, update, scores, d_out))
        adjoint_maps.append(jnp.stack([jnp.swapaxes(transit, 1, 2), source]))
        state = state + product("hrv,hrk->hvk", update, key_blk)
    adjoint_block = identity
    for block_id in reversed(range(count)):
        adjoint_block = compose(adjoint_block, adjoint_maps[block_id])
    axes = ("dp", "outer", "inner")
    sizes = [lax.axis_size(axis) for axis in axes]
    if all(size & (size - 1) == 0 for size in sizes):
        inner_bits = axis_bits("inner", 1)
        outer_bits = axis_bits("outer", sizes[2])
        dp_bits = axis_bits("dp", sizes[1] * sizes[2])
        gain_sum = butterfly(gain_sum, axes, dp_bits + inner_bits)
    adjoint = scan_split(adjoint_block, identity, -1)
    if all(size & (size - 1) == 0 for size in sizes):
        adjoint, gain_sum = lax.optimization_barrier((adjoint, gain_sum))
        total = butterfly(gain_sum, axes, outer_bits)
    else:
        total = lax.psum(gain_sum, axes)
    grad_q_parts = [None] * count
    grad_k_parts = [None] * count
    grad_v_parts = [None] * count
    for block_id in reversed(range(count)):
        inverse, w_mat, t_vals, transit = factors_of(block_id)
        start_state, update, scores, d_out = records[block_id]
        key_blk = refl_rows(key_n, block_id)
        query_blk = token_rows(query_n, block_id)
        rate_blk = refl_rows(rate_all, block_id)
        d_update = product("htr,htv->hrv", scores, d_out) + product(
            "hrk,hvk->hrv", key_blk, adjoint
        )
        solved = product("hsr,hsv->hrv", inverse, d_update)
        d_target = rate_blk[:, :, None] * solved
        d_scores = product("htv,hrv->htr", d_out, update) * read_mask
        grad_q_parts[block_id] = product("htv,hvk->htk", d_out, start_state) + product(
            "htr,hrk->htk", d_scores, key_blk
        )
        d_gram = -product("hrv,hsv->hrs", d_target, update) * strict
        grad_k_parts[block_id] = (
            product("hrv,hvk->hrk", update, adjoint)
            + product("htr,htk->hrk", d_scores, query_blk)
            - product("hrv,hvk->hrk", d_target, start_state)
            + product("hrs,hsk->hrk", d_gram + jnp.swapaxes(d_gram, 1, 2), key_blk)
        )
        grad_v_parts[block_id] = d_target
        adjoint = (
            adjoint
            + product("htv,htk->hvk", d_out, query_blk)
            - product("hrv,hrk->hvk", d_target, key_blk)
        )
    grad_qn = jnp.concatenate(grad_q_parts, axis=1)
    grad_kn = jnp.concatenate(grad_k_parts, axis=1)
    grad_val = jnp.concatenate(grad_v_parts, axis=1)
    grad_q = unit_back(query_n, query_inv, grad_qn)
    grad_k = unit_back(key_n, key_inv, grad_kn)
    grad_q = (
        grad_q.transpose(1, 0, 2).reshape(1, length_here, heads * head_dim).astype(jnp.bfloat16)
    )
    grad_k = (
        grad_k.reshape(heads, length_here, 2, head_dim)
        .transpose(1, 2, 0, 3)
        .reshape(1, length_here, 2, heads * head_dim)
        .astype(jnp.bfloat16)
    )
    grad_val = (
        grad_val.reshape(heads, length_here, 2, head_dim)
        .transpose(1, 2, 0, 3)
        .reshape(1, length_here, 2, heads * head_dim)
        .astype(jnp.bfloat16)
    )
    tokens_all = length_here * lax.axis_size("dp") * lax.axis_size("outer") * lax.axis_size("inner")
    gain_grad = total.reshape(heads * head_dim) * (1.0 / math.sqrt(tokens_all))
    return (grad_q, grad_k, grad_val, gain_grad)


def solution(mesh):
    return jax.shard_map(
        on_device,
        mesh=mesh,
        in_specs=(
            P("dp", ("outer", "inner"), None),
            P("dp", ("outer", "inner"), None, None),
            P("dp", ("outer", "inner"), None, None),
            P("dp", None, None, ("outer", "inner")),
            P("dp", ("outer", "inner"), None),
            P(),
        ),
        out_specs=(
            P("dp", ("outer", "inner"), None),
            P("dp", ("outer", "inner"), None, None),
            P("dp", ("outer", "inner"), None, None),
            P(),
        ),
        check_vma=False,
    )
```

```python
import math

import jax
import jax.numpy as jnp
from jax import lax
from jax.sharding import PartitionSpec as P

HEADS = 8
HEAD_DIM = 128
STRETCH = 64


EXACT = lax.Precision.HIGH
FULL = lax.Precision.HIGHEST
EPS_KEY = 1e-06
EPS_OUT = 1e-05


def total_over(value, axes):
    size = 1
    for axis in axes:
        size *= lax.axis_size(axis)
    if size & (size - 1):
        return lax.psum(value, axes)
    distance = size // 2
    while distance >= 1:
        route = [(i, i ^ distance) for i in range(size)]
        value = value + lax.ppermute(value, axes, route)
        distance //= 2
    return value


def product(spec, left, right):
    return jnp.einsum(spec, left, right, precision=EXACT, preferred_element_type=jnp.float32)


def unit_rows(raw):
    scale_inv = lax.rsqrt(jnp.sum(raw * raw, axis=-1, keepdims=True) + EPS_KEY)
    return (raw * scale_inv, scale_inv)


def unit_back(unit, scale_inv, grad):
    width = unit.shape[-1]
    ones = jnp.ones((width, width), jnp.float32)
    along = jnp.einsum(
        "hrd,de->hre", unit * grad, ones, precision=FULL, preferred_element_type=jnp.float32
    )
    return scale_inv * (grad - unit * along)


def compose(earlier, later):
    through = product("mhij,hjk->mhik", earlier, later[0])
    return through + jnp.stack([jnp.zeros_like(later[1]), later[1]])


def unit_lower_inverse(lower_mat):
    size = lower_mat.shape[-1]
    row_ids = lax.broadcasted_iota(jnp.int32, (size, size), 0)
    col_ids = lax.broadcasted_iota(jnp.int32, (size, size), 1)
    eye = (row_ids == col_ids).astype(jnp.float32)
    first = ((row_ids // 2) == (col_ids // 2)) & (row_ids > col_ids)
    inverse = eye - lower_mat * first.astype(jnp.float32)
    width = 2
    while width < size:
        inside = (row_ids // (2 * width)) == (col_ids // (2 * width))
        below = (row_ids // width) > (col_ids // width)
        coupling = lower_mat * (inside & below).astype(jnp.float32)
        left = product("bij,bjk->bik", inverse, coupling)
        inverse = inverse - product("bij,bjk->bik", left, inverse)
        width *= 2
    return inverse


def scan_maps(own_map, identity, step, axes):
    size = 1
    here = 0
    for axis in axes:
        size *= lax.axis_size(axis)
        here = here * lax.axis_size(axis) + lax.axis_index(axis)

    def shifted(block, distance):
        route = [(i, i + step * distance) for i in range(size) if 0 <= i + step * distance < size]
        return lax.ppermute(block, axes, route)

    def reached(distance):
        source = here - step * distance
        return (source >= 0) & (source < size)

    excl = jnp.where(reached(1), shifted(own_map, 1), identity)
    incl = compose(excl, own_map)
    distance = 2
    while distance < size:
        if 2 * distance >= size:
            got = shifted(incl[1], distance)
            state = product("hij,hjk->hik", got, excl[0]) + excl[1]
            return jnp.where(reached(distance), state, excl[1])
        got = shifted(incl, distance)
        ok = reached(distance)
        excl = jnp.where(ok, compose(got, excl), excl)
        incl = jnp.where(ok, compose(got, incl), incl)
        distance *= 2
    return excl[1]


def scan_split(own_map, identity, step):
    heads = own_map.shape[1]
    if lax.axis_size("inner") != 2 or heads % 2:
        return scan_maps(own_map, identity, step, ("outer", "inner"))
    half = heads // 2
    core = lax.axis_index("inner")
    lead = core == (0 if step > 0 else 1)
    swap = [(0, 1), (1, 0)]
    low = own_map[:, :half]
    high = own_map[:, half:]
    own_part = jnp.where(core == 0, low, high)
    other_part = jnp.where(core == 0, high, low)
    got = lax.ppermute(other_part, "inner", swap)
    first = jnp.where(lead, own_part, got)
    second = jnp.where(lead, got, own_part)
    chip_map = compose(first, second)
    start = scan_maps(chip_map, identity[:, :half], step, ("outer",))
    applied = product("hij,hjk->hik", start, first[0]) + first[1]
    for_other = jnp.where(lead, applied, start)
    keep = jnp.where(lead, start, applied)
    back = lax.ppermute(for_other, "inner", swap)
    return jnp.where(
        core == 0,
        jnp.concatenate([keep, back], axis=0),
        jnp.concatenate([back, keep], axis=0),
    )


def on_device(queries, keys, values, betas, grad_out, gain):
    length_here = queries.shape[1]
    heads = HEADS
    head_dim = HEAD_DIM
    span = STRETCH
    refl = 2 * span
    count = length_here // span
    query_raw = (
        queries[0].astype(jnp.float32).reshape(length_here, heads, head_dim).transpose(1, 0, 2)
    )
    key_raw = (
        keys[0]
        .astype(jnp.float32)
        .reshape(length_here, 2, heads, head_dim)
        .transpose(2, 0, 1, 3)
        .reshape(heads, 2 * length_here, head_dim)
    )
    value_all = (
        values[0]
        .astype(jnp.float32)
        .reshape(length_here, 2, heads, head_dim)
        .transpose(2, 0, 1, 3)
        .reshape(heads, 2 * length_here, head_dim)
    )
    rate_all = betas[0].transpose(0, 2, 1).reshape(heads, 2 * length_here)
    cotan_all = (
        grad_out[0].astype(jnp.float32).reshape(length_here, heads, head_dim).transpose(1, 0, 2)
    )
    gains = gain.reshape(heads, head_dim)
    query_n, query_inv = unit_rows(query_raw)
    key_n, key_inv = unit_rows(key_raw)
    token_ids = lax.broadcasted_iota(jnp.int32, (span, refl), 0)
    refl_ids = lax.broadcasted_iota(jnp.int32, (span, refl), 1)
    read_mask = (refl_ids <= 2 * token_ids + 1).astype(jnp.float32)
    row_ids = lax.broadcasted_iota(jnp.int32, (refl, refl), 0)
    col_ids = lax.broadcasted_iota(jnp.int32, (refl, refl), 1)
    strict = (col_ids < row_ids).astype(jnp.float32)
    eye_refl = jnp.eye(refl, dtype=jnp.float32)
    eye_head = jnp.eye(head_dim, dtype=jnp.float32)
    identity = jnp.stack(
        [
            jnp.broadcast_to(eye_head, (heads, head_dim, head_dim)),
            jnp.zeros((heads, head_dim, head_dim), jnp.float32),
        ]
    )

    def blocks(array, rows):
        shape = array.shape
        split = array.reshape((shape[0], count, rows) + shape[2:])
        return jnp.swapaxes(split, 0, 1).reshape((count * shape[0], rows) + shape[2:])

    def unblocks(array):
        shape = array.shape
        split = array.reshape((count, heads) + shape[1:])
        return jnp.swapaxes(split, 0, 1).reshape((heads, count * shape[1]) + shape[2:])

    def per_block(array):
        return array.reshape((count, heads) + array.shape[1:])

    key_b = blocks(key_n, refl)
    query_b = blocks(query_n, span)
    value_b = blocks(value_all, refl)
    rate_b = blocks(rate_all, refl)
    cotan_b = blocks(cotan_all, span)
    gram = product("brd,bsd->brs", key_b, key_b)
    lower_b = eye_refl + rate_b[:, :, None] * gram * strict
    inverse_b = unit_lower_inverse(lower_b)
    rhs = jnp.concatenate([rate_b[:, :, None] * key_b, rate_b[:, :, None] * value_b], axis=2)
    solved = product("brs,bsd->brd", inverse_b, rhs)
    w_b = solved[:, :, :head_dim]
    t_b = solved[:, :, head_dim:]
    transit_b = eye_head - product("brd,bre->bde", w_b, key_b)
    offset_b = product("brv,bre->bve", t_b, key_b)
    transit_k = per_block(transit_b)
    offset_k = per_block(offset_b)
    block_map = jnp.stack([transit_k[0], offset_k[0]])
    for block_id in range(1, count):
        block_map = compose(block_map, jnp.stack([transit_k[block_id], offset_k[block_id]]))
    state = scan_split(block_map, identity, 1)
    starts = [state]
    for block_id in range(count - 1):
        state = product("hvd,hde->hve", state, transit_k[block_id]) + offset_k[block_id]
        starts.append(state)
    state_b = jnp.concatenate(starts, axis=0)
    update_b = t_b - product("brk,bvk->brv", w_b, state_b)
    scores_b = product("btd,brd->btr", query_b, key_b) * read_mask
    output_b = product("btk,bvk->btv", query_b, state_b) + product("btr,brv->btv", scores_b, update_b)
    scale_inv = lax.rsqrt(jnp.mean(output_b * output_b, axis=2, keepdims=True) + EPS_OUT)
    normed = output_b * scale_inv
    gains_b = jnp.concatenate([gains] * count, axis=0)
    scaled = cotan_b * gains_b[:, None, :]
    d_out = scale_inv * (scaled - normed * jnp.mean(normed * scaled, axis=2, keepdims=True))
    gain_sum = jnp.sum(per_block(jnp.sum(cotan_b * normed, axis=1)), axis=0)
    source_b = product(
        "btv,btk->bvk", d_out, query_b - product("btr,brk->btk", scores_b, w_b)
    )
    transpose_k = per_block(jnp.swapaxes(transit_b, 1, 2))
    source_k = per_block(source_b)
    adjoint_block = jnp.stack([transpose_k[count - 1], source_k[count - 1]])
    for block_id in reversed(range(count - 1)):
        adjoint_block = compose(adjoint_block, jnp.stack([transpose_k[block_id], source_k[block_id]]))
    adjoint = scan_split(adjoint_block, identity, -1)
    ends = [adjoint]
    for block_id in reversed(range(1, count)):
        adjoint = product("hvd,hde->hve", adjoint, transpose_k[block_id]) + source_k[block_id]
        ends.append(adjoint)
    adjoint_b = jnp.concatenate(ends[::-1], axis=0)
    d_update = product("btr,btv->brv", scores_b, d_out) + product("brk,bvk->brv", key_b, adjoint_b)
    d_target = rate_b[:, :, None] * product("bsr,bsv->brv", inverse_b, d_update)
    d_scores = product("btv,brv->btr", d_out, update_b) * read_mask
    grad_q_b = product("btv,bvk->btk", d_out, state_b) + product("btr,brk->btk", d_scores, key_b)
    d_gram = -product("brv,bsv->brs", d_target, update_b) * strict
    grad_k_b = (
        product("brv,bvk->brk", update_b, adjoint_b)
        + product("btr,btk->brk", d_scores, query_b)
        - product("brv,bvk->brk", d_target, state_b)
        + product("brs,bsk->brk", d_gram + jnp.swapaxes(d_gram, 1, 2), key_b)
    )
    grad_qn = unblocks(grad_q_b)
    grad_kn = unblocks(grad_k_b)
    grad_val = unblocks(d_target)
    grad_q = unit_back(query_n, query_inv, grad_qn)
    grad_k = unit_back(key_n, key_inv, grad_kn)
    grad_q = (
        grad_q.transpose(1, 0, 2).reshape(1, length_here, heads * head_dim).astype(jnp.bfloat16)
    )
    grad_k = (
        grad_k.reshape(heads, length_here, 2, head_dim)
        .transpose(1, 2, 0, 3)
        .reshape(1, length_here, 2, heads * head_dim)
        .astype(jnp.bfloat16)
    )
    grad_val = (
        grad_val.reshape(heads, length_here, 2, head_dim)
        .transpose(1, 2, 0, 3)
        .reshape(1, length_here, 2, heads * head_dim)
        .astype(jnp.bfloat16)
    )
    total = total_over(gain_sum, ("dp", "outer", "inner"))
    tokens_all = length_here * lax.axis_size("dp") * lax.axis_size("outer") * lax.axis_size("inner")
    gain_grad = total.reshape(heads * head_dim) * (1.0 / math.sqrt(tokens_all))
    return (grad_q, grad_k, grad_val, gain_grad)


def solution(mesh):
    return jax.shard_map(
        on_device,
        mesh=mesh,
        in_specs=(
            P("dp", ("outer", "inner"), None),
            P("dp", ("outer", "inner"), None, None),
            P("dp", ("outer", "inner"), None, None),
            P("dp", None, None, ("outer", "inner")),
            P("dp", ("outer", "inner"), None),
            P(),
        ),
        out_specs=(
            P("dp", ("outer", "inner"), None),
            P("dp", ("outer", "inner"), None, None),
            P("dp", ("outer", "inner"), None, None),
            P(),
        ),
        check_vma=False,
    )
```

```python
import math

import jax
import jax.numpy as jnp
from jax import lax
from jax.sharding import PartitionSpec as P

HEADS = 8
HEAD_DIM = 128
STRETCH = 64


EXACT = lax.Precision.HIGH
FULL = lax.Precision.HIGHEST
EPS_KEY = 1e-06
EPS_OUT = 1e-05


def total_over(value, axes):
    size = 1
    for axis in axes:
        size *= lax.axis_size(axis)
    if size & (size - 1):
        return lax.psum(value, axes)
    distance = size // 2
    while distance >= 1:
        route = [(i, i ^ distance) for i in range(size)]
        value = value + lax.ppermute(value, axes, route)
        distance //= 2
    return value


def product(spec, left, right):
    return jnp.einsum(spec, left, right, precision=EXACT, preferred_element_type=jnp.float32)


def unit_rows(raw):
    scale_inv = lax.rsqrt(jnp.sum(raw * raw, axis=-1, keepdims=True) + EPS_KEY)
    return (raw * scale_inv, scale_inv)


def unit_back(unit, scale_inv, grad):
    width = unit.shape[-1]
    ones = jnp.ones((width, width), jnp.float32)
    along = jnp.einsum(
        "hrd,de->hre", unit * grad, ones, precision=FULL, preferred_element_type=jnp.float32
    )
    return scale_inv * (grad - unit * along)


def compose(earlier, later):
    through = product("mhij,hjk->mhik", earlier, later[0])
    return through + jnp.stack([jnp.zeros_like(later[1]), later[1]])


def unit_lower_inverse(lower_mat):
    size = lower_mat.shape[-1]
    row_ids = lax.broadcasted_iota(jnp.int32, (size, size), 0)
    col_ids = lax.broadcasted_iota(jnp.int32, (size, size), 1)
    eye = (row_ids == col_ids).astype(jnp.float32)
    first = ((row_ids // 2) == (col_ids // 2)) & (row_ids > col_ids)
    inverse = eye - lower_mat * first.astype(jnp.float32)
    width = 2
    while width < size:
        inside = (row_ids // (2 * width)) == (col_ids // (2 * width))
        below = (row_ids // width) > (col_ids // width)
        coupling = lower_mat * (inside & below).astype(jnp.float32)
        left = jnp.einsum("bij,bjk->bik", inverse, coupling, precision=FULL)
        inverse = inverse - jnp.einsum("bij,bjk->bik", left, inverse, precision=FULL)
        width *= 2
    return inverse


def stretch_factors(key_blk, value_blk, rate_blk, inverse, eye_head):
    head_dim = key_blk.shape[2]
    rhs = jnp.concatenate(
        [rate_blk[:, :, None] * key_blk, rate_blk[:, :, None] * value_blk], axis=2
    )
    solved = product("hrs,hsd->hrd", inverse, rhs)
    w_mat = solved[:, :, :head_dim]
    t_vals = solved[:, :, head_dim:]
    transit = eye_head - product("hrd,hre->hde", w_mat, key_blk)
    return (inverse, w_mat, t_vals, transit)


def scan_maps(own_map, identity, step, axes):
    size = 1
    here = 0
    for axis in axes:
        size *= lax.axis_size(axis)
        here = here * lax.axis_size(axis) + lax.axis_index(axis)

    def shifted(block, distance):
        route = [(i, i + step * distance) for i in range(size) if 0 <= i + step * distance < size]
        return lax.ppermute(block, axes, route)

    def reached(distance):
        source = here - step * distance
        return (source >= 0) & (source < size)

    excl = jnp.where(reached(1), shifted(own_map, 1), identity)
    incl = compose(excl, own_map)
    distance = 2
    while distance < size:
        if 2 * distance >= size:
            got = shifted(incl[1], distance)
            state = product("hij,hjk->hik", got, excl[0]) + excl[1]
            return jnp.where(reached(distance), state, excl[1])
        got = shifted(incl, distance)
        ok = reached(distance)
        excl = jnp.where(ok, compose(got, excl), excl)
        incl = jnp.where(ok, compose(got, incl), incl)
        distance *= 2
    return excl[1]


def scan_split(own_map, identity, step):
    heads = own_map.shape[1]
    if lax.axis_size("inner") != 2 or heads % 2:
        return scan_maps(own_map, identity, step, ("outer", "inner"))
    half = heads // 2
    core = lax.axis_index("inner")
    lead = core == (0 if step > 0 else 1)
    swap = [(0, 1), (1, 0)]
    low = own_map[:, :half]
    high = own_map[:, half:]
    own_part = jnp.where(core == 0, low, high)
    other_part = jnp.where(core == 0, high, low)
    got = lax.ppermute(other_part, "inner", swap)
    first = jnp.where(lead, own_part, got)
    second = jnp.where(lead, got, own_part)
    chip_map = compose(first, second)
    start = scan_maps(chip_map, identity[:, :half], step, ("outer",))
    applied = product("hij,hjk->hik", start, first[0]) + first[1]
    for_other = jnp.where(lead, applied, start)
    keep = jnp.where(lead, start, applied)
    back = lax.ppermute(for_other, "inner", swap)
    return jnp.where(
        core == 0,
        jnp.concatenate([keep, back], axis=0),
        jnp.concatenate([back, keep], axis=0),
    )


def on_device(queries, keys, values, betas, grad_out, gain):
    length_here = queries.shape[1]
    heads = HEADS
    head_dim = HEAD_DIM
    span = STRETCH
    refl = 2 * span
    count = length_here // span
    query_raw = (
        queries[0].astype(jnp.float32).reshape(length_here, heads, head_dim).transpose(1, 0, 2)
    )
    key_raw = (
        keys[0]
        .astype(jnp.float32)
        .reshape(length_here, 2, heads, head_dim)
        .transpose(2, 0, 1, 3)
        .reshape(heads, 2 * length_here, head_dim)
    )
    value_all = (
        values[0]
        .astype(jnp.float32)
        .reshape(length_here, 2, heads, head_dim)
        .transpose(2, 0, 1, 3)
        .reshape(heads, 2 * length_here, head_dim)
    )
    rate_all = betas[0].transpose(0, 2, 1).reshape(heads, 2 * length_here)
    cotan_all = (
        grad_out[0].astype(jnp.float32).reshape(length_here, heads, head_dim).transpose(1, 0, 2)
    )
    gains = gain.reshape(heads, head_dim)
    query_n, query_inv = unit_rows(query_raw)
    key_n, key_inv = unit_rows(key_raw)
    token_ids = lax.broadcasted_iota(jnp.int32, (span, refl), 0)
    refl_ids = lax.broadcasted_iota(jnp.int32, (span, refl), 1)
    read_mask = (refl_ids <= 2 * token_ids + 1).astype(jnp.float32)
    row_ids = lax.broadcasted_iota(jnp.int32, (refl, refl), 0)
    col_ids = lax.broadcasted_iota(jnp.int32, (refl, refl), 1)
    strict = (col_ids < row_ids).astype(jnp.float32)
    eye_refl = jnp.eye(refl, dtype=jnp.float32)
    eye_head = jnp.eye(head_dim, dtype=jnp.float32)
    identity = jnp.stack(
        [
            jnp.broadcast_to(eye_head, (heads, head_dim, head_dim)),
            jnp.zeros((heads, head_dim, head_dim), jnp.float32),
        ]
    )

    def refl_rows(array, block_id):
        return array[:, block_id * refl : (block_id + 1) * refl]

    def token_rows(array, block_id):
        return array[:, block_id * span : (block_id + 1) * span]

    lower_all = []
    for block_id in range(count):
        key_blk = refl_rows(key_n, block_id)
        gram = product("hrd,hsd->hrs", key_blk, key_blk)
        lower_all.append(eye_refl + refl_rows(rate_all, block_id)[:, :, None] * gram * strict)
    inverse_all = unit_lower_inverse(jnp.concatenate(lower_all, axis=0)).reshape(
        count, heads, refl, refl
    )
    stash = []
    block_map = identity
    for block_id in range(count):
        key_blk = refl_rows(key_n, block_id)
        factor_set = stretch_factors(
            key_blk,
            refl_rows(value_all, block_id),
            refl_rows(rate_all, block_id),
            inverse_all[block_id],
            eye_head,
        )
        offset = product("hrv,hre->hve", factor_set[2], key_blk)
        block_map = compose(block_map, jnp.stack([factor_set[3], offset]))
        stash.append(factor_set)

    def factors_of(block_id):
        return stash[block_id]

    state = scan_split(block_map, identity, 1)
    records = []
    adjoint_maps = []
    gain_sum = jnp.zeros((heads, head_dim), jnp.float32)
    for block_id in range(count):
        inverse, w_mat, t_vals, transit = factors_of(block_id)
        key_blk = refl_rows(key_n, block_id)
        query_blk = token_rows(query_n, block_id)
        cotan_blk = token_rows(cotan_all, block_id)
        update = t_vals - product("hrk,hvk->hrv", w_mat, state)
        scores = product("htd,hrd->htr", query_blk, key_blk) * read_mask
        output = product("htk,hvk->htv", query_blk, state) + product("htr,hrv->htv", scores, update)
        scale_inv = lax.rsqrt(jnp.mean(output * output, axis=2, keepdims=True) + EPS_OUT)
        normed = output * scale_inv
        scaled = cotan_blk * gains[:, None, :]
        d_out = scale_inv * (scaled - normed * jnp.mean(normed * scaled, axis=2, keepdims=True))
        gain_sum = gain_sum + jnp.sum(cotan_blk * normed, axis=1)
        source = product("htv,htk->hvk", d_out, query_blk - product("htr,hrk->htk", scores, w_mat))
        records.append((state, update, scores, d_out))
        adjoint_maps.append(jnp.stack([jnp.swapaxes(transit, 1, 2), source]))
        state = state + product("hrv,hrk->hvk", update, key_blk)
    adjoint_block = identity
    for block_id in reversed(range(count)):
        adjoint_block = compose(adjoint_block, adjoint_maps[block_id])
    adjoint = scan_split(adjoint_block, identity, -1)
    grad_q_parts = [None] * count
    grad_k_parts = [None] * count
    grad_v_parts = [None] * count
    for block_id in reversed(range(count)):
        inverse, w_mat, t_vals, transit = factors_of(block_id)
        start_state, update, scores, d_out = records[block_id]
        key_blk = refl_rows(key_n, block_id)
        query_blk = token_rows(query_n, block_id)
        rate_blk = refl_rows(rate_all, block_id)
        d_update = product("htr,htv->hrv", scores, d_out) + product(
            "hrk,hvk->hrv", key_blk, adjoint
        )
        solved = product("hsr,hsv->hrv", inverse, d_update)
        d_target = rate_blk[:, :, None] * solved
        d_scores = product("htv,hrv->htr", d_out, update) * read_mask
        grad_q_parts[block_id] = product("htv,hvk->htk", d_out, start_state) + product(
            "htr,hrk->htk", d_scores, key_blk
        )
        d_gram = -product("hrv,hsv->hrs", d_target, update) * strict
        grad_k_parts[block_id] = (
            product("hrv,hvk->hrk", update, adjoint)
            + product("htr,htk->hrk", d_scores, query_blk)
            - product("hrv,hvk->hrk", d_target, start_state)
            + product("hrs,hsk->hrk", d_gram + jnp.swapaxes(d_gram, 1, 2), key_blk)
        )
        grad_v_parts[block_id] = d_target
        adjoint = (
            adjoint
            + product("htv,htk->hvk", d_out, query_blk)
            - product("hrv,hrk->hvk", d_target, key_blk)
        )
    grad_qn = jnp.concatenate(grad_q_parts, axis=1)
    grad_kn = jnp.concatenate(grad_k_parts, axis=1)
    grad_val = jnp.concatenate(grad_v_parts, axis=1)
    grad_q = unit_back(query_n, query_inv, grad_qn)
    grad_k = unit_back(key_n, key_inv, grad_kn)
    grad_q = (
        grad_q.transpose(1, 0, 2).reshape(1, length_here, heads * head_dim).astype(jnp.bfloat16)
    )
    grad_k = (
        grad_k.reshape(heads, length_here, 2, head_dim)
        .transpose(1, 2, 0, 3)
        .reshape(1, length_here, 2, heads * head_dim)
        .astype(jnp.bfloat16)
    )
    grad_val = (
        grad_val.reshape(heads, length_here, 2, head_dim)
        .transpose(1, 2, 0, 3)
        .reshape(1, length_here, 2, heads * head_dim)
        .astype(jnp.bfloat16)
    )
    total = total_over(gain_sum, ("dp", "outer", "inner"))
    tokens_all = length_here * lax.axis_size("dp") * lax.axis_size("outer") * lax.axis_size("inner")
    gain_grad = total.reshape(heads * head_dim) * (1.0 / math.sqrt(tokens_all))
    return (grad_q, grad_k, grad_val, gain_grad)


def solution(mesh):
    return jax.shard_map(
        on_device,
        mesh=mesh,
        in_specs=(
            P("dp", ("outer", "inner"), None),
            P("dp", ("outer", "inner"), None, None),
            P("dp", ("outer", "inner"), None, None),
            P("dp", None, None, ("outer", "inner")),
            P("dp", ("outer", "inner"), None),
            P(),
        ),
        out_specs=(
            P("dp", ("outer", "inner"), None),
            P("dp", ("outer", "inner"), None, None),
            P("dp", ("outer", "inner"), None, None),
            P(),
        ),
        check_vma=False,
    )
```

```python
import math

import jax
import jax.numpy as jnp
from jax import lax
from jax.sharding import PartitionSpec as P

HEADS = 8
HEAD_DIM = 128
STRETCH = 64


EXACT = lax.Precision.HIGH
EPS_KEY = 1e-06
EPS_OUT = 1e-05


def total_over(value, axes):
    size = 1
    for axis in axes:
        size *= lax.axis_size(axis)
    if size & (size - 1):
        return lax.psum(value, axes)
    distance = size // 2
    while distance >= 1:
        route = [(i, i ^ distance) for i in range(size)]
        value = value + lax.ppermute(value, axes, route)
        distance //= 2
    return value


def product(spec, left, right):
    return jnp.einsum(spec, left, right, precision=EXACT, preferred_element_type=jnp.float32)


def unit_rows(raw):
    scale_inv = lax.rsqrt(jnp.sum(raw * raw, axis=-1, keepdims=True) + EPS_KEY)
    return (raw * scale_inv, scale_inv)


def unit_back(unit, scale_inv, grad):
    width = unit.shape[-1]
    ones = jnp.ones((width, width), jnp.float32)
    along = product("hrd,de->hre", unit * grad, ones)
    return scale_inv * (grad - unit * along)


def compose(earlier, later):
    through = product("mhij,hjk->mhik", earlier, later[0])
    return through + jnp.stack([jnp.zeros_like(later[1]), later[1]])


def unit_lower_inverse(lower_mat):
    size = lower_mat.shape[-1]
    row_ids = lax.broadcasted_iota(jnp.int32, (size, size), 0)
    col_ids = lax.broadcasted_iota(jnp.int32, (size, size), 1)
    eye = (row_ids == col_ids).astype(jnp.float32)
    first = ((row_ids // 2) == (col_ids // 2)) & (row_ids > col_ids)
    inverse = eye - lower_mat * first.astype(jnp.float32)
    width = 2
    while width < size:
        inside = (row_ids // (2 * width)) == (col_ids // (2 * width))
        below = (row_ids // width) > (col_ids // width)
        coupling = lower_mat * (inside & below).astype(jnp.float32)
        left = product("bij,bjk->bik", inverse, coupling)
        inverse = inverse - product("bij,bjk->bik", left, inverse)
        width *= 2
    return inverse


def stretch_factors(key_blk, value_blk, rate_blk, inverse, eye_head):
    head_dim = key_blk.shape[2]
    rhs = jnp.concatenate(
        [rate_blk[:, :, None] * key_blk, rate_blk[:, :, None] * value_blk], axis=2
    )
    solved = product("hrs,hsd->hrd", inverse, rhs)
    w_mat = solved[:, :, :head_dim]
    t_vals = solved[:, :, head_dim:]
    transit = eye_head - product("hrd,hre->hde", w_mat, key_blk)
    return (inverse, w_mat, t_vals, transit)


def scan_maps(own_map, identity, step, axes, known=None):
    size = 1
    here = 0
    for axis in axes:
        size *= lax.axis_size(axis)
        here = here * lax.axis_size(axis) + lax.axis_index(axis)

    def shifted(block, distance):
        route = [(i, i + step * distance) for i in range(size) if 0 <= i + step * distance < size]
        return lax.ppermute(block, axes, route)

    def reached(distance):
        source = here - step * distance
        return (source >= 0) & (source < size)

    if known is None:
        excl = jnp.where(reached(1), shifted(own_map, 1), identity)
    else:
        got = jnp.stack([known, shifted(own_map[1], 1)])
        excl = jnp.where(reached(1), got, identity)
    incl = compose(excl, own_map)
    distance = 2
    while distance < size:
        if 2 * distance >= size:
            got = shifted(incl[1], distance)
            state = product("hij,hjk->hik", got, excl[0]) + excl[1]
            return jnp.where(reached(distance), state, excl[1])
        got = shifted(incl, distance)
        ok = reached(distance)
        excl = jnp.where(ok, compose(got, excl), excl)
        incl = jnp.where(ok, compose(got, incl), incl)
        distance *= 2
    return excl[1]


def scan_split(own_map, identity, step, known=None):
    heads = own_map.shape[1]
    if lax.axis_size("inner") != 2 or heads % 2:
        return scan_maps(own_map, identity, step, ("outer", "inner")), None
    half = heads // 2
    core = lax.axis_index("inner")
    lead = core == (0 if step > 0 else 1)
    swap = [(0, 1), (1, 0)]
    low = own_map[:, :half]
    high = own_map[:, half:]
    own_part = jnp.where(core == 0, low, high)
    other_part = jnp.where(core == 0, high, low)
    got = lax.ppermute(other_part, "inner", swap)
    first = jnp.where(lead, own_part, got)
    second = jnp.where(lead, got, own_part)
    chip_map = compose(first, second)
    chips = lax.axis_size("outer")
    back_route = [(i, i - step) for i in range(chips) if 0 <= i - step < chips]
    ahead = lax.ppermute(chip_map[0], "outer", back_route) if known is None else None
    start = scan_maps(chip_map, identity[:, :half], step, ("outer",), known)
    applied = product("hij,hjk->hik", start, first[0]) + first[1]
    for_other = jnp.where(lead, applied, start)
    keep = jnp.where(lead, start, applied)
    back = lax.ppermute(for_other, "inner", swap)
    whole = jnp.where(
        core == 0,
        jnp.concatenate([keep, back], axis=0),
        jnp.concatenate([back, keep], axis=0),
    )
    return whole, ahead


def on_device(queries, keys, values, betas, grad_out, gain):
    length_here = queries.shape[1]
    heads = HEADS
    head_dim = HEAD_DIM
    span = STRETCH
    refl = 2 * span
    count = length_here // span
    query_raw = (
        queries[0].astype(jnp.float32).reshape(length_here, heads, head_dim).transpose(1, 0, 2)
    )
    key_raw = (
        keys[0]
        .astype(jnp.float32)
        .reshape(length_here, 2, heads, head_dim)
        .transpose(2, 0, 1, 3)
        .reshape(heads, 2 * length_here, head_dim)
    )
    value_all = (
        values[0]
        .astype(jnp.float32)
        .reshape(length_here, 2, heads, head_dim)
        .transpose(2, 0, 1, 3)
        .reshape(heads, 2 * length_here, head_dim)
    )
    rate_all = betas[0].transpose(0, 2, 1).reshape(heads, 2 * length_here)
    cotan_all = (
        grad_out[0].astype(jnp.float32).reshape(length_here, heads, head_dim).transpose(1, 0, 2)
    )
    gains = gain.reshape(heads, head_dim)
    query_n, query_inv = unit_rows(query_raw)
    key_n, key_inv = unit_rows(key_raw)
    token_ids = lax.broadcasted_iota(jnp.int32, (span, refl), 0)
    refl_ids = lax.broadcasted_iota(jnp.int32, (span, refl), 1)
    read_mask = (refl_ids <= 2 * token_ids + 1).astype(jnp.float32)
    row_ids = lax.broadcasted_iota(jnp.int32, (refl, refl), 0)
    col_ids = lax.broadcasted_iota(jnp.int32, (refl, refl), 1)
    strict = (col_ids < row_ids).astype(jnp.float32)
    eye_refl = jnp.eye(refl, dtype=jnp.float32)
    eye_head = jnp.eye(head_dim, dtype=jnp.float32)
    identity = jnp.stack(
        [
            jnp.broadcast_to(eye_head, (heads, head_dim, head_dim)),
            jnp.zeros((heads, head_dim, head_dim), jnp.float32),
        ]
    )

    def refl_rows(array, block_id):
        return array[:, block_id * refl : (block_id + 1) * refl]

    def token_rows(array, block_id):
        return array[:, block_id * span : (block_id + 1) * span]

    lower_all = []
    for block_id in range(count):
        key_blk = refl_rows(key_n, block_id)
        gram = product("hrd,hsd->hrs", key_blk, key_blk)
        lower_all.append(eye_refl + refl_rows(rate_all, block_id)[:, :, None] * gram * strict)
    inverse_all = unit_lower_inverse(jnp.concatenate(lower_all, axis=0)).reshape(
        count, heads, refl, refl
    )
    stash = []
    block_map = identity
    for block_id in range(count):
        key_blk = refl_rows(key_n, block_id)
        factor_set = stretch_factors(
            key_blk,
            refl_rows(value_all, block_id),
            refl_rows(rate_all, block_id),
            inverse_all[block_id],
            eye_head,
        )
        offset = product("hrv,hre->hve", factor_set[2], key_blk)
        block_map = compose(block_map, jnp.stack([factor_set[3], offset]))
        stash.append(factor_set)

    def factors_of(block_id):
        return stash[block_id]

    state, ahead = scan_split(block_map, identity, 1)
    records = []
    adjoint_maps = []
    gain_sum = jnp.zeros((heads, head_dim), jnp.float32)
    for block_id in range(count):
        inverse, w_mat, t_vals, transit = factors_of(block_id)
        key_blk = refl_rows(key_n, block_id)
        query_blk = token_rows(query_n, block_id)
        cotan_blk = token_rows(cotan_all, block_id)
        update = t_vals - product("hrk,hvk->hrv", w_mat, state)
        scores = product("htd,hrd->htr", query_blk, key_blk) * read_mask
        output = product("htk,hvk->htv", query_blk, state) + product("htr,hrv->htv", scores, update)
        scale_inv = lax.rsqrt(jnp.mean(output * output, axis=2, keepdims=True) + EPS_OUT)
        normed = output * scale_inv
        scaled = cotan_blk * gains[:, None, :]
        d_out = scale_inv * (scaled - normed * jnp.mean(normed * scaled, axis=2, keepdims=True))
        gain_sum = gain_sum + jnp.sum(cotan_blk * normed, axis=1)
        source = product("htv,htk->hvk", d_out, query_blk - product("htr,hrk->htk", scores, w_mat))
        records.append((state, update, scores, d_out))
        adjoint_maps.append(jnp.stack([jnp.swapaxes(transit, 1, 2), source]))
        state = state + product("hrv,hrk->hvk", update, key_blk)
    adjoint_block = identity
    for block_id in reversed(range(count)):
        adjoint_block = compose(adjoint_block, adjoint_maps[block_id])
    known = None if ahead is None else jnp.swapaxes(ahead, 1, 2)
    adjoint, _ = scan_split(adjoint_block, identity, -1, known)
    grad_q_parts = [None] * count
    grad_k_parts = [None] * count
    grad_v_parts = [None] * count
    for block_id in reversed(range(count)):
        inverse, w_mat, t_vals, transit = factors_of(block_id)
        start_state, update, scores, d_out = records[block_id]
        key_blk = refl_rows(key_n, block_id)
        query_blk = token_rows(query_n, block_id)
        rate_blk = refl_rows(rate_all, block_id)
        d_update = product("htr,htv->hrv", scores, d_out) + product(
            "hrk,hvk->hrv", key_blk, adjoint
        )
        solved = product("hsr,hsv->hrv", inverse, d_update)
        d_target = rate_blk[:, :, None] * solved
        d_scores = product("htv,hrv->htr", d_out, update) * read_mask
        grad_q_parts[block_id] = product("htv,hvk->htk", d_out, start_state) + product(
            "htr,hrk->htk", d_scores, key_blk
        )
        d_gram = -product("hrv,hsv->hrs", d_target, update) * strict
        grad_k_parts[block_id] = (
            product("hrv,hvk->hrk", update, adjoint)
            + product("htr,htk->hrk", d_scores, query_blk)
            - product("hrv,hvk->hrk", d_target, start_state)
            + product("hrs,hsk->hrk", d_gram + jnp.swapaxes(d_gram, 1, 2), key_blk)
        )
        grad_v_parts[block_id] = d_target
        adjoint = (
            adjoint
            + product("htv,htk->hvk", d_out, query_blk)
            - product("hrv,hrk->hvk", d_target, key_blk)
        )
    grad_qn = jnp.concatenate(grad_q_parts, axis=1)
    grad_kn = jnp.concatenate(grad_k_parts, axis=1)
    grad_val = jnp.concatenate(grad_v_parts, axis=1)
    grad_q = unit_back(query_n, query_inv, grad_qn)
    grad_k = unit_back(key_n, key_inv, grad_kn)
    grad_q = (
        grad_q.transpose(1, 0, 2).reshape(1, length_here, heads * head_dim).astype(jnp.bfloat16)
    )
    grad_k = (
        grad_k.reshape(heads, length_here, 2, head_dim)
        .transpose(1, 2, 0, 3)
        .reshape(1, length_here, 2, heads * head_dim)
        .astype(jnp.bfloat16)
    )
    grad_val = (
        grad_val.reshape(heads, length_here, 2, head_dim)
        .transpose(1, 2, 0, 3)
        .reshape(1, length_here, 2, heads * head_dim)
        .astype(jnp.bfloat16)
    )
    total = total_over(gain_sum, ("dp", "outer", "inner"))
    tokens_all = length_here * lax.axis_size("dp") * lax.axis_size("outer") * lax.axis_size("inner")
    gain_grad = total.reshape(heads * head_dim) * (1.0 / math.sqrt(tokens_all))
    return (grad_q, grad_k, grad_val, gain_grad)


def solution(mesh):
    return jax.shard_map(
        on_device,
        mesh=mesh,
        in_specs=(
            P("dp", ("outer", "inner"), None),
            P("dp", ("outer", "inner"), None, None),
            P("dp", ("outer", "inner"), None, None),
            P("dp", None, None, ("outer", "inner")),
            P("dp", ("outer", "inner"), None),
            P(),
        ),
        out_specs=(
            P("dp", ("outer", "inner"), None),
            P("dp", ("outer", "inner"), None, None),
            P("dp", ("outer", "inner"), None, None),
            P(),
        ),
        check_vma=False,
    )
```

```python
import math

import jax
import jax.numpy as jnp
from jax import lax
from jax.sharding import PartitionSpec as P

HEADS = 8
HEAD_DIM = 128
STRETCH = 64


EXACT = lax.Precision.HIGH
EPS_KEY = 1e-06
EPS_OUT = 1e-05


def total_over(value, axes):
    size = 1
    for axis in axes:
        size *= lax.axis_size(axis)
    if size & (size - 1):
        return lax.psum(value, axes)
    distance = size // 2
    while distance >= 1:
        route = [(i, i ^ distance) for i in range(size)]
        value = value + lax.ppermute(value, axes, route)
        distance //= 2
    return value


def product(spec, left, right):
    return jnp.einsum(spec, left, right, precision=EXACT, preferred_element_type=jnp.float32)


def unit_rows(raw):
    scale_inv = lax.rsqrt(jnp.sum(raw * raw, axis=-1, keepdims=True) + EPS_KEY)
    return (raw * scale_inv, scale_inv)


def unit_back(unit, scale_inv, grad):
    width = unit.shape[-1]
    ones = jnp.ones((width, width), jnp.float32)
    along = product("hrd,de->hre", unit * grad, ones)
    return scale_inv * (grad - unit * along)


def compose(earlier, later):
    through = product("mhij,hjk->mhik", earlier, later[0])
    return through + jnp.stack([jnp.zeros_like(later[1]), later[1]])


def unit_lower_inverse(lower_mat):
    size = lower_mat.shape[-1]
    row_ids = lax.broadcasted_iota(jnp.int32, (size, size), 0)
    col_ids = lax.broadcasted_iota(jnp.int32, (size, size), 1)
    eye = (row_ids == col_ids).astype(jnp.float32)
    first = ((row_ids // 2) == (col_ids // 2)) & (row_ids > col_ids)
    inverse = eye - lower_mat * first.astype(jnp.float32)
    width = 2
    while width < size:
        inside = (row_ids // (2 * width)) == (col_ids // (2 * width))
        below = (row_ids // width) > (col_ids // width)
        coupling = lower_mat * (inside & below).astype(jnp.float32)
        left = product("bij,bjk->bik", inverse, coupling)
        inverse = inverse - product("bij,bjk->bik", left, inverse)
        width *= 2
    return inverse


def stretch_factors(key_blk, value_blk, rate_blk, inverse, eye_head):
    head_dim = key_blk.shape[2]
    rhs = jnp.concatenate(
        [rate_blk[:, :, None] * key_blk, rate_blk[:, :, None] * value_blk], axis=2
    )
    solved = product("hrs,hsd->hrd", inverse, rhs)
    w_mat = solved[:, :, :head_dim]
    t_vals = solved[:, :, head_dim:]
    transit = eye_head - product("hrd,hre->hde", w_mat, key_blk)
    return (inverse, w_mat, t_vals, transit)


def scan_maps(own_map, identity, step, axes, known=None, carry=None):
    size = 1
    here = 0
    for axis in axes:
        size *= lax.axis_size(axis)
        here = here * lax.axis_size(axis) + lax.axis_index(axis)

    def shifted(block, distance):
        route = [(i, i + step * distance) for i in range(size) if 0 <= i + step * distance < size]
        return lax.ppermute(block, axes, route)

    def reached(distance):
        source = here - step * distance
        return (source >= 0) & (source < size)

    if known is None:
        excl = jnp.where(reached(1), shifted(own_map, 1), identity)
    else:
        got = jnp.stack([known, shifted(own_map[1], 1)])
        excl = jnp.where(reached(1), got, identity)
    incl = compose(excl, own_map)
    carry, incl = lax.optimization_barrier((carry, incl))
    distance = 2
    while distance < size:
        if 2 * distance >= size:
            got = shifted(incl[1], distance)
            state = product("hij,hjk->hik", got, excl[0]) + excl[1]
            return jnp.where(reached(distance), state, excl[1]), carry
        got = shifted(incl, distance)
        ok = reached(distance)
        excl = jnp.where(ok, compose(got, excl), excl)
        incl = jnp.where(ok, compose(got, incl), incl)
        distance *= 2
    return excl[1], carry


def scan_split(own_map, identity, step, known=None):
    heads = own_map.shape[1]
    if lax.axis_size("inner") != 2 or heads % 2:
        return scan_maps(own_map, identity, step, ("outer", "inner"))[0], None
    half = heads // 2
    core = lax.axis_index("inner")
    lead = core == (0 if step > 0 else 1)
    swap = [(0, 1), (1, 0)]
    low = own_map[:, :half]
    high = own_map[:, half:]
    own_part = jnp.where(core == 0, low, high)
    other_part = jnp.where(core == 0, high, low)
    got = lax.ppermute(other_part, "inner", swap)
    first = jnp.where(lead, own_part, got)
    second = jnp.where(lead, got, own_part)
    chip_map = compose(first, second)
    chips = lax.axis_size("outer")
    back_route = [(i, i - step) for i in range(chips) if 0 <= i - step < chips]
    ahead = lax.ppermute(chip_map[0], "outer", back_route) if known is None else None
    start, ahead = scan_maps(chip_map, identity[:, :half], step, ("outer",), known, ahead)
    applied = product("hij,hjk->hik", start, first[0]) + first[1]
    for_other = jnp.where(lead, applied, start)
    keep = jnp.where(lead, start, applied)
    back = lax.ppermute(for_other, "inner", swap)
    whole = jnp.where(
        core == 0,
        jnp.concatenate([keep, back], axis=0),
        jnp.concatenate([back, keep], axis=0),
    )
    return whole, ahead


def on_device(queries, keys, values, betas, grad_out, gain):
    length_here = queries.shape[1]
    heads = HEADS
    head_dim = HEAD_DIM
    span = STRETCH
    refl = 2 * span
    count = length_here // span
    query_raw = (
        queries[0].astype(jnp.float32).reshape(length_here, heads, head_dim).transpose(1, 0, 2)
    )
    key_raw = (
        keys[0]
        .astype(jnp.float32)
        .reshape(length_here, 2, heads, head_dim)
        .transpose(2, 0, 1, 3)
        .reshape(heads, 2 * length_here, head_dim)
    )
    value_all = (
        values[0]
        .astype(jnp.float32)
        .reshape(length_here, 2, heads, head_dim)
        .transpose(2, 0, 1, 3)
        .reshape(heads, 2 * length_here, head_dim)
    )
    rate_all = betas[0].transpose(0, 2, 1).reshape(heads, 2 * length_here)
    cotan_all = (
        grad_out[0].astype(jnp.float32).reshape(length_here, heads, head_dim).transpose(1, 0, 2)
    )
    gains = gain.reshape(heads, head_dim)
    query_n, query_inv = unit_rows(query_raw)
    key_n, key_inv = unit_rows(key_raw)
    token_ids = lax.broadcasted_iota(jnp.int32, (span, refl), 0)
    refl_ids = lax.broadcasted_iota(jnp.int32, (span, refl), 1)
    read_mask = (refl_ids <= 2 * token_ids + 1).astype(jnp.float32)
    row_ids = lax.broadcasted_iota(jnp.int32, (refl, refl), 0)
    col_ids = lax.broadcasted_iota(jnp.int32, (refl, refl), 1)
    strict = (col_ids < row_ids).astype(jnp.float32)
    eye_refl = jnp.eye(refl, dtype=jnp.float32)
    eye_head = jnp.eye(head_dim, dtype=jnp.float32)
    identity = jnp.stack(
        [
            jnp.broadcast_to(eye_head, (heads, head_dim, head_dim)),
            jnp.zeros((heads, head_dim, head_dim), jnp.float32),
        ]
    )

    def refl_rows(array, block_id):
        return array[:, block_id * refl : (block_id + 1) * refl]

    def token_rows(array, block_id):
        return array[:, block_id * span : (block_id + 1) * span]

    lower_all = []
    for block_id in range(count):
        key_blk = refl_rows(key_n, block_id)
        gram = product("hrd,hsd->hrs", key_blk, key_blk)
        lower_all.append(eye_refl + refl_rows(rate_all, block_id)[:, :, None] * gram * strict)
    inverse_all = unit_lower_inverse(jnp.concatenate(lower_all, axis=0)).reshape(
        count, heads, refl, refl
    )
    stash = []
    block_map = identity
    for block_id in range(count):
        key_blk = refl_rows(key_n, block_id)
        factor_set = stretch_factors(
            key_blk,
            refl_rows(value_all, block_id),
            refl_rows(rate_all, block_id),
            inverse_all[block_id],
            eye_head,
        )
        offset = product("hrv,hre->hve", factor_set[2], key_blk)
        block_map = compose(block_map, jnp.stack([factor_set[3], offset]))
        stash.append(factor_set)

    def factors_of(block_id):
        return stash[block_id]

    state, ahead = scan_split(block_map, identity, 1)
    records = []
    adjoint_maps = []
    gain_sum = jnp.zeros((heads, head_dim), jnp.float32)
    for block_id in range(count):
        inverse, w_mat, t_vals, transit = factors_of(block_id)
        key_blk = refl_rows(key_n, block_id)
        query_blk = token_rows(query_n, block_id)
        cotan_blk = token_rows(cotan_all, block_id)
        update = t_vals - product("hrk,hvk->hrv", w_mat, state)
        scores = product("htd,hrd->htr", query_blk, key_blk) * read_mask
        output = product("htk,hvk->htv", query_blk, state) + product("htr,hrv->htv", scores, update)
        scale_inv = lax.rsqrt(jnp.mean(output * output, axis=2, keepdims=True) + EPS_OUT)
        normed = output * scale_inv
        scaled = cotan_blk * gains[:, None, :]
        d_out = scale_inv * (scaled - normed * jnp.mean(normed * scaled, axis=2, keepdims=True))
        gain_sum = gain_sum + jnp.sum(cotan_blk * normed, axis=1)
        source = product("htv,htk->hvk", d_out, query_blk - product("htr,hrk->htk", scores, w_mat))
        records.append((state, update, scores, d_out))
        adjoint_maps.append(jnp.stack([jnp.swapaxes(transit, 1, 2), source]))
        state = state + product("hrv,hrk->hvk", update, key_blk)
    adjoint_block = identity
    for block_id in reversed(range(count)):
        adjoint_block = compose(adjoint_block, adjoint_maps[block_id])
    known = None if ahead is None else jnp.swapaxes(ahead, 1, 2)
    adjoint, _ = scan_split(adjoint_block, identity, -1, known)
    grad_q_parts = [None] * count
    grad_k_parts = [None] * count
    grad_v_parts = [None] * count
    for block_id in reversed(range(count)):
        inverse, w_mat, t_vals, transit = factors_of(block_id)
        start_state, update, scores, d_out = records[block_id]
        key_blk = refl_rows(key_n, block_id)
        query_blk = token_rows(query_n, block_id)
        rate_blk = refl_rows(rate_all, block_id)
        d_update = product("htr,htv->hrv", scores, d_out) + product(
            "hrk,hvk->hrv", key_blk, adjoint
        )
        solved = product("hsr,hsv->hrv", inverse, d_update)
        d_target = rate_blk[:, :, None] * solved
        d_scores = product("htv,hrv->htr", d_out, update) * read_mask
        grad_q_parts[block_id] = product("htv,hvk->htk", d_out, start_state) + product(
            "htr,hrk->htk", d_scores, key_blk
        )
        d_gram = -product("hrv,hsv->hrs", d_target, update) * strict
        grad_k_parts[block_id] = (
            product("hrv,hvk->hrk", update, adjoint)
            + product("htr,htk->hrk", d_scores, query_blk)
            - product("hrv,hvk->hrk", d_target, start_state)
            + product("hrs,hsk->hrk", d_gram + jnp.swapaxes(d_gram, 1, 2), key_blk)
        )
        grad_v_parts[block_id] = d_target
        adjoint = (
            adjoint
            + product("htv,htk->hvk", d_out, query_blk)
            - product("hrv,hrk->hvk", d_target, key_blk)
        )
    grad_qn = jnp.concatenate(grad_q_parts, axis=1)
    grad_kn = jnp.concatenate(grad_k_parts, axis=1)
    grad_val = jnp.concatenate(grad_v_parts, axis=1)
    grad_q = unit_back(query_n, query_inv, grad_qn)
    grad_k = unit_back(key_n, key_inv, grad_kn)
    grad_q = (
        grad_q.transpose(1, 0, 2).reshape(1, length_here, heads * head_dim).astype(jnp.bfloat16)
    )
    grad_k = (
        grad_k.reshape(heads, length_here, 2, head_dim)
        .transpose(1, 2, 0, 3)
        .reshape(1, length_here, 2, heads * head_dim)
        .astype(jnp.bfloat16)
    )
    grad_val = (
        grad_val.reshape(heads, length_here, 2, head_dim)
        .transpose(1, 2, 0, 3)
        .reshape(1, length_here, 2, heads * head_dim)
        .astype(jnp.bfloat16)
    )
    total = total_over(gain_sum, ("dp", "outer", "inner"))
    tokens_all = length_here * lax.axis_size("dp") * lax.axis_size("outer") * lax.axis_size("inner")
    gain_grad = total.reshape(heads * head_dim) * (1.0 / math.sqrt(tokens_all))
    return (grad_q, grad_k, grad_val, gain_grad)


def solution(mesh):
    return jax.shard_map(
        on_device,
        mesh=mesh,
        in_specs=(
            P("dp", ("outer", "inner"), None),
            P("dp", ("outer", "inner"), None, None),
            P("dp", ("outer", "inner"), None, None),
            P("dp", None, None, ("outer", "inner")),
            P("dp", ("outer", "inner"), None),
            P(),
        ),
        out_specs=(
            P("dp", ("outer", "inner"), None),
            P("dp", ("outer", "inner"), None, None),
            P("dp", ("outer", "inner"), None, None),
            P(),
        ),
        check_vma=False,
    )
```

```python
import math

import jax
import jax.numpy as jnp
from jax import lax
from jax.sharding import PartitionSpec as P

HEADS = 8
HEAD_DIM = 128
STRETCH = 64


EXACT = lax.Precision.HIGH
EPS_KEY = 1e-06
EPS_OUT = 1e-05


def butterfly(value, axes, distances):
    size = 1
    for axis in axes:
        size *= lax.axis_size(axis)
    for distance in distances:
        route = [(i, i ^ distance) for i in range(size)]
        value = value + lax.ppermute(value, axes, route)
    return value


def axis_bits(axis, stride):
    count = lax.axis_size(axis)
    return [stride * (count >> k) for k in range(1, count.bit_length())]


def product(spec, left, right):
    return jnp.einsum(spec, left, right, precision=EXACT, preferred_element_type=jnp.float32)


def unit_rows(raw):
    scale_inv = lax.rsqrt(jnp.sum(raw * raw, axis=-1, keepdims=True) + EPS_KEY)
    return (raw * scale_inv, scale_inv)


def unit_back(unit, scale_inv, grad):
    width = unit.shape[-1]
    ones = jnp.ones((width, width), jnp.float32)
    along = product("hrd,de->hre", unit * grad, ones)
    return scale_inv * (grad - unit * along)


def compose(earlier, later):
    through = product("mhij,hjk->mhik", earlier, later[0])
    return through + jnp.stack([jnp.zeros_like(later[1]), later[1]])


def unit_lower_inverse(lower_mat):
    size = lower_mat.shape[-1]
    row_ids = lax.broadcasted_iota(jnp.int32, (size, size), 0)
    col_ids = lax.broadcasted_iota(jnp.int32, (size, size), 1)
    eye = (row_ids == col_ids).astype(jnp.float32)
    first = ((row_ids // 2) == (col_ids // 2)) & (row_ids > col_ids)
    inverse = eye - lower_mat * first.astype(jnp.float32)
    width = 2
    while width < size:
        inside = (row_ids // (2 * width)) == (col_ids // (2 * width))
        below = (row_ids // width) > (col_ids // width)
        coupling = lower_mat * (inside & below).astype(jnp.float32)
        left = product("bij,bjk->bik", inverse, coupling)
        inverse = inverse - product("bij,bjk->bik", left, inverse)
        width *= 2
    return inverse


def stretch_factors(key_blk, value_blk, rate_blk, inverse, eye_head):
    head_dim = key_blk.shape[2]
    rhs = jnp.concatenate(
        [rate_blk[:, :, None] * key_blk, rate_blk[:, :, None] * value_blk], axis=2
    )
    solved = product("hrs,hsd->hrd", inverse, rhs)
    w_mat = solved[:, :, :head_dim]
    t_vals = solved[:, :, head_dim:]
    transit = eye_head - product("hrd,hre->hde", w_mat, key_blk)
    return (inverse, w_mat, t_vals, transit)


def scan_maps(own_map, identity, step, axes, known=None, carry=None):
    size = 1
    here = 0
    for axis in axes:
        size *= lax.axis_size(axis)
        here = here * lax.axis_size(axis) + lax.axis_index(axis)

    def shifted(block, distance):
        route = [(i, i + step * distance) for i in range(size) if 0 <= i + step * distance < size]
        return lax.ppermute(block, axes, route)

    def reached(distance):
        source = here - step * distance
        return (source >= 0) & (source < size)

    if known is None:
        excl = jnp.where(reached(1), shifted(own_map, 1), identity)
    else:
        got = jnp.stack([known, shifted(own_map[1], 1)])
        excl = jnp.where(reached(1), got, identity)
    incl = compose(excl, own_map)
    carry, incl = lax.optimization_barrier((carry, incl))
    distance = 2
    while distance < size:
        if 2 * distance >= size:
            got = shifted(incl[1], distance)
            state = product("hij,hjk->hik", got, excl[0]) + excl[1]
            return jnp.where(reached(distance), state, excl[1]), carry
        got = shifted(incl, distance)
        ok = reached(distance)
        excl = jnp.where(ok, compose(got, excl), excl)
        incl = jnp.where(ok, compose(got, incl), incl)
        distance *= 2
    return excl[1], carry


def scan_split(own_map, identity, step, known=None):
    heads = own_map.shape[1]
    if lax.axis_size("inner") != 2 or heads % 2:
        return scan_maps(own_map, identity, step, ("outer", "inner"))[0], None
    half = heads // 2
    core = lax.axis_index("inner")
    lead = core == (0 if step > 0 else 1)
    swap = [(0, 1), (1, 0)]
    low = own_map[:, :half]
    high = own_map[:, half:]
    own_part = jnp.where(core == 0, low, high)
    other_part = jnp.where(core == 0, high, low)
    got = lax.ppermute(other_part, "inner", swap)
    first = jnp.where(lead, own_part, got)
    second = jnp.where(lead, got, own_part)
    chip_map = compose(first, second)
    chips = lax.axis_size("outer")
    back_route = [(i, i - step) for i in range(chips) if 0 <= i - step < chips]
    ahead = lax.ppermute(chip_map[0], "outer", back_route) if known is None else None
    start, ahead = scan_maps(chip_map, identity[:, :half], step, ("outer",), known, ahead)
    applied = product("hij,hjk->hik", start, first[0]) + first[1]
    for_other = jnp.where(lead, applied, start)
    keep = jnp.where(lead, start, applied)
    back = lax.ppermute(for_other, "inner", swap)
    whole = jnp.where(
        core == 0,
        jnp.concatenate([keep, back], axis=0),
        jnp.concatenate([back, keep], axis=0),
    )
    return whole, ahead


def on_device(queries, keys, values, betas, grad_out, gain):
    length_here = queries.shape[1]
    heads = HEADS
    head_dim = HEAD_DIM
    span = STRETCH
    refl = 2 * span
    count = length_here // span
    query_raw = (
        queries[0].astype(jnp.float32).reshape(length_here, heads, head_dim).transpose(1, 0, 2)
    )
    key_raw = (
        keys[0]
        .astype(jnp.float32)
        .reshape(length_here, 2, heads, head_dim)
        .transpose(2, 0, 1, 3)
        .reshape(heads, 2 * length_here, head_dim)
    )
    value_all = (
        values[0]
        .astype(jnp.float32)
        .reshape(length_here, 2, heads, head_dim)
        .transpose(2, 0, 1, 3)
        .reshape(heads, 2 * length_here, head_dim)
    )
    rate_all = betas[0].transpose(0, 2, 1).reshape(heads, 2 * length_here)
    cotan_all = (
        grad_out[0].astype(jnp.float32).reshape(length_here, heads, head_dim).transpose(1, 0, 2)
    )
    gains = gain.reshape(heads, head_dim)
    query_n, query_inv = unit_rows(query_raw)
    key_n, key_inv = unit_rows(key_raw)
    token_ids = lax.broadcasted_iota(jnp.int32, (span, refl), 0)
    refl_ids = lax.broadcasted_iota(jnp.int32, (span, refl), 1)
    read_mask = (refl_ids <= 2 * token_ids + 1).astype(jnp.float32)
    row_ids = lax.broadcasted_iota(jnp.int32, (refl, refl), 0)
    col_ids = lax.broadcasted_iota(jnp.int32, (refl, refl), 1)
    strict = (col_ids < row_ids).astype(jnp.float32)
    eye_refl = jnp.eye(refl, dtype=jnp.float32)
    eye_head = jnp.eye(head_dim, dtype=jnp.float32)
    identity = jnp.stack(
        [
            jnp.broadcast_to(eye_head, (heads, head_dim, head_dim)),
            jnp.zeros((heads, head_dim, head_dim), jnp.float32),
        ]
    )

    def refl_rows(array, block_id):
        return array[:, block_id * refl : (block_id + 1) * refl]

    def token_rows(array, block_id):
        return array[:, block_id * span : (block_id + 1) * span]

    lower_all = []
    for block_id in range(count):
        key_blk = refl_rows(key_n, block_id)
        gram = product("hrd,hsd->hrs", key_blk, key_blk)
        lower_all.append(eye_refl + refl_rows(rate_all, block_id)[:, :, None] * gram * strict)
    inverse_all = unit_lower_inverse(jnp.concatenate(lower_all, axis=0)).reshape(
        count, heads, refl, refl
    )
    stash = []
    block_map = identity
    for block_id in range(count):
        key_blk = refl_rows(key_n, block_id)
        factor_set = stretch_factors(
            key_blk,
            refl_rows(value_all, block_id),
            refl_rows(rate_all, block_id),
            inverse_all[block_id],
            eye_head,
        )
        offset = product("hrv,hre->hve", factor_set[2], key_blk)
        block_map = compose(block_map, jnp.stack([factor_set[3], offset]))
        stash.append(factor_set)

    def factors_of(block_id):
        return stash[block_id]

    state, ahead = scan_split(block_map, identity, 1)
    records = []
    adjoint_maps = []
    gain_sum = jnp.zeros((heads, head_dim), jnp.float32)
    for block_id in range(count):
        inverse, w_mat, t_vals, transit = factors_of(block_id)
        key_blk = refl_rows(key_n, block_id)
        query_blk = token_rows(query_n, block_id)
        cotan_blk = token_rows(cotan_all, block_id)
        update = t_vals - product("hrk,hvk->hrv", w_mat, state)
        scores = product("htd,hrd->htr", query_blk, key_blk) * read_mask
        output = product("htk,hvk->htv", query_blk, state) + product("htr,hrv->htv", scores, update)
        scale_inv = lax.rsqrt(jnp.mean(output * output, axis=2, keepdims=True) + EPS_OUT)
        normed = output * scale_inv
        scaled = cotan_blk * gains[:, None, :]
        d_out = scale_inv * (scaled - normed * jnp.mean(normed * scaled, axis=2, keepdims=True))
        gain_sum = gain_sum + jnp.sum(cotan_blk * normed, axis=1)
        source = product("htv,htk->hvk", d_out, query_blk - product("htr,hrk->htk", scores, w_mat))
        records.append((state, update, scores, d_out))
        adjoint_maps.append(jnp.stack([jnp.swapaxes(transit, 1, 2), source]))
        state = state + product("hrv,hrk->hvk", update, key_blk)
    adjoint_block = identity
    for block_id in reversed(range(count)):
        adjoint_block = compose(adjoint_block, adjoint_maps[block_id])
    known = None if ahead is None else jnp.swapaxes(ahead, 1, 2)
    axes = ("dp", "outer", "inner")
    sizes = [lax.axis_size(axis) for axis in axes]
    split = all(size & (size - 1) == 0 for size in sizes)
    if split:
        outer_bits = axis_bits("outer", sizes[2])
        first_bits = axis_bits("dp", sizes[1] * sizes[2]) + axis_bits("inner", 1)
        gain_sum = butterfly(gain_sum, axes, first_bits)
    adjoint, _ = scan_split(adjoint_block, identity, -1, known)
    if split:
        adjoint, gain_sum = lax.optimization_barrier((adjoint, gain_sum))
        total = butterfly(gain_sum, axes, outer_bits)
    else:
        total = lax.psum(gain_sum, axes)
    grad_q_parts = [None] * count
    grad_k_parts = [None] * count
    grad_v_parts = [None] * count
    for block_id in reversed(range(count)):
        inverse, w_mat, t_vals, transit = factors_of(block_id)
        start_state, update, scores, d_out = records[block_id]
        key_blk = refl_rows(key_n, block_id)
        query_blk = token_rows(query_n, block_id)
        rate_blk = refl_rows(rate_all, block_id)
        d_update = product("htr,htv->hrv", scores, d_out) + product(
            "hrk,hvk->hrv", key_blk, adjoint
        )
        solved = product("hsr,hsv->hrv", inverse, d_update)
        d_target = rate_blk[:, :, None] * solved
        d_scores = product("htv,hrv->htr", d_out, update) * read_mask
        grad_q_parts[block_id] = product("htv,hvk->htk", d_out, start_state) + product(
            "htr,hrk->htk", d_scores, key_blk
        )
        d_gram = -product("hrv,hsv->hrs", d_target, update) * strict
        grad_k_parts[block_id] = (
            product("hrv,hvk->hrk", update, adjoint)
            + product("htr,htk->hrk", d_scores, query_blk)
            - product("hrv,hvk->hrk", d_target, start_state)
            + product("hrs,hsk->hrk", d_gram + jnp.swapaxes(d_gram, 1, 2), key_blk)
        )
        grad_v_parts[block_id] = d_target
        adjoint = (
            adjoint
            + product("htv,htk->hvk", d_out, query_blk)
            - product("hrv,hrk->hvk", d_target, key_blk)
        )
    grad_qn = jnp.concatenate(grad_q_parts, axis=1)
    grad_kn = jnp.concatenate(grad_k_parts, axis=1)
    grad_val = jnp.concatenate(grad_v_parts, axis=1)
    grad_q = unit_back(query_n, query_inv, grad_qn)
    grad_k = unit_back(key_n, key_inv, grad_kn)
    grad_q = (
        grad_q.transpose(1, 0, 2).reshape(1, length_here, heads * head_dim).astype(jnp.bfloat16)
    )
    grad_k = (
        grad_k.reshape(heads, length_here, 2, head_dim)
        .transpose(1, 2, 0, 3)
        .reshape(1, length_here, 2, heads * head_dim)
        .astype(jnp.bfloat16)
    )
    grad_val = (
        grad_val.reshape(heads, length_here, 2, head_dim)
        .transpose(1, 2, 0, 3)
        .reshape(1, length_here, 2, heads * head_dim)
        .astype(jnp.bfloat16)
    )
    tokens_all = length_here * lax.axis_size("dp") * lax.axis_size("outer") * lax.axis_size("inner")
    gain_grad = total.reshape(heads * head_dim) * (1.0 / math.sqrt(tokens_all))
    return (grad_q, grad_k, grad_val, gain_grad)


def solution(mesh):
    return jax.shard_map(
        on_device,
        mesh=mesh,
        in_specs=(
            P("dp", ("outer", "inner"), None),
            P("dp", ("outer", "inner"), None, None),
            P("dp", ("outer", "inner"), None, None),
            P("dp", None, None, ("outer", "inner")),
            P("dp", ("outer", "inner"), None),
            P(),
        ),
        out_specs=(
            P("dp", ("outer", "inner"), None),
            P("dp", ("outer", "inner"), None, None),
            P("dp", ("outer", "inner"), None, None),
            P(),
        ),
        check_vma=False,
    )
```

```python
import math

import jax
import jax.numpy as jnp
from jax import lax
from jax.sharding import PartitionSpec as P

HEADS = 8
HEAD_DIM = 128
STRETCH = 64


EXACT = lax.Precision.HIGH
EPS_KEY = 1e-06
EPS_OUT = 1e-05


def total_over(value, axes):
    size = 1
    for axis in axes:
        size *= lax.axis_size(axis)
    if size & (size - 1):
        return lax.psum(value, axes)
    order = [1 << k for k in reversed(range(size.bit_length() - 1))]
    order = [d for d in order if d >= 8] + [d for d in order if d < 8][::-1]
    for distance in order:
        route = [(i, i ^ distance) for i in range(size)]
        value = value + lax.ppermute(value, axes, route)
    return value


def product(spec, left, right):
    return jnp.einsum(spec, left, right, precision=EXACT, preferred_element_type=jnp.float32)


def unit_rows(raw):
    scale_inv = lax.rsqrt(jnp.sum(raw * raw, axis=-1, keepdims=True) + EPS_KEY)
    return (raw * scale_inv, scale_inv)


def unit_back(unit, scale_inv, grad):
    width = unit.shape[-1]
    ones = jnp.ones((width, width), jnp.float32)
    along = product("hrd,de->hre", unit * grad, ones)
    return scale_inv * (grad - unit * along)


def compose(earlier, later):
    through = product("mhij,hjk->mhik", earlier, later[0])
    return through + jnp.stack([jnp.zeros_like(later[1]), later[1]])


def unit_lower_inverse(lower_mat):
    size = lower_mat.shape[-1]
    row_ids = lax.broadcasted_iota(jnp.int32, (size, size), 0)
    col_ids = lax.broadcasted_iota(jnp.int32, (size, size), 1)
    eye = (row_ids == col_ids).astype(jnp.float32)
    first = ((row_ids // 2) == (col_ids // 2)) & (row_ids > col_ids)
    inverse = eye - lower_mat * first.astype(jnp.float32)
    width = 2
    while width < size:
        inside = (row_ids // (2 * width)) == (col_ids // (2 * width))
        below = (row_ids // width) > (col_ids // width)
        coupling = lower_mat * (inside & below).astype(jnp.float32)
        left = product("bij,bjk->bik", inverse, coupling)
        inverse = inverse - product("bij,bjk->bik", left, inverse)
        width *= 2
    return inverse


def stretch_factors(key_blk, value_blk, rate_blk, inverse, eye_head):
    head_dim = key_blk.shape[2]
    rhs = jnp.concatenate(
        [rate_blk[:, :, None] * key_blk, rate_blk[:, :, None] * value_blk], axis=2
    )
    solved = product("hrs,hsd->hrd", inverse, rhs)
    w_mat = solved[:, :, :head_dim]
    t_vals = solved[:, :, head_dim:]
    transit = eye_head - product("hrd,hre->hde", w_mat, key_blk)
    return (inverse, w_mat, t_vals, transit)


def scan_maps(own_map, identity, step, axes):
    size = 1
    here = 0
    for axis in axes:
        size *= lax.axis_size(axis)
        here = here * lax.axis_size(axis) + lax.axis_index(axis)

    def shifted(block, distance):
        route = [(i, i + step * distance) for i in range(size) if 0 <= i + step * distance < size]
        return lax.ppermute(block, axes, route)

    def reached(distance):
        source = here - step * distance
        return (source >= 0) & (source < size)

    excl = jnp.where(reached(1), shifted(own_map, 1), identity)
    incl = compose(excl, own_map)
    distance = 2
    while distance < size:
        if 2 * distance >= size:
            got = shifted(incl[1], distance)
            state = product("hij,hjk->hik", got, excl[0]) + excl[1]
            return jnp.where(reached(distance), state, excl[1])
        got = shifted(incl, distance)
        ok = reached(distance)
        excl = jnp.where(ok, compose(got, excl), excl)
        incl = jnp.where(ok, compose(got, incl), incl)
        distance *= 2
    return excl[1]


def scan_split(own_map, identity, step):
    heads = own_map.shape[1]
    if lax.axis_size("inner") != 2 or heads % 2:
        return scan_maps(own_map, identity, step, ("outer", "inner"))
    half = heads // 2
    core = lax.axis_index("inner")
    lead = core == (0 if step > 0 else 1)
    swap = [(0, 1), (1, 0)]
    low = own_map[:, :half]
    high = own_map[:, half:]
    own_part = jnp.where(core == 0, low, high)
    other_part = jnp.where(core == 0, high, low)
    got = lax.ppermute(other_part, "inner", swap)
    first = jnp.where(lead, own_part, got)
    second = jnp.where(lead, got, own_part)
    chip_map = compose(first, second)
    start = scan_maps(chip_map, identity[:, :half], step, ("outer",))
    applied = product("hij,hjk->hik", start, first[0]) + first[1]
    for_other = jnp.where(lead, applied, start)
    keep = jnp.where(lead, start, applied)
    back = lax.ppermute(for_other, "inner", swap)
    return jnp.where(
        core == 0,
        jnp.concatenate([keep, back], axis=0),
        jnp.concatenate([back, keep], axis=0),
    )


def on_device(queries, keys, values, betas, grad_out, gain):
    length_here = queries.shape[1]
    heads = HEADS
    head_dim = HEAD_DIM
    span = STRETCH
    refl = 2 * span
    count = length_here // span
    query_raw = (
        queries[0].astype(jnp.float32).reshape(length_here, heads, head_dim).transpose(1, 0, 2)
    )
    key_raw = (
        keys[0]
        .astype(jnp.float32)
        .reshape(length_here, 2, heads, head_dim)
        .transpose(2, 0, 1, 3)
        .reshape(heads, 2 * length_here, head_dim)
    )
    value_all = (
        values[0]
        .astype(jnp.float32)
        .reshape(length_here, 2, heads, head_dim)
        .transpose(2, 0, 1, 3)
        .reshape(heads, 2 * length_here, head_dim)
    )
    rate_all = betas[0].transpose(0, 2, 1).reshape(heads, 2 * length_here)
    cotan_all = (
        grad_out[0].astype(jnp.float32).reshape(length_here, heads, head_dim).transpose(1, 0, 2)
    )
    gains = gain.reshape(heads, head_dim)
    query_n, query_inv = unit_rows(query_raw)
    key_n, key_inv = unit_rows(key_raw)
    token_ids = lax.broadcasted_iota(jnp.int32, (span, refl), 0)
    refl_ids = lax.broadcasted_iota(jnp.int32, (span, refl), 1)
    read_mask = (refl_ids <= 2 * token_ids + 1).astype(jnp.float32)
    row_ids = lax.broadcasted_iota(jnp.int32, (refl, refl), 0)
    col_ids = lax.broadcasted_iota(jnp.int32, (refl, refl), 1)
    strict = (col_ids < row_ids).astype(jnp.float32)
    eye_refl = jnp.eye(refl, dtype=jnp.float32)
    eye_head = jnp.eye(head_dim, dtype=jnp.float32)
    identity = jnp.stack(
        [
            jnp.broadcast_to(eye_head, (heads, head_dim, head_dim)),
            jnp.zeros((heads, head_dim, head_dim), jnp.float32),
        ]
    )

    def refl_rows(array, block_id):
        return array[:, block_id * refl : (block_id + 1) * refl]

    def token_rows(array, block_id):
        return array[:, block_id * span : (block_id + 1) * span]

    lower_all = []
    for block_id in range(count):
        key_blk = refl_rows(key_n, block_id)
        gram = product("hrd,hsd->hrs", key_blk, key_blk)
        lower_all.append(eye_refl + refl_rows(rate_all, block_id)[:, :, None] * gram * strict)
    inverse_all = unit_lower_inverse(jnp.concatenate(lower_all, axis=0)).reshape(
        count, heads, refl, refl
    )
    stash = []
    block_map = identity
    for block_id in range(count):
        key_blk = refl_rows(key_n, block_id)
        factor_set = stretch_factors(
            key_blk,
            refl_rows(value_all, block_id),
            refl_rows(rate_all, block_id),
            inverse_all[block_id],
            eye_head,
        )
        offset = product("hrv,hre->hve", factor_set[2], key_blk)
        block_map = compose(block_map, jnp.stack([factor_set[3], offset]))
        stash.append(factor_set)

    def factors_of(block_id):
        return stash[block_id]

    state = scan_split(block_map, identity, 1)
    records = []
    adjoint_maps = []
    gain_sum = jnp.zeros((heads, head_dim), jnp.float32)
    for block_id in range(count):
        inverse, w_mat, t_vals, transit = factors_of(block_id)
        key_blk = refl_rows(key_n, block_id)
        query_blk = token_rows(query_n, block_id)
        cotan_blk = token_rows(cotan_all, block_id)
        update = t_vals - product("hrk,hvk->hrv", w_mat, state)
        scores = product("htd,hrd->htr", query_blk, key_blk) * read_mask
        output = product("htk,hvk->htv", query_blk, state) + product("htr,hrv->htv", scores, update)
        scale_inv = lax.rsqrt(jnp.mean(output * output, axis=2, keepdims=True) + EPS_OUT)
        normed = output * scale_inv
        scaled = cotan_blk * gains[:, None, :]
        d_out = scale_inv * (scaled - normed * jnp.mean(normed * scaled, axis=2, keepdims=True))
        gain_sum = gain_sum + jnp.sum(cotan_blk * normed, axis=1)
        source = product("htv,htk->hvk", d_out, query_blk - product("htr,hrk->htk", scores, w_mat))
        records.append((state, update, scores, d_out))
        adjoint_maps.append(jnp.stack([jnp.swapaxes(transit, 1, 2), source]))
        state = state + product("hrv,hrk->hvk", update, key_blk)
    adjoint_block = identity
    for block_id in reversed(range(count)):
        adjoint_block = compose(adjoint_block, adjoint_maps[block_id])
    adjoint = scan_split(adjoint_block, identity, -1)
    grad_q_parts = [None] * count
    grad_k_parts = [None] * count
    grad_v_parts = [None] * count
    for block_id in reversed(range(count)):
        inverse, w_mat, t_vals, transit = factors_of(block_id)
        start_state, update, scores, d_out = records[block_id]
        key_blk = refl_rows(key_n, block_id)
        query_blk = token_rows(query_n, block_id)
        rate_blk = refl_rows(rate_all, block_id)
        d_update = product("htr,htv->hrv", scores, d_out) + product(
            "hrk,hvk->hrv", key_blk, adjoint
        )
        solved = product("hsr,hsv->hrv", inverse, d_update)
        d_target = rate_blk[:, :, None] * solved
        d_scores = product("htv,hrv->htr", d_out, update) * read_mask
        grad_q_parts[block_id] = product("htv,hvk->htk", d_out, start_state) + product(
            "htr,hrk->htk", d_scores, key_blk
        )
        d_gram = -product("hrv,hsv->hrs", d_target, update) * strict
        grad_k_parts[block_id] = (
            product("hrv,hvk->hrk", update, adjoint)
            + product("htr,htk->hrk", d_scores, query_blk)
            - product("hrv,hvk->hrk", d_target, start_state)
            + product("hrs,hsk->hrk", d_gram + jnp.swapaxes(d_gram, 1, 2), key_blk)
        )
        grad_v_parts[block_id] = d_target
        adjoint = (
            adjoint
            + product("htv,htk->hvk", d_out, query_blk)
            - product("hrv,hrk->hvk", d_target, key_blk)
        )
    grad_qn = jnp.concatenate(grad_q_parts, axis=1)
    grad_kn = jnp.concatenate(grad_k_parts, axis=1)
    grad_val = jnp.concatenate(grad_v_parts, axis=1)
    grad_q = unit_back(query_n, query_inv, grad_qn)
    grad_k = unit_back(key_n, key_inv, grad_kn)
    grad_q = (
        grad_q.transpose(1, 0, 2).reshape(1, length_here, heads * head_dim).astype(jnp.bfloat16)
    )
    grad_k = (
        grad_k.reshape(heads, length_here, 2, head_dim)
        .transpose(1, 2, 0, 3)
        .reshape(1, length_here, 2, heads * head_dim)
        .astype(jnp.bfloat16)
    )
    grad_val = (
        grad_val.reshape(heads, length_here, 2, head_dim)
        .transpose(1, 2, 0, 3)
        .reshape(1, length_here, 2, heads * head_dim)
        .astype(jnp.bfloat16)
    )
    total = total_over(gain_sum, ("dp", "outer", "inner"))
    tokens_all = length_here * lax.axis_size("dp") * lax.axis_size("outer") * lax.axis_size("inner")
    gain_grad = total.reshape(heads * head_dim) * (1.0 / math.sqrt(tokens_all))
    return (grad_q, grad_k, grad_val, gain_grad)


def solution(mesh):
    return jax.shard_map(
        on_device,
        mesh=mesh,
        in_specs=(
            P("dp", ("outer", "inner"), None),
            P("dp", ("outer", "inner"), None, None),
            P("dp", ("outer", "inner"), None, None),
            P("dp", None, None, ("outer", "inner")),
            P("dp", ("outer", "inner"), None),
            P(),
        ),
        out_specs=(
            P("dp", ("outer", "inner"), None),
            P("dp", ("outer", "inner"), None, None),
            P("dp", ("outer", "inner"), None, None),
            P(),
        ),
        check_vma=False,
    )
```

```python
import math

import jax
import jax.numpy as jnp
from jax import lax
from jax.sharding import PartitionSpec as P

HEADS = 8
HEAD_DIM = 128
STRETCH = 64


EXACT = lax.Precision.HIGH
EPS_KEY = 1e-06
EPS_OUT = 1e-05


def total_over(value, axes):
    size = 1
    for axis in axes:
        size *= lax.axis_size(axis)
    if size & (size - 1):
        return lax.psum(value, axes)
    distance = size // 2
    while distance >= 1:
        route = [(i, i ^ distance) for i in range(size)]
        value = value + lax.ppermute(value, axes, route)
        distance //= 2
    return value


def product(spec, left, right):
    return jnp.einsum(spec, left, right, precision=EXACT, preferred_element_type=jnp.float32)


def unit_rows(raw):
    scale_inv = lax.rsqrt(jnp.sum(raw * raw, axis=-1, keepdims=True) + EPS_KEY)
    return (raw * scale_inv, scale_inv)


def unit_back(unit, scale_inv, grad):
    width = unit.shape[-1]
    ones = jnp.ones((width, width), jnp.float32)
    along = product("hrd,de->hre", unit * grad, ones)
    return scale_inv * (grad - unit * along)


def compose(earlier, later):
    through = product("mhij,hjk->mhik", earlier, later[0])
    return through + jnp.stack([jnp.zeros_like(later[1]), later[1]])


def unit_lower_inverse(lower_mat):
    size = lower_mat.shape[-1]
    row_ids = lax.broadcasted_iota(jnp.int32, (size, size), 0)
    col_ids = lax.broadcasted_iota(jnp.int32, (size, size), 1)
    eye = (row_ids == col_ids).astype(jnp.float32)
    first = ((row_ids // 2) == (col_ids // 2)) & (row_ids > col_ids)
    inverse = eye - lower_mat * first.astype(jnp.float32)
    levels = max(size.bit_length() - 2, 0)

    def level(step, inverse):
        width = jnp.left_shift(jnp.int32(2), step)
        inside = (row_ids // (2 * width)) == (col_ids // (2 * width))
        below = (row_ids // width) > (col_ids // width)
        coupling = lower_mat * (inside & below).astype(jnp.float32)
        left = product("bij,bjk->bik", inverse, coupling)
        return inverse - product("bij,bjk->bik", left, inverse)

    return lax.fori_loop(0, levels, level, inverse)


def stretch_factors(key_blk, value_blk, rate_blk, inverse, eye_head):
    head_dim = key_blk.shape[2]
    rhs = jnp.concatenate(
        [rate_blk[:, :, None] * key_blk, rate_blk[:, :, None] * value_blk], axis=2
    )
    solved = product("hrs,hsd->hrd", inverse, rhs)
    w_mat = solved[:, :, :head_dim]
    t_vals = solved[:, :, head_dim:]
    transit = eye_head - product("hrd,hre->hde", w_mat, key_blk)
    return (inverse, w_mat, t_vals, transit)


def scan_maps(own_map, identity, step, axes):
    size = 1
    here = 0
    for axis in axes:
        size *= lax.axis_size(axis)
        here = here * lax.axis_size(axis) + lax.axis_index(axis)

    def shifted(block, distance):
        route = [(i, i + step * distance) for i in range(size) if 0 <= i + step * distance < size]
        return lax.ppermute(block, axes, route)

    def reached(distance):
        source = here - step * distance
        return (source >= 0) & (source < size)

    excl = jnp.where(reached(1), shifted(own_map, 1), identity)
    incl = compose(excl, own_map)
    distance = 2
    while distance < size:
        if 2 * distance >= size:
            got = shifted(incl[1], distance)
            state = product("hij,hjk->hik", got, excl[0]) + excl[1]
            return jnp.where(reached(distance), state, excl[1])
        got = shifted(incl, distance)
        ok = reached(distance)
        excl = jnp.where(ok, compose(got, excl), excl)
        incl = jnp.where(ok, compose(got, incl), incl)
        distance *= 2
    return excl[1]


def scan_split(own_map, identity, step):
    heads = own_map.shape[1]
    if lax.axis_size("inner") != 2 or heads % 2:
        return scan_maps(own_map, identity, step, ("outer", "inner"))
    half = heads // 2
    core = lax.axis_index("inner")
    lead = core == (0 if step > 0 else 1)
    swap = [(0, 1), (1, 0)]
    low = own_map[:, :half]
    high = own_map[:, half:]
    own_part = jnp.where(core == 0, low, high)
    other_part = jnp.where(core == 0, high, low)
    got = lax.ppermute(other_part, "inner", swap)
    first = jnp.where(lead, own_part, got)
    second = jnp.where(lead, got, own_part)
    chip_map = compose(first, second)
    start = scan_maps(chip_map, identity[:, :half], step, ("outer",))
    applied = product("hij,hjk->hik", start, first[0]) + first[1]
    for_other = jnp.where(lead, applied, start)
    keep = jnp.where(lead, start, applied)
    back = lax.ppermute(for_other, "inner", swap)
    return jnp.where(
        core == 0,
        jnp.concatenate([keep, back], axis=0),
        jnp.concatenate([back, keep], axis=0),
    )


def on_device(queries, keys, values, betas, grad_out, gain):
    length_here = queries.shape[1]
    heads = HEADS
    head_dim = HEAD_DIM
    span = STRETCH
    refl = 2 * span
    count = length_here // span
    query_raw = (
        queries[0].astype(jnp.float32).reshape(length_here, heads, head_dim).transpose(1, 0, 2)
    )
    key_raw = (
        keys[0]
        .astype(jnp.float32)
        .reshape(length_here, 2, heads, head_dim)
        .transpose(2, 0, 1, 3)
        .reshape(heads, 2 * length_here, head_dim)
    )
    value_all = (
        values[0]
        .astype(jnp.float32)
        .reshape(length_here, 2, heads, head_dim)
        .transpose(2, 0, 1, 3)
        .reshape(heads, 2 * length_here, head_dim)
    )
    rate_all = betas[0].transpose(0, 2, 1).reshape(heads, 2 * length_here)
    cotan_all = (
        grad_out[0].astype(jnp.float32).reshape(length_here, heads, head_dim).transpose(1, 0, 2)
    )
    gains = gain.reshape(heads, head_dim)
    query_n, query_inv = unit_rows(query_raw)
    key_n, key_inv = unit_rows(key_raw)
    token_ids = lax.broadcasted_iota(jnp.int32, (span, refl), 0)
    refl_ids = lax.broadcasted_iota(jnp.int32, (span, refl), 1)
    read_mask = (refl_ids <= 2 * token_ids + 1).astype(jnp.float32)
    row_ids = lax.broadcasted_iota(jnp.int32, (refl, refl), 0)
    col_ids = lax.broadcasted_iota(jnp.int32, (refl, refl), 1)
    strict = (col_ids < row_ids).astype(jnp.float32)
    eye_refl = jnp.eye(refl, dtype=jnp.float32)
    eye_head = jnp.eye(head_dim, dtype=jnp.float32)
    identity = jnp.stack(
        [
            jnp.broadcast_to(eye_head, (heads, head_dim, head_dim)),
            jnp.zeros((heads, head_dim, head_dim), jnp.float32),
        ]
    )

    def refl_rows(array, block_id):
        return array[:, block_id * refl : (block_id + 1) * refl]

    def token_rows(array, block_id):
        return array[:, block_id * span : (block_id + 1) * span]

    lower_all = []
    for block_id in range(count):
        key_blk = refl_rows(key_n, block_id)
        gram = product("hrd,hsd->hrs", key_blk, key_blk)
        lower_all.append(eye_refl + refl_rows(rate_all, block_id)[:, :, None] * gram * strict)
    inverse_all = unit_lower_inverse(jnp.concatenate(lower_all, axis=0)).reshape(
        count, heads, refl, refl
    )
    stash = []
    block_map = identity
    for block_id in range(count):
        key_blk = refl_rows(key_n, block_id)
        factor_set = stretch_factors(
            key_blk,
            refl_rows(value_all, block_id),
            refl_rows(rate_all, block_id),
            inverse_all[block_id],
            eye_head,
        )
        offset = product("hrv,hre->hve", factor_set[2], key_blk)
        block_map = compose(block_map, jnp.stack([factor_set[3], offset]))
        stash.append(factor_set)

    def factors_of(block_id):
        return stash[block_id]

    state = scan_split(block_map, identity, 1)
    records = []
    adjoint_maps = []
    gain_sum = jnp.zeros((heads, head_dim), jnp.float32)
    for block_id in range(count):
        inverse, w_mat, t_vals, transit = factors_of(block_id)
        key_blk = refl_rows(key_n, block_id)
        query_blk = token_rows(query_n, block_id)
        cotan_blk = token_rows(cotan_all, block_id)
        update = t_vals - product("hrk,hvk->hrv", w_mat, state)
        scores = product("htd,hrd->htr", query_blk, key_blk) * read_mask
        output = product("htk,hvk->htv", query_blk, state) + product("htr,hrv->htv", scores, update)
        scale_inv = lax.rsqrt(jnp.mean(output * output, axis=2, keepdims=True) + EPS_OUT)
        normed = output * scale_inv
        scaled = cotan_blk * gains[:, None, :]
        d_out = scale_inv * (scaled - normed * jnp.mean(normed * scaled, axis=2, keepdims=True))
        gain_sum = gain_sum + jnp.sum(cotan_blk * normed, axis=1)
        source = product("htv,htk->hvk", d_out, query_blk - product("htr,hrk->htk", scores, w_mat))
        records.append((state, update, scores, d_out))
        adjoint_maps.append(jnp.stack([jnp.swapaxes(transit, 1, 2), source]))
        state = state + product("hrv,hrk->hvk", update, key_blk)
    adjoint_block = identity
    for block_id in reversed(range(count)):
        adjoint_block = compose(adjoint_block, adjoint_maps[block_id])
    adjoint = scan_split(adjoint_block, identity, -1)
    grad_q_parts = [None] * count
    grad_k_parts = [None] * count
    grad_v_parts = [None] * count
    for block_id in reversed(range(count)):
        inverse, w_mat, t_vals, transit = factors_of(block_id)
        start_state, update, scores, d_out = records[block_id]
        key_blk = refl_rows(key_n, block_id)
        query_blk = token_rows(query_n, block_id)
        rate_blk = refl_rows(rate_all, block_id)
        d_update = product("htr,htv->hrv", scores, d_out) + product(
            "hrk,hvk->hrv", key_blk, adjoint
        )
        solved = product("hsr,hsv->hrv", inverse, d_update)
        d_target = rate_blk[:, :, None] * solved
        d_scores = product("htv,hrv->htr", d_out, update) * read_mask
        grad_q_parts[block_id] = product("htv,hvk->htk", d_out, start_state) + product(
            "htr,hrk->htk", d_scores, key_blk
        )
        d_gram = -product("hrv,hsv->hrs", d_target, update) * strict
        grad_k_parts[block_id] = (
            product("hrv,hvk->hrk", update, adjoint)
            + product("htr,htk->hrk", d_scores, query_blk)
            - product("hrv,hvk->hrk", d_target, start_state)
            + product("hrs,hsk->hrk", d_gram + jnp.swapaxes(d_gram, 1, 2), key_blk)
        )
        grad_v_parts[block_id] = d_target
        adjoint = (
            adjoint
            + product("htv,htk->hvk", d_out, query_blk)
            - product("hrv,hrk->hvk", d_target, key_blk)
        )
    grad_qn = jnp.concatenate(grad_q_parts, axis=1)
    grad_kn = jnp.concatenate(grad_k_parts, axis=1)
    grad_val = jnp.concatenate(grad_v_parts, axis=1)
    grad_q = unit_back(query_n, query_inv, grad_qn)
    grad_k = unit_back(key_n, key_inv, grad_kn)
    grad_q = (
        grad_q.transpose(1, 0, 2).reshape(1, length_here, heads * head_dim).astype(jnp.bfloat16)
    )
    grad_k = (
        grad_k.reshape(heads, length_here, 2, head_dim)
        .transpose(1, 2, 0, 3)
        .reshape(1, length_here, 2, heads * head_dim)
        .astype(jnp.bfloat16)
    )
    grad_val = (
        grad_val.reshape(heads, length_here, 2, head_dim)
        .transpose(1, 2, 0, 3)
        .reshape(1, length_here, 2, heads * head_dim)
        .astype(jnp.bfloat16)
    )
    total = total_over(gain_sum, ("dp", "outer", "inner"))
    tokens_all = length_here * lax.axis_size("dp") * lax.axis_size("outer") * lax.axis_size("inner")
    gain_grad = total.reshape(heads * head_dim) * (1.0 / math.sqrt(tokens_all))
    return (grad_q, grad_k, grad_val, gain_grad)


def solution(mesh):
    return jax.shard_map(
        on_device,
        mesh=mesh,
        in_specs=(
            P("dp", ("outer", "inner"), None),
            P("dp", ("outer", "inner"), None, None),
            P("dp", ("outer", "inner"), None, None),
            P("dp", None, None, ("outer", "inner")),
            P("dp", ("outer", "inner"), None),
            P(),
        ),
        out_specs=(
            P("dp", ("outer", "inner"), None),
            P("dp", ("outer", "inner"), None, None),
            P("dp", ("outer", "inner"), None, None),
            P(),
        ),
        check_vma=False,
    )
```

```python
import math

import jax
import jax.numpy as jnp
from jax import lax
from jax.sharding import PartitionSpec as P

HEADS = 8
HEAD_DIM = 128
STRETCH = 64


EXACT = lax.Precision.HIGH
EPS_KEY = 1e-06
EPS_OUT = 1e-05


def total_over(value, axes):
    size = 1
    for axis in axes:
        size *= lax.axis_size(axis)
    if size & (size - 1):
        return lax.psum(value, axes)
    chips = lax.axis_size("outer")
    cores = lax.axis_size("inner")
    near = chips == 4 and axes == ("dp", "outer", "inner")
    distance = size // 2
    while distance >= 1:
        if not (near and distance == 2 * cores):
            route = [(i, i ^ distance) for i in range(size)]
            value = value + lax.ppermute(value, axes, route)
        distance //= 2
    if near:
        chip = lax.axis_index("outer")
        place = [(i // cores) % chips for i in range(size)]
        middle = [(i, i + cores) for i in range(size) if place[i] == 1]
        middle += [(i, i - cores) for i in range(size) if place[i] == 2]
        got = lax.ppermute(value, axes, middle)
        value = jnp.where((chip == 1) | (chip == 2), value + got, value)
        outward = [(i, i - cores) for i in range(size) if place[i] == 1]
        outward += [(i, i + cores) for i in range(size) if place[i] == 2]
        got = lax.ppermute(value, axes, outward)
        value = jnp.where((chip == 0) | (chip == 3), got, value)
    return value


def product(spec, left, right):
    return jnp.einsum(spec, left, right, precision=EXACT, preferred_element_type=jnp.float32)


def unit_rows(raw):
    scale_inv = lax.rsqrt(jnp.sum(raw * raw, axis=-1, keepdims=True) + EPS_KEY)
    return (raw * scale_inv, scale_inv)


def unit_back(unit, scale_inv, grad):
    width = unit.shape[-1]
    ones = jnp.ones((width, width), jnp.float32)
    along = product("hrd,de->hre", unit * grad, ones)
    return scale_inv * (grad - unit * along)


def compose(earlier, later):
    through = product("mhij,hjk->mhik", earlier, later[0])
    return through + jnp.stack([jnp.zeros_like(later[1]), later[1]])


def unit_lower_inverse(lower_mat):
    size = lower_mat.shape[-1]
    row_ids = lax.broadcasted_iota(jnp.int32, (size, size), 0)
    col_ids = lax.broadcasted_iota(jnp.int32, (size, size), 1)
    eye = (row_ids == col_ids).astype(jnp.float32)
    first = ((row_ids // 2) == (col_ids // 2)) & (row_ids > col_ids)
    inverse = eye - lower_mat * first.astype(jnp.float32)
    width = 2
    while width < size:
        inside = (row_ids // (2 * width)) == (col_ids // (2 * width))
        below = (row_ids // width) > (col_ids // width)
        coupling = lower_mat * (inside & below).astype(jnp.float32)
        left = product("bij,bjk->bik", inverse, coupling)
        inverse = inverse - product("bij,bjk->bik", left, inverse)
        width *= 2
    return inverse


def stretch_factors(key_blk, value_blk, rate_blk, inverse, eye_head):
    head_dim = key_blk.shape[2]
    rhs = jnp.concatenate(
        [rate_blk[:, :, None] * key_blk, rate_blk[:, :, None] * value_blk], axis=2
    )
    solved = product("hrs,hsd->hrd", inverse, rhs)
    w_mat = solved[:, :, :head_dim]
    t_vals = solved[:, :, head_dim:]
    transit = eye_head - product("hrd,hre->hde", w_mat, key_blk)
    return (inverse, w_mat, t_vals, transit)


def scan_maps(own_map, identity, step, axes):
    size = 1
    here = 0
    for axis in axes:
        size *= lax.axis_size(axis)
        here = here * lax.axis_size(axis) + lax.axis_index(axis)

    def shifted(block, distance):
        route = [(i, i + step * distance) for i in range(size) if 0 <= i + step * distance < size]
        return lax.ppermute(block, axes, route)

    def reached(distance):
        source = here - step * distance
        return (source >= 0) & (source < size)

    excl = jnp.where(reached(1), shifted(own_map, 1), identity)
    incl = compose(excl, own_map)
    distance = 2
    while distance < size:
        if 2 * distance >= size:
            got = shifted(incl[1], distance)
            state = product("hij,hjk->hik", got, excl[0]) + excl[1]
            return jnp.where(reached(distance), state, excl[1])
        got = shifted(incl, distance)
        ok = reached(distance)
        excl = jnp.where(ok, compose(got, excl), excl)
        incl = jnp.where(ok, compose(got, incl), incl)
        distance *= 2
    return excl[1]


def scan_split(own_map, identity, step):
    heads = own_map.shape[1]
    if lax.axis_size("inner") != 2 or heads % 2:
        return scan_maps(own_map, identity, step, ("outer", "inner"))
    half = heads // 2
    core = lax.axis_index("inner")
    lead = core == (0 if step > 0 else 1)
    swap = [(0, 1), (1, 0)]
    low = own_map[:, :half]
    high = own_map[:, half:]
    own_part = jnp.where(core == 0, low, high)
    other_part = jnp.where(core == 0, high, low)
    got = lax.ppermute(other_part, "inner", swap)
    first = jnp.where(lead, own_part, got)
    second = jnp.where(lead, got, own_part)
    chip_map = compose(first, second)
    start = scan_maps(chip_map, identity[:, :half], step, ("outer",))
    applied = product("hij,hjk->hik", start, first[0]) + first[1]
    for_other = jnp.where(lead, applied, start)
    keep = jnp.where(lead, start, applied)
    back = lax.ppermute(for_other, "inner", swap)
    return jnp.where(
        core == 0,
        jnp.concatenate([keep, back], axis=0),
        jnp.concatenate([back, keep], axis=0),
    )


def on_device(queries, keys, values, betas, grad_out, gain):
    length_here = queries.shape[1]
    heads = HEADS
    head_dim = HEAD_DIM
    span = STRETCH
    refl = 2 * span
    count = length_here // span
    query_raw = (
        queries[0].astype(jnp.float32).reshape(length_here, heads, head_dim).transpose(1, 0, 2)
    )
    key_raw = (
        keys[0]
        .astype(jnp.float32)
        .reshape(length_here, 2, heads, head_dim)
        .transpose(2, 0, 1, 3)
        .reshape(heads, 2 * length_here, head_dim)
    )
    value_all = (
        values[0]
        .astype(jnp.float32)
        .reshape(length_here, 2, heads, head_dim)
        .transpose(2, 0, 1, 3)
        .reshape(heads, 2 * length_here, head_dim)
    )
    rate_all = betas[0].transpose(0, 2, 1).reshape(heads, 2 * length_here)
    cotan_all = (
        grad_out[0].astype(jnp.float32).reshape(length_here, heads, head_dim).transpose(1, 0, 2)
    )
    gains = gain.reshape(heads, head_dim)
    query_n, query_inv = unit_rows(query_raw)
    key_n, key_inv = unit_rows(key_raw)
    token_ids = lax.broadcasted_iota(jnp.int32, (span, refl), 0)
    refl_ids = lax.broadcasted_iota(jnp.int32, (span, refl), 1)
    read_mask = (refl_ids <= 2 * token_ids + 1).astype(jnp.float32)
    row_ids = lax.broadcasted_iota(jnp.int32, (refl, refl), 0)
    col_ids = lax.broadcasted_iota(jnp.int32, (refl, refl), 1)
    strict = (col_ids < row_ids).astype(jnp.float32)
    eye_refl = jnp.eye(refl, dtype=jnp.float32)
    eye_head = jnp.eye(head_dim, dtype=jnp.float32)
    identity = jnp.stack(
        [
            jnp.broadcast_to(eye_head, (heads, head_dim, head_dim)),
            jnp.zeros((heads, head_dim, head_dim), jnp.float32),
        ]
    )

    def refl_rows(array, block_id):
        return array[:, block_id * refl : (block_id + 1) * refl]

    def token_rows(array, block_id):
        return array[:, block_id * span : (block_id + 1) * span]

    lower_all = []
    for block_id in range(count):
        key_blk = refl_rows(key_n, block_id)
        gram = product("hrd,hsd->hrs", key_blk, key_blk)
        lower_all.append(eye_refl + refl_rows(rate_all, block_id)[:, :, None] * gram * strict)
    inverse_all = unit_lower_inverse(jnp.concatenate(lower_all, axis=0)).reshape(
        count, heads, refl, refl
    )
    stash = []
    block_map = identity
    for block_id in range(count):
        key_blk = refl_rows(key_n, block_id)
        factor_set = stretch_factors(
            key_blk,
            refl_rows(value_all, block_id),
            refl_rows(rate_all, block_id),
            inverse_all[block_id],
            eye_head,
        )
        offset = product("hrv,hre->hve", factor_set[2], key_blk)
        block_map = compose(block_map, jnp.stack([factor_set[3], offset]))
        stash.append(factor_set)

    def factors_of(block_id):
        return stash[block_id]

    state = scan_split(block_map, identity, 1)
    records = []
    adjoint_maps = []
    gain_sum = jnp.zeros((heads, head_dim), jnp.float32)
    for block_id in range(count):
        inverse, w_mat, t_vals, transit = factors_of(block_id)
        key_blk = refl_rows(key_n, block_id)
        query_blk = token_rows(query_n, block_id)
        cotan_blk = token_rows(cotan_all, block_id)
        update = t_vals - product("hrk,hvk->hrv", w_mat, state)
        scores = product("htd,hrd->htr", query_blk, key_blk) * read_mask
        output = product("htk,hvk->htv", query_blk, state) + product("htr,hrv->htv", scores, update)
        scale_inv = lax.rsqrt(jnp.mean(output * output, axis=2, keepdims=True) + EPS_OUT)
        normed = output * scale_inv
        scaled = cotan_blk * gains[:, None, :]
        d_out = scale_inv * (scaled - normed * jnp.mean(normed * scaled, axis=2, keepdims=True))
        gain_sum = gain_sum + jnp.sum(cotan_blk * normed, axis=1)
        source = product("htv,htk->hvk", d_out, query_blk - product("htr,hrk->htk", scores, w_mat))
        records.append((state, update, scores, d_out))
        adjoint_maps.append(jnp.stack([jnp.swapaxes(transit, 1, 2), source]))
        state = state + product("hrv,hrk->hvk", update, key_blk)
    adjoint_block = identity
    for block_id in reversed(range(count)):
        adjoint_block = compose(adjoint_block, adjoint_maps[block_id])
    adjoint = scan_split(adjoint_block, identity, -1)
    grad_q_parts = [None] * count
    grad_k_parts = [None] * count
    grad_v_parts = [None] * count
    for block_id in reversed(range(count)):
        inverse, w_mat, t_vals, transit = factors_of(block_id)
        start_state, update, scores, d_out = records[block_id]
        key_blk = refl_rows(key_n, block_id)
        query_blk = token_rows(query_n, block_id)
        rate_blk = refl_rows(rate_all, block_id)
        d_update = product("htr,htv->hrv", scores, d_out) + product(
            "hrk,hvk->hrv", key_blk, adjoint
        )
        solved = product("hsr,hsv->hrv", inverse, d_update)
        d_target = rate_blk[:, :, None] * solved
        d_scores = product("htv,hrv->htr", d_out, update) * read_mask
        grad_q_parts[block_id] = product("htv,hvk->htk", d_out, start_state) + product(
            "htr,hrk->htk", d_scores, key_blk
        )
        d_gram = -product("hrv,hsv->hrs", d_target, update) * strict
        grad_k_parts[block_id] = (
            product("hrv,hvk->hrk", update, adjoint)
            + product("htr,htk->hrk", d_scores, query_blk)
            - product("hrv,hvk->hrk", d_target, start_state)
            + product("hrs,hsk->hrk", d_gram + jnp.swapaxes(d_gram, 1, 2), key_blk)
        )
        grad_v_parts[block_id] = d_target
        adjoint = (
            adjoint
            + product("htv,htk->hvk", d_out, query_blk)
            - product("hrv,hrk->hvk", d_target, key_blk)
        )
    grad_qn = jnp.concatenate(grad_q_parts, axis=1)
    grad_kn = jnp.concatenate(grad_k_parts, axis=1)
    grad_val = jnp.concatenate(grad_v_parts, axis=1)
    grad_q = unit_back(query_n, query_inv, grad_qn)
    grad_k = unit_back(key_n, key_inv, grad_kn)
    grad_q = (
        grad_q.transpose(1, 0, 2).reshape(1, length_here, heads * head_dim).astype(jnp.bfloat16)
    )
    grad_k = (
        grad_k.reshape(heads, length_here, 2, head_dim)
        .transpose(1, 2, 0, 3)
        .reshape(1, length_here, 2, heads * head_dim)
        .astype(jnp.bfloat16)
    )
    grad_val = (
        grad_val.reshape(heads, length_here, 2, head_dim)
        .transpose(1, 2, 0, 3)
        .reshape(1, length_here, 2, heads * head_dim)
        .astype(jnp.bfloat16)
    )
    total = total_over(gain_sum, ("dp", "outer", "inner"))
    tokens_all = length_here * lax.axis_size("dp") * lax.axis_size("outer") * lax.axis_size("inner")
    gain_grad = total.reshape(heads * head_dim) * (1.0 / math.sqrt(tokens_all))
    return (grad_q, grad_k, grad_val, gain_grad)


def solution(mesh):
    return jax.shard_map(
        on_device,
        mesh=mesh,
        in_specs=(
            P("dp", ("outer", "inner"), None),
            P("dp", ("outer", "inner"), None, None),
            P("dp", ("outer", "inner"), None, None),
            P("dp", None, None, ("outer", "inner")),
            P("dp", ("outer", "inner"), None),
            P(),
        ),
        out_specs=(
            P("dp", ("outer", "inner"), None),
            P("dp", ("outer", "inner"), None, None),
            P("dp", ("outer", "inner"), None, None),
            P(),
        ),
        check_vma=False,
    )
```

```python
import math

import jax
import jax.numpy as jnp
from jax import lax
from jax.sharding import PartitionSpec as P

HEADS = 8
HEAD_DIM = 128
STRETCH = 64


EXACT = lax.Precision.HIGH
EPS_KEY = 1e-06
EPS_OUT = 1e-05


def total_over(value, axes):
    size = 1
    for axis in axes:
        size *= lax.axis_size(axis)
    if size & (size - 1):
        return lax.psum(value, axes)
    distance = size // 2
    while distance >= 1:
        route = [(i, i ^ distance) for i in range(size)]
        value = value + lax.ppermute(value, axes, route)
        distance //= 2
    return value


def product(spec, left, right):
    return jnp.einsum(spec, left, right, precision=EXACT, preferred_element_type=jnp.float32)


def unit_rows(raw):
    scale_inv = lax.rsqrt(jnp.sum(raw * raw, axis=-1, keepdims=True) + EPS_KEY)
    return (raw * scale_inv, scale_inv)


def unit_back(unit, scale_inv, grad):
    width = unit.shape[-1]
    ones = jnp.ones((width, width), jnp.float32)
    along = product("hrd,de->hre", unit * grad, ones)
    return scale_inv * (grad - unit * along)


def compose(earlier, later):
    through = product("mhij,hjk->mhik", earlier, later[0])
    return through + jnp.stack([jnp.zeros_like(later[1]), later[1]])


def unit_lower_inverse(lower_mat):
    size = lower_mat.shape[-1]
    row_ids = lax.broadcasted_iota(jnp.int32, (size, size), 0)
    col_ids = lax.broadcasted_iota(jnp.int32, (size, size), 1)
    eye = (row_ids == col_ids).astype(jnp.float32)
    first = ((row_ids // 2) == (col_ids // 2)) & (row_ids > col_ids)
    inverse = eye - lower_mat * first.astype(jnp.float32)
    width = 2
    while width < size:
        inside = (row_ids // (2 * width)) == (col_ids // (2 * width))
        below = (row_ids // width) > (col_ids // width)
        coupling = lower_mat * (inside & below).astype(jnp.float32)
        left = product("bij,bjk->bik", inverse, coupling)
        inverse = inverse - product("bij,bjk->bik", left, inverse)
        width *= 2
    return inverse


def stretch_factors(key_blk, value_blk, rate_blk, inverse, eye_head):
    head_dim = key_blk.shape[2]
    rhs = jnp.concatenate(
        [rate_blk[:, :, None] * key_blk, rate_blk[:, :, None] * value_blk], axis=2
    )
    solved = product("hrs,hsd->hrd", inverse, rhs)
    w_mat = solved[:, :, :head_dim]
    t_vals = solved[:, :, head_dim:]
    transit = eye_head - product("hrd,hre->hde", w_mat, key_blk)
    return (inverse, w_mat, t_vals, transit)


def scan_maps(own_map, identity, step, axes):
    size = 1
    here = 0
    for axis in axes:
        size *= lax.axis_size(axis)
        here = here * lax.axis_size(axis) + lax.axis_index(axis)

    def shifted(block, distance):
        route = [(i, i + step * distance) for i in range(size) if 0 <= i + step * distance < size]
        return lax.ppermute(block, axes, route)

    def reached(distance):
        source = here - step * distance
        return (source >= 0) & (source < size)

    excl = jnp.where(reached(1), shifted(own_map, 1), identity)
    incl = compose(excl, own_map)
    distance = 2
    while distance < size:
        if 2 * distance >= size:
            got = shifted(incl[1], distance)
            state = product("hij,hjk->hik", got, excl[0]) + excl[1]
            return jnp.where(reached(distance), state, excl[1])
        got = shifted(incl, distance)
        ok = reached(distance)
        excl = jnp.where(ok, compose(got, excl), excl)
        incl = jnp.where(ok, compose(got, incl), incl)
        distance *= 2
    return excl[1]


def scan_split(own_map, identity, step):
    heads = own_map.shape[1]
    if lax.axis_size("inner") != 2 or heads % 2:
        return scan_maps(own_map, identity, step, ("outer", "inner"))
    half = heads // 2
    core = lax.axis_index("inner")
    lead = core == (0 if step > 0 else 1)
    swap = [(0, 1), (1, 0)]
    low = own_map[:, :half]
    high = own_map[:, half:]
    own_part = jnp.where(core == 0, low, high)
    other_part = jnp.where(core == 0, high, low)
    got = lax.ppermute(other_part, "inner", swap)
    first = jnp.where(lead, own_part, got)
    second = jnp.where(lead, got, own_part)
    chip_map = compose(first, second)
    start = scan_maps(chip_map, identity[:, :half], step, ("outer",))
    applied = product("hij,hjk->hik", start, first[0]) + first[1]
    for_other = jnp.where(lead, applied, start)
    keep = jnp.where(lead, start, applied)
    back = lax.ppermute(for_other, "inner", swap)
    return jnp.where(
        core == 0,
        jnp.concatenate([keep, back], axis=0),
        jnp.concatenate([back, keep], axis=0),
    )


def on_device(queries, keys, values, betas, grad_out, gain):
    length_here = queries.shape[1]
    heads = HEADS
    head_dim = HEAD_DIM
    span = STRETCH
    refl = 2 * span
    count = length_here // span
    query_raw = (
        queries[0].reshape(length_here, heads, head_dim).transpose(1, 0, 2).astype(jnp.float32)
    )
    key_raw = (
        keys[0]
        .reshape(length_here, 2, heads, head_dim)
        .transpose(2, 0, 1, 3)
        .reshape(heads, 2 * length_here, head_dim)
        .astype(jnp.float32)
    )
    value_all = (
        values[0]
        .reshape(length_here, 2, heads, head_dim)
        .transpose(2, 0, 1, 3)
        .reshape(heads, 2 * length_here, head_dim)
        .astype(jnp.float32)
    )
    rate_all = betas[0].transpose(0, 2, 1).reshape(heads, 2 * length_here)
    cotan_all = (
        grad_out[0].reshape(length_here, heads, head_dim).transpose(1, 0, 2).astype(jnp.float32)
    )
    gains = gain.reshape(heads, head_dim)
    query_n, query_inv = unit_rows(query_raw)
    key_n, key_inv = unit_rows(key_raw)
    token_ids = lax.broadcasted_iota(jnp.int32, (span, refl), 0)
    refl_ids = lax.broadcasted_iota(jnp.int32, (span, refl), 1)
    read_mask = (refl_ids <= 2 * token_ids + 1).astype(jnp.float32)
    row_ids = lax.broadcasted_iota(jnp.int32, (refl, refl), 0)
    col_ids = lax.broadcasted_iota(jnp.int32, (refl, refl), 1)
    strict = (col_ids < row_ids).astype(jnp.float32)
    eye_refl = jnp.eye(refl, dtype=jnp.float32)
    eye_head = jnp.eye(head_dim, dtype=jnp.float32)
    identity = jnp.stack(
        [
            jnp.broadcast_to(eye_head, (heads, head_dim, head_dim)),
            jnp.zeros((heads, head_dim, head_dim), jnp.float32),
        ]
    )

    def refl_rows(array, block_id):
        return array[:, block_id * refl : (block_id + 1) * refl]

    def token_rows(array, block_id):
        return array[:, block_id * span : (block_id + 1) * span]

    lower_all = []
    for block_id in range(count):
        key_blk = refl_rows(key_n, block_id)
        gram = product("hrd,hsd->hrs", key_blk, key_blk)
        lower_all.append(eye_refl + refl_rows(rate_all, block_id)[:, :, None] * gram * strict)
    inverse_all = unit_lower_inverse(jnp.concatenate(lower_all, axis=0)).reshape(
        count, heads, refl, refl
    )
    stash = []
    block_map = identity
    for block_id in range(count):
        key_blk = refl_rows(key_n, block_id)
        factor_set = stretch_factors(
            key_blk,
            refl_rows(value_all, block_id),
            refl_rows(rate_all, block_id),
            inverse_all[block_id],
            eye_head,
        )
        offset = product("hrv,hre->hve", factor_set[2], key_blk)
        block_map = compose(block_map, jnp.stack([factor_set[3], offset]))
        stash.append(factor_set)

    def factors_of(block_id):
        return stash[block_id]

    state = scan_split(block_map, identity, 1)
    records = []
    adjoint_maps = []
    gain_sum = jnp.zeros((heads, head_dim), jnp.float32)
    for block_id in range(count):
        inverse, w_mat, t_vals, transit = factors_of(block_id)
        key_blk = refl_rows(key_n, block_id)
        query_blk = token_rows(query_n, block_id)
        cotan_blk = token_rows(cotan_all, block_id)
        update = t_vals - product("hrk,hvk->hrv", w_mat, state)
        scores = product("htd,hrd->htr", query_blk, key_blk) * read_mask
        output = product("htk,hvk->htv", query_blk, state) + product("htr,hrv->htv", scores, update)
        scale_inv = lax.rsqrt(jnp.mean(output * output, axis=2, keepdims=True) + EPS_OUT)
        normed = output * scale_inv
        scaled = cotan_blk * gains[:, None, :]
        d_out = scale_inv * (scaled - normed * jnp.mean(normed * scaled, axis=2, keepdims=True))
        gain_sum = gain_sum + jnp.sum(cotan_blk * normed, axis=1)
        source = product("htv,htk->hvk", d_out, query_blk - product("htr,hrk->htk", scores, w_mat))
        records.append((state, update, scores, d_out))
        adjoint_maps.append(jnp.stack([jnp.swapaxes(transit, 1, 2), source]))
        state = state + product("hrv,hrk->hvk", update, key_blk)
    adjoint_block = identity
    for block_id in reversed(range(count)):
        adjoint_block = compose(adjoint_block, adjoint_maps[block_id])
    adjoint = scan_split(adjoint_block, identity, -1)
    grad_q_parts = [None] * count
    grad_k_parts = [None] * count
    grad_v_parts = [None] * count
    for block_id in reversed(range(count)):
        inverse, w_mat, t_vals, transit = factors_of(block_id)
        start_state, update, scores, d_out = records[block_id]
        key_blk = refl_rows(key_n, block_id)
        query_blk = token_rows(query_n, block_id)
        rate_blk = refl_rows(rate_all, block_id)
        d_update = product("htr,htv->hrv", scores, d_out) + product(
            "hrk,hvk->hrv", key_blk, adjoint
        )
        solved = product("hsr,hsv->hrv", inverse, d_update)
        d_target = rate_blk[:, :, None] * solved
        d_scores = product("htv,hrv->htr", d_out, update) * read_mask
        grad_q_parts[block_id] = product("htv,hvk->htk", d_out, start_state) + product(
            "htr,hrk->htk", d_scores, key_blk
        )
        d_gram = -product("hrv,hsv->hrs", d_target, update) * strict
        grad_k_parts[block_id] = (
            product("hrv,hvk->hrk", update, adjoint)
            + product("htr,htk->hrk", d_scores, query_blk)
            - product("hrv,hvk->hrk", d_target, start_state)
            + product("hrs,hsk->hrk", d_gram + jnp.swapaxes(d_gram, 1, 2), key_blk)
        )
        grad_v_parts[block_id] = d_target
        adjoint = (
            adjoint
            + product("htv,htk->hvk", d_out, query_blk)
            - product("hrv,hrk->hvk", d_target, key_blk)
        )
    grad_qn = jnp.concatenate(grad_q_parts, axis=1)
    grad_kn = jnp.concatenate(grad_k_parts, axis=1)
    grad_val = jnp.concatenate(grad_v_parts, axis=1)
    grad_q = unit_back(query_n, query_inv, grad_qn)
    grad_k = unit_back(key_n, key_inv, grad_kn)
    grad_q = (
        grad_q.transpose(1, 0, 2).reshape(1, length_here, heads * head_dim).astype(jnp.bfloat16)
    )
    grad_k = (
        grad_k.reshape(heads, length_here, 2, head_dim)
        .transpose(1, 2, 0, 3)
        .reshape(1, length_here, 2, heads * head_dim)
        .astype(jnp.bfloat16)
    )
    grad_val = (
        grad_val.reshape(heads, length_here, 2, head_dim)
        .transpose(1, 2, 0, 3)
        .reshape(1, length_here, 2, heads * head_dim)
        .astype(jnp.bfloat16)
    )
    total = total_over(gain_sum, ("dp", "outer", "inner"))
    tokens_all = length_here * lax.axis_size("dp") * lax.axis_size("outer") * lax.axis_size("inner")
    gain_grad = total.reshape(heads * head_dim) * (1.0 / math.sqrt(tokens_all))
    return (grad_q, grad_k, grad_val, gain_grad)


def solution(mesh):
    return jax.shard_map(
        on_device,
        mesh=mesh,
        in_specs=(
            P("dp", ("outer", "inner"), None),
            P("dp", ("outer", "inner"), None, None),
            P("dp", ("outer", "inner"), None, None),
            P("dp", None, None, ("outer", "inner")),
            P("dp", ("outer", "inner"), None),
            P(),
        ),
        out_specs=(
            P("dp", ("outer", "inner"), None),
            P("dp", ("outer", "inner"), None, None),
            P("dp", ("outer", "inner"), None, None),
            P(),
        ),
        check_vma=False,
    )
```
